128 devices in a mesh: frame: 32 (over z, x_hi, y), head: 4 (over x_lo, core).
Axes of the slice: x: 4 (x_hi: 2, x_lo: 2; x = x_hi * 2 + x_lo), y: 4, z: 4, core: 2. Of those that a mesh axis runs over, the one named last changes fastest.
Arguments:
- queries: bfloat16 [24576, 5120], P('frame', 'head'), may hold values from -6.4 to 6.4
- keys: bfloat16 [24576, 5120], P('frame', 'head'), may hold values from -6.4 to 6.4
- values: bfloat16 [24576, 5120], P('frame', 'head'), may hold values from -6 to 6
- out_weight: bfloat16 [5120, 5120], P('head'), may hold values from -0.078125 to 0.078125
- sink_owner: int32 [32], replicated, may hold values from 0 to 31, each once
- frame_pos: int32 [32], P('frame'), may hold values from 0 to 93, as said below
Outputs:
- mixed: bfloat16 [24576, 5120], P('frame', 'head')
The draws below stay inside these ranges and needn't reach their ends.
Inputs may be any that keep to these rules, and one draw needn't show every extreme that they name: `frame_pos`: strictly increasing, first entry 0, steps of 2 to 4. `sink_owner`: each number once.
All inputs are finite; a program needn't handle non-finite values.
Results may differ from the reference program's by a relative error of at most 0.01.
Values may be sent and summed in bfloat16 or wider, within the bound.
No kernel may reach another device: no remote copies, remote signals or barrier semaphores. Data moves between devices by JAX's collectives and lax.ppermute only.
A program may use at most 192 MiB of HBM per device.

```python
import jax
import jax.numpy as jnp
from jax import lax

D = 5120
HDIM = 128
CT = 768
GRID_W = 32
NTOK = 24576
N_FRAME = 32
N_HEAD = 4


def draw_keys(key, part):
    base = jnp.clip(jax.random.normal(jax.random.fold_in(key, 11), (NTOK, D), jnp.float32), -6.0, 6.0)
    return base.astype(jnp.bfloat16)


def draw_queries(key, part):
    base = jnp.clip(jax.random.normal(jax.random.fold_in(key, 12), (NTOK, D), jnp.float32), -6.0, 6.0)
    return base.astype(jnp.bfloat16)


def draw_frame_pos(key, part):
    index = jnp.arange(N_FRAME)
    lower = jax.random.randint(jax.random.fold_in(key, 21), (N_FRAME,), 0, 2)
    inner = (index > 0) & (index < N_FRAME - 1)
    return (3 * index - jnp.where(inner, lower, 0)).astype(jnp.int32)


def block_levels(stream_key, dims, shards, least, high):
    level = 1.0
    for dim, blocks in shards:
        draws = jax.random.uniform(jax.random.fold_in(jax.random.fold_in(stream_key, 6), dim), (blocks,), jnp.float32, least / len(shards), high / len(shards))
        level = level * jnp.repeat(jnp.exp(draws), dims[dim] // blocks).reshape((-1,) + (1,) * (len(dims) - 1 - dim))
    return level


def normal_values(rng, dims, scale, limit, shards=(), kind=jnp.bfloat16):
    loudness = block_levels(rng, dims, shards, -0.22, 0.18) if shards else 1.0
    values = jax.random.normal(rng, dims, jnp.float32) * scale * loudness
    return jnp.minimum(jnp.maximum(values, -limit), limit).astype(kind)


def setup_inputs(seed: int = 0) -> dict:
    splits = jax.random.split(jax.random.key(seed), 7)
    queries = draw_queries(jax.random.fold_in(splits[6], 71), 0)
    keys = draw_keys(jax.random.fold_in(splits[6], 71), 0)
    values = normal_values(splits[2], (NTOK, D), 1.0, 6.0, ((0, 32), (1, 4)))
    out_weight = normal_values(splits[3], (D, D), D ** -0.5, 0.078125, ((0, 4),))
    sink_owner = jax.random.permutation(splits[4], N_FRAME).astype(jnp.int32)
    frame_pos = draw_frame_pos(jax.random.fold_in(splits[6], 71), 0)
    return {"queries": queries, "keys": keys, "values": values, "out_weight": out_weight, "sink_owner": sink_owner, "frame_pos": frame_pos}


def pair_angles(frame_value, count):
    half = HDIM // 2
    tdim = HDIM - 4 * (HDIM // 6)
    sdim = 2 * (HDIM // 6)
    tcount = tdim // 2
    scount = sdim // 2
    index = jnp.arange(half)
    findex = index.astype(jnp.float32)
    freq = jnp.where(index < tcount, jnp.power(10000.0, -2.0 * findex / tdim), jnp.where(index < tcount + scount, jnp.power(10000.0, -2.0 * (findex - tcount) / sdim), jnp.power(10000.0, -2.0 * (findex - tcount - scount) / sdim)))
    token = jnp.arange(count)
    row_pos = (token // GRID_W).astype(jnp.float32)[:, None]
    col_pos = (token % GRID_W).astype(jnp.float32)[:, None]
    frame_f = jnp.zeros((count, 1), jnp.float32) + frame_value.astype(jnp.float32)
    pos = jnp.where(index[None, :] < tcount, frame_f, jnp.where(index[None, :] < tcount + scount, row_pos, col_pos))
    return pos * freq[None, :]

def rotate(block, angle):
    count = block.shape[0]
    heads_here = block.shape[1] // HDIM
    parts = block.astype(jnp.float32).reshape(count, heads_here, HDIM // 2, 2)
    cosine = jnp.cos(angle)[:, None, :]
    sine = jnp.sin(angle)[:, None, :]
    first = parts[..., 0] * cosine - parts[..., 1] * sine
    second = parts[..., 0] * sine + parts[..., 1] * cosine
    return jnp.stack([first, second], axis=-1).reshape(count, heads_here * HDIM).astype(jnp.bfloat16)

def attend_block(query, key_block, value_block):
    count = query.shape[0]
    heads_here = query.shape[1] // HDIM
    qh = query.astype(jnp.float32).reshape(count, heads_here, HDIM)
    kh = key_block.astype(jnp.float32).reshape(-1, heads_here, HDIM)
    vh = value_block.astype(jnp.float32).reshape(-1, heads_here, HDIM)
    scores = jnp.einsum('qhd,khd->hqk', qh, kh) / jnp.sqrt(jnp.float32(HDIM))
    peak = lax.optimization_barrier(jnp.max(scores, axis=-1))
    weights = jnp.exp(scores - peak[..., None]).astype(jnp.bfloat16)
    wf = weights.astype(jnp.float32)
    total = lax.optimization_barrier(jnp.sum(wf, axis=-1))
    partial_value = jnp.einsum('hqk,khd->hqd', wf, vh)
    return (peak, total, partial_value)

def combine(query, self_kv, prev_kv, sink_kv, prev_used, sink_used):
    m_self, l_self, o_self = attend_block(query, self_kv[0], self_kv[1])
    m_prev, l_prev, o_prev = attend_block(query, prev_kv[0], prev_kv[1])
    m_sink, l_sink, o_sink = attend_block(query, sink_kv[0], sink_kv[1])
    top = jnp.maximum(m_self, jnp.where(prev_used, m_prev, m_self))
    top = jnp.maximum(top, jnp.where(sink_used, m_sink, m_self))
    c_self = jnp.exp(m_self - top)
    c_prev = jnp.where(prev_used, jnp.exp(m_prev - top), 0.0)
    c_sink = jnp.where(sink_used, jnp.exp(m_sink - top), 0.0)
    numer = o_self * c_self[..., None] + o_prev * c_prev[..., None] + o_sink * c_sink[..., None]
    denom = l_self * c_self + l_prev * c_prev + l_sink * c_sink
    out = numer / denom[..., None]
    count = query.shape[0]
    return jnp.transpose(out, (1, 0, 2)).reshape(count, -1).astype(jnp.bfloat16)

def reference(queries, keys, values, out_weight, sink_owner, frame_pos):
    q3 = queries.reshape(N_FRAME, CT, D)
    k3 = keys.reshape(N_FRAME, CT, D)
    v3 = values.reshape(N_FRAME, CT, D)

    def rot_span(index):
        angle = pair_angles(frame_pos[index], CT)
        return (rotate(q3[index], angle), rotate(k3[index], angle))
    rot_q, rot_k = lax.map(rot_span, jnp.arange(N_FRAME))
    sink = sink_owner[0] % (N_FRAME // 2)

    def span_fn(index):
        prev = jnp.maximum(index - 1, 0)
        prev_used = (index >= 1) & (index - 1 != sink)
        return combine(rot_q[index], (rot_k[index], v3[index]), (rot_k[prev], v3[prev]), (rot_k[sink], v3[sink]), prev_used, sink < index)
    attended = lax.map(span_fn, jnp.arange(N_FRAME)).reshape(NTOK, D)
    width = D // N_HEAD
    mixed = jnp.zeros((NTOK, D), jnp.float32)
    for group in range(N_HEAD):
        part_sum = jnp.dot(attended[:, group * width:(group + 1) * width], out_weight[group * width:(group + 1) * width], preferred_element_type=jnp.float32)
        rounded = lax.optimization_barrier(part_sum.astype(jnp.bfloat16))
        mixed = mixed + rounded.astype(jnp.float32)
    return mixed.astype(jnp.bfloat16)
```

```python
import jax
import jax.numpy as jnp
from jax import lax
from jax.sharding import Mesh, NamedSharding, PartitionSpec as P

HDIM = 128
GRID_W = 32


def shifted(array, axis, by):
    length = lax.axis_size(axis)
    pairs = [(i, i + by) for i in range(length) if 0 <= i + by < length]
    return lax.ppermute(array, axis, pairs)


def broadcast(value, axis, source):
    kept = jnp.where(lax.axis_index(axis) == source, value, 0).astype(value.dtype)
    return lax.psum(kept, axis)


def pair_angles(frame_value, count):
    half = HDIM // 2
    tdim = HDIM - 4 * (HDIM // 6)
    sdim = 2 * (HDIM // 6)
    tcount = tdim // 2
    scount = sdim // 2
    index = jnp.arange(half)
    findex = index.astype(jnp.float32)
    freq = jnp.where(
        index < tcount,
        jnp.power(10000.0, -2.0 * findex / tdim),
        jnp.where(
            index < tcount + scount,
            jnp.power(10000.0, -2.0 * (findex - tcount) / sdim),
            jnp.power(10000.0, -2.0 * (findex - tcount - scount) / sdim),
        ),
    )
    token = jnp.arange(count)
    row_pos = (token // GRID_W).astype(jnp.float32)[:, None]
    col_pos = (token % GRID_W).astype(jnp.float32)[:, None]
    frame_f = jnp.zeros((count, 1), jnp.float32) + frame_value.astype(jnp.float32)
    pos = jnp.where(
        index[None, :] < tcount,
        frame_f,
        jnp.where(index[None, :] < tcount + scount, row_pos, col_pos),
    )
    return pos * freq[None, :]


def rotate(block, angle):
    count = block.shape[0]
    heads_here = block.shape[1] // HDIM
    parts = block.astype(jnp.float32).reshape(count, heads_here, HDIM // 2, 2)
    cosine = jnp.cos(angle)[:, None, :]
    sine = jnp.sin(angle)[:, None, :]
    first = parts[..., 0] * cosine - parts[..., 1] * sine
    second = parts[..., 0] * sine + parts[..., 1] * cosine
    return (
        jnp.stack([first, second], axis=-1).reshape(count, heads_here * HDIM).astype(jnp.bfloat16)
    )


def attend_block(query, key_block, value_block):
    count = query.shape[0]
    heads_here = query.shape[1] // HDIM
    qh = query.reshape(count, heads_here, HDIM)
    kh = key_block.reshape(-1, heads_here, HDIM)
    vh = value_block.reshape(-1, heads_here, HDIM)
    scores = jnp.einsum("qhd,khd->hqk", qh, kh, preferred_element_type=jnp.float32) / jnp.sqrt(
        jnp.float32(HDIM)
    )
    peak = jnp.max(scores, axis=-1)
    weights = jnp.exp(scores - peak[..., None]).astype(jnp.bfloat16)
    total = jnp.sum(weights.astype(jnp.float32), axis=-1)
    partial_value = jnp.einsum("hqk,khd->hqd", weights, vh, preferred_element_type=jnp.float32)
    return (peak, total, partial_value)


FRAME_AXES = ("z", "xh", "y")
HEAD_AXES = ("xl", "c")


def frame_index():
    return (lax.axis_index("z") * lax.axis_size("xh") + lax.axis_index("xh")) * lax.axis_size("y") + lax.axis_index(
        "y"
    )


def cyclic(array, axis, by):
    length = lax.axis_size(axis)
    return lax.ppermute(array, axis, [(i, (i + by) % length) for i in range(length)])


def ring_stage(data, axis, source):
    length = lax.axis_size(axis)
    if length == 1:
        return data
    rel = (lax.axis_index(axis) - source) % length
    if length == 2:
        got = cyclic(data, axis, 1)
        return jnp.where(rel == 0, data, got)
    assert length == 4
    half = data.shape[0] // 2
    h0, h1 = data[:half], data[half:]
    g0 = cyclic(h0, axis, 1)
    g1 = cyclic(h1, axis, -1)
    a0 = jnp.where(rel == 1, g0, h0)
    a1 = jnp.where(rel == 3, g1, h1)
    r_p = cyclic(jnp.where(rel == 0, h1, a0), axis, 1)
    r_m = cyclic(jnp.where(rel == 0, h0, a1), axis, -1)
    out0 = jnp.where(rel == 0, h0, jnp.where(rel == 1, g0, jnp.where(rel == 2, r_p, r_m)))
    out1 = jnp.where(rel == 0, h1, jnp.where(rel == 1, r_p, jnp.where(rel == 2, r_m, g1)))
    return jnp.concatenate([out0, out1], axis=0)


def sink_broadcast(data, sink):
    y_size, xh_size = lax.axis_size("y"), lax.axis_size("xh")
    source = {
        "y": sink % y_size,
        "xh": (sink // y_size) % xh_size,
        "z": sink // (y_size * xh_size),
    }
    orders = (("y", "z", "xh"), ("z", "xh", "y"), ("xh", "y", "z"))
    rows = data.shape[0] // len(orders)
    parts = [data[i * rows : (i + 1) * rows] for i in range(len(orders))]
    for stage in range(3):
        parts = [ring_stage(p, order[stage], source[order[stage]]) for p, order in zip(parts, orders)]
    return jnp.concatenate(parts, axis=0)


def shards(queries, keys, values, out_weight, sink_owner, frame_pos):
    count = queries.shape[0]
    angle = pair_angles(frame_pos[0], count)
    rot_k = rotate(keys, angle)
    place = frame_index()
    n_frame = lax.axis_size(FRAME_AXES)
    sink = sink_owner[0] % (n_frame // 2)
    prev_k, prev_v = shifted((rot_k, values), FRAME_AXES, 1)
    sink_kv = sink_broadcast(jnp.concatenate([rot_k, values], axis=0), sink)
    sink_k, sink_v = sink_kv[:count], sink_kv[count:]
    rot_q = rotate(queries, angle)
    prev_used = (place >= 1) & (place - 1 != sink)
    sink_used = sink < place
    m_self, l_self, o_self = attend_block(rot_q, rot_k, values)
    m_prev, l_prev, o_prev = attend_block(rot_q, prev_k, prev_v)
    m_sink, l_sink, o_sink = attend_block(rot_q, sink_k, sink_v)
    top = jnp.maximum(m_self, jnp.where(prev_used, m_prev, m_self))
    top = jnp.maximum(top, jnp.where(sink_used, m_sink, m_self))
    c_self = jnp.exp(m_self - top)
    c_prev = jnp.where(prev_used, jnp.exp(m_prev - top), 0.0)
    c_sink = jnp.where(sink_used, jnp.exp(m_sink - top), 0.0)
    numer = o_self * c_self[..., None] + o_prev * c_prev[..., None] + o_sink * c_sink[..., None]
    denom = l_self * c_self + l_prev * c_prev + l_sink * c_sink
    attended = (
        jnp.transpose(numer / denom[..., None], (1, 0, 2)).reshape(count, -1).astype(jnp.bfloat16)
    )
    terms = jnp.dot(attended, out_weight, preferred_element_type=jnp.float32)
    mixed = lax.psum_scatter(terms.astype(jnp.bfloat16), HEAD_AXES, scatter_dimension=1, tiled=True)
    return mixed


def solution(mesh):
    frame_phys = {"z": 4, "xh": 2, "y": 4}
    head_phys = {"xl": 2, "c": 2}
    assert mesh.shape["frame"] == 32 and mesh.shape["head"] == 4
    devices = mesh.devices.reshape(tuple(frame_phys.values()) + tuple(head_phys.values()))
    fine = Mesh(devices, FRAME_AXES + HEAD_AXES)
    in_specs = (
        P(FRAME_AXES, HEAD_AXES),
        P(FRAME_AXES, HEAD_AXES),
        P(FRAME_AXES, HEAD_AXES),
        P(HEAD_AXES, None),
        P(),
        P(FRAME_AXES),
    )
    out_specs = P(FRAME_AXES, HEAD_AXES)
    inner = jax.shard_map(shards, mesh=fine, in_specs=in_specs, out_specs=out_specs, check_vma=False)

    def run(*args):
        out = inner(*args)
        return jax.lax.with_sharding_constraint(out, NamedSharding(mesh, P("frame", "head")))

    return run
```

```python
import jax
import jax.numpy as jnp
from jax import lax
from jax.sharding import Mesh, NamedSharding, PartitionSpec as P

HDIM = 128
GRID_W = 32


def shifted(array, axis, by):
    length = lax.axis_size(axis)
    pairs = [(i, i + by) for i in range(length) if 0 <= i + by < length]
    return lax.ppermute(array, axis, pairs)


def broadcast(value, axis, source):
    kept = jnp.where(lax.axis_index(axis) == source, value, 0).astype(value.dtype)
    return lax.psum(kept, axis)


def pair_angles(frame_value, count):
    half = HDIM // 2
    tdim = HDIM - 4 * (HDIM // 6)
    sdim = 2 * (HDIM // 6)
    tcount = tdim // 2
    scount = sdim // 2
    index = jnp.arange(half)
    findex = index.astype(jnp.float32)
    freq = jnp.where(
        index < tcount,
        jnp.power(10000.0, -2.0 * findex / tdim),
        jnp.where(
            index < tcount + scount,
            jnp.power(10000.0, -2.0 * (findex - tcount) / sdim),
            jnp.power(10000.0, -2.0 * (findex - tcount - scount) / sdim),
        ),
    )
    token = jnp.arange(count)
    row_pos = (token // GRID_W).astype(jnp.float32)[:, None]
    col_pos = (token % GRID_W).astype(jnp.float32)[:, None]
    frame_f = jnp.zeros((count, 1), jnp.float32) + frame_value.astype(jnp.float32)
    pos = jnp.where(
        index[None, :] < tcount,
        frame_f,
        jnp.where(index[None, :] < tcount + scount, row_pos, col_pos),
    )
    return pos * freq[None, :]


def rotate(block, angle):
    count = block.shape[0]
    heads_here = block.shape[1] // HDIM
    parts = block.astype(jnp.float32).reshape(count, heads_here, HDIM // 2, 2)
    cosine = jnp.cos(angle)[:, None, :]
    sine = jnp.sin(angle)[:, None, :]
    first = parts[..., 0] * cosine - parts[..., 1] * sine
    second = parts[..., 0] * sine + parts[..., 1] * cosine
    return (
        jnp.stack([first, second], axis=-1).reshape(count, heads_here * HDIM).astype(jnp.bfloat16)
    )


def attend_block(query, key_block, value_block):
    count = query.shape[0]
    heads_here = query.shape[1] // HDIM
    qh = query.reshape(count, heads_here, HDIM)
    kh = key_block.reshape(-1, heads_here, HDIM)
    vh = value_block.reshape(-1, heads_here, HDIM)
    scores = jnp.einsum("qhd,khd->hqk", qh, kh, preferred_element_type=jnp.float32) / jnp.sqrt(
        jnp.float32(HDIM)
    )
    peak = jnp.max(scores, axis=-1)
    weights = jnp.exp(scores - peak[..., None]).astype(jnp.bfloat16)
    total = jnp.sum(weights.astype(jnp.float32), axis=-1)
    partial_value = jnp.einsum("hqk,khd->hqd", weights, vh, preferred_element_type=jnp.float32)
    return (peak, total, partial_value)


FRAME_AXES = ("z", "xh", "y")
HEAD_AXES = ("xl", "c")


def frame_index():
    return (lax.axis_index("z") * lax.axis_size("xh") + lax.axis_index("xh")) * lax.axis_size("y") + lax.axis_index(
        "y"
    )


def cyclic(array, axis, by):
    length = lax.axis_size(axis)
    return lax.ppermute(array, axis, [(i, (i + by) % length) for i in range(length)])


def ring_stage(data, axis, source):
    length = lax.axis_size(axis)
    if length == 1:
        return data
    rel = (lax.axis_index(axis) - source) % length
    if length == 2:
        got = cyclic(data, axis, 1)
        return jnp.where(rel == 0, data, got)
    assert length == 4
    half = data.shape[0] // 2
    h0, h1 = data[:half], data[half:]
    g0 = cyclic(h0, axis, 1)
    g1 = cyclic(h1, axis, -1)
    a0 = jnp.where(rel == 1, g0, h0)
    a1 = jnp.where(rel == 3, g1, h1)
    r_p = cyclic(jnp.where(rel == 0, h1, a0), axis, 1)
    r_m = cyclic(jnp.where(rel == 0, h0, a1), axis, -1)
    out0 = jnp.where(rel == 0, h0, jnp.where(rel == 1, g0, jnp.where(rel == 2, r_p, r_m)))
    out1 = jnp.where(rel == 0, h1, jnp.where(rel == 1, r_p, jnp.where(rel == 2, r_m, g1)))
    return jnp.concatenate([out0, out1], axis=0)


def sink_broadcast(data, sink):
    y_size, xh_size = lax.axis_size("y"), lax.axis_size("xh")
    source = {
        "y": sink % y_size,
        "xh": (sink // y_size) % xh_size,
        "z": sink // (y_size * xh_size),
    }
    orders = (("xh", "z", "y"), ("z", "xh", "y"))
    rows = data.shape[0] // len(orders)
    parts = [data[i * rows : (i + 1) * rows] for i in range(len(orders))]
    for stage in range(3):
        parts = [ring_stage(p, order[stage], source[order[stage]]) for p, order in zip(parts, orders)]
    return jnp.concatenate(parts, axis=0)


def shards(queries, keys, values, out_weight, sink_owner, frame_pos):
    count = queries.shape[0]
    angle = pair_angles(frame_pos[0], count)
    rot_k = rotate(keys, angle)
    place = frame_index()
    n_frame = lax.axis_size(FRAME_AXES)
    sink = sink_owner[0] % (n_frame // 2)
    prev_k, prev_v = shifted((rot_k, values), FRAME_AXES, 1)
    sink_kv = sink_broadcast(jnp.concatenate([rot_k, values], axis=0), sink)
    sink_k, sink_v = sink_kv[:count], sink_kv[count:]
    rot_q = rotate(queries, angle)
    prev_used = (place >= 1) & (place - 1 != sink)
    sink_used = sink < place
    m_self, l_self, o_self = attend_block(rot_q, rot_k, values)
    m_prev, l_prev, o_prev = attend_block(rot_q, prev_k, prev_v)
    m_sink, l_sink, o_sink = attend_block(rot_q, sink_k, sink_v)
    top = jnp.maximum(m_self, jnp.where(prev_used, m_prev, m_self))
    top = jnp.maximum(top, jnp.where(sink_used, m_sink, m_self))
    c_self = jnp.exp(m_self - top)
    c_prev = jnp.where(prev_used, jnp.exp(m_prev - top), 0.0)
    c_sink = jnp.where(sink_used, jnp.exp(m_sink - top), 0.0)
    numer = o_self * c_self[..., None] + o_prev * c_prev[..., None] + o_sink * c_sink[..., None]
    denom = l_self * c_self + l_prev * c_prev + l_sink * c_sink
    attended = (
        jnp.transpose(numer / denom[..., None], (1, 0, 2)).reshape(count, -1).astype(jnp.bfloat16)
    )
    terms = jnp.dot(attended, out_weight, preferred_element_type=jnp.float32)
    mixed = lax.psum_scatter(terms.astype(jnp.bfloat16), HEAD_AXES, scatter_dimension=1, tiled=True)
    return mixed


def solution(mesh):
    frame_phys = {"z": 4, "xh": 2, "y": 4}
    head_phys = {"xl": 2, "c": 2}
    assert mesh.shape["frame"] == 32 and mesh.shape["head"] == 4
    devices = mesh.devices.reshape(tuple(frame_phys.values()) + tuple(head_phys.values()))
    fine = Mesh(devices, FRAME_AXES + HEAD_AXES)
    in_specs = (
        P(FRAME_AXES, HEAD_AXES),
        P(FRAME_AXES, HEAD_AXES),
        P(FRAME_AXES, HEAD_AXES),
        P(HEAD_AXES, None),
        P(),
        P(FRAME_AXES),
    )
    out_specs = P(FRAME_AXES, HEAD_AXES)
    inner = jax.shard_map(shards, mesh=fine, in_specs=in_specs, out_specs=out_specs, check_vma=False)

    def run(*args):
        out = inner(*args)
        return jax.lax.with_sharding_constraint(out, NamedSharding(mesh, P("frame", "head")))

    return run
```

```python
import jax
import jax.numpy as jnp
from jax import lax
from jax.sharding import Mesh, NamedSharding, PartitionSpec as P

HDIM = 128
GRID_W = 32


def shifted(array, axis, by):
    length = lax.axis_size(axis)
    pairs = [(i, i + by) for i in range(length) if 0 <= i + by < length]
    return lax.ppermute(array, axis, pairs)


def broadcast(value, axis, source):
    kept = jnp.where(lax.axis_index(axis) == source, value, 0).astype(value.dtype)
    return lax.psum(kept, axis)


def pair_angles(frame_value, count):
    half = HDIM // 2
    tdim = HDIM - 4 * (HDIM // 6)
    sdim = 2 * (HDIM // 6)
    tcount = tdim // 2
    scount = sdim // 2
    index = jnp.arange(half)
    findex = index.astype(jnp.float32)
    freq = jnp.where(
        index < tcount,
        jnp.power(10000.0, -2.0 * findex / tdim),
        jnp.where(
            index < tcount + scount,
            jnp.power(10000.0, -2.0 * (findex - tcount) / sdim),
            jnp.power(10000.0, -2.0 * (findex - tcount - scount) / sdim),
        ),
    )
    token = jnp.arange(count)
    row_pos = (token // GRID_W).astype(jnp.float32)[:, None]
    col_pos = (token % GRID_W).astype(jnp.float32)[:, None]
    frame_f = jnp.zeros((count, 1), jnp.float32) + frame_value.astype(jnp.float32)
    pos = jnp.where(
        index[None, :] < tcount,
        frame_f,
        jnp.where(index[None, :] < tcount + scount, row_pos, col_pos),
    )
    return pos * freq[None, :]


def rotate(block, angle):
    count = block.shape[0]
    heads_here = block.shape[1] // HDIM
    parts = block.astype(jnp.float32).reshape(count, heads_here, HDIM // 2, 2)
    cosine = jnp.cos(angle)[:, None, :]
    sine = jnp.sin(angle)[:, None, :]
    first = parts[..., 0] * cosine - parts[..., 1] * sine
    second = parts[..., 0] * sine + parts[..., 1] * cosine
    return (
        jnp.stack([first, second], axis=-1).reshape(count, heads_here * HDIM).astype(jnp.bfloat16)
    )


def attend_block(query, key_block, value_block):
    count = query.shape[0]
    heads_here = query.shape[1] // HDIM
    qh = query.reshape(count, heads_here, HDIM)
    kh = key_block.reshape(-1, heads_here, HDIM)
    vh = value_block.reshape(-1, heads_here, HDIM)
    scores = jnp.einsum("qhd,khd->hqk", qh, kh, preferred_element_type=jnp.float32) / jnp.sqrt(
        jnp.float32(HDIM)
    )
    peak = jnp.max(scores, axis=-1)
    weights = jnp.exp(scores - peak[..., None]).astype(jnp.bfloat16)
    total = jnp.sum(weights.astype(jnp.float32), axis=-1)
    partial_value = jnp.einsum("hqk,khd->hqd", weights, vh, preferred_element_type=jnp.float32)
    return (peak, total, partial_value)


FRAME_AXES = ("z", "xh", "y")
HEAD_AXES = ("xl", "c")


def frame_index():
    return (lax.axis_index("z") * lax.axis_size("xh") + lax.axis_index("xh")) * lax.axis_size("y") + lax.axis_index(
        "y"
    )


def cyclic(array, axis, by):
    length = lax.axis_size(axis)
    return lax.ppermute(array, axis, [(i, (i + by) % length) for i in range(length)])


def ring_stage(data, axis, source):
    length = lax.axis_size(axis)
    if length == 1:
        return data
    rel = (lax.axis_index(axis) - source) % length
    if length == 2:
        got = cyclic(data, axis, 1)
        return jnp.where(rel == 0, data, got)
    assert length == 4
    half = data.shape[0] // 2
    h0, h1 = data[:half], data[half:]
    g0 = cyclic(h0, axis, 1)
    g1 = cyclic(h1, axis, -1)
    a0 = jnp.where(rel == 1, g0, h0)
    a1 = jnp.where(rel == 3, g1, h1)
    r_p = cyclic(jnp.where(rel == 0, h1, a0), axis, 1)
    r_m = cyclic(jnp.where(rel == 0, h0, a1), axis, -1)
    out0 = jnp.where(rel == 0, h0, jnp.where(rel == 1, g0, jnp.where(rel == 2, r_p, r_m)))
    out1 = jnp.where(rel == 0, h1, jnp.where(rel == 1, r_p, jnp.where(rel == 2, r_m, g1)))
    return jnp.concatenate([out0, out1], axis=0)


def sink_broadcast(data, sink):
    n_frame = lax.axis_size(FRAME_AXES)
    piece = data.shape[0] // n_frame
    spread = lax.all_to_all(data, FRAME_AXES, 0, 0, tiled=True)
    mine = lax.dynamic_slice_in_dim(spread, sink * piece, piece, axis=0)
    return lax.all_gather(mine, FRAME_AXES, axis=0, tiled=True)


def shards(queries, keys, values, out_weight, sink_owner, frame_pos):
    count = queries.shape[0]
    angle = pair_angles(frame_pos[0], count)
    rot_k = rotate(keys, angle)
    place = frame_index()
    n_frame = lax.axis_size(FRAME_AXES)
    sink = sink_owner[0] % (n_frame // 2)
    prev_k, prev_v = shifted((rot_k, values), FRAME_AXES, 1)
    sink_kv = sink_broadcast(jnp.concatenate([rot_k, values], axis=0), sink)
    sink_k, sink_v = sink_kv[:count], sink_kv[count:]
    rot_q = rotate(queries, angle)
    prev_used = (place >= 1) & (place - 1 != sink)
    sink_used = sink < place
    m_self, l_self, o_self = attend_block(rot_q, rot_k, values)
    m_prev, l_prev, o_prev = attend_block(rot_q, prev_k, prev_v)
    m_sink, l_sink, o_sink = attend_block(rot_q, sink_k, sink_v)
    top = jnp.maximum(m_self, jnp.where(prev_used, m_prev, m_self))
    top = jnp.maximum(top, jnp.where(sink_used, m_sink, m_self))
    c_self = jnp.exp(m_self - top)
    c_prev = jnp.where(prev_used, jnp.exp(m_prev - top), 0.0)
    c_sink = jnp.where(sink_used, jnp.exp(m_sink - top), 0.0)
    numer = o_self * c_self[..., None] + o_prev * c_prev[..., None] + o_sink * c_sink[..., None]
    denom = l_self * c_self + l_prev * c_prev + l_sink * c_sink
    attended = (
        jnp.transpose(numer / denom[..., None], (1, 0, 2)).reshape(count, -1).astype(jnp.bfloat16)
    )
    terms = jnp.dot(attended, out_weight, preferred_element_type=jnp.float32)
    mixed = lax.psum_scatter(terms.astype(jnp.bfloat16), HEAD_AXES, scatter_dimension=1, tiled=True)
    return mixed


def solution(mesh):
    frame_phys = {"z": 4, "xh": 2, "y": 4}
    head_phys = {"xl": 2, "c": 2}
    assert mesh.shape["frame"] == 32 and mesh.shape["head"] == 4
    devices = mesh.devices.reshape(tuple(frame_phys.values()) + tuple(head_phys.values()))
    fine = Mesh(devices, FRAME_AXES + HEAD_AXES)
    in_specs = (
        P(FRAME_AXES, HEAD_AXES),
        P(FRAME_AXES, HEAD_AXES),
        P(FRAME_AXES, HEAD_AXES),
        P(HEAD_AXES, None),
        P(),
        P(FRAME_AXES),
    )
    out_specs = P(FRAME_AXES, HEAD_AXES)
    inner = jax.shard_map(shards, mesh=fine, in_specs=in_specs, out_specs=out_specs, check_vma=False)

    def run(*args):
        out = inner(*args)
        return jax.lax.with_sharding_constraint(out, NamedSharding(mesh, P("frame", "head")))

    return run
```

```python
import jax
import jax.numpy as jnp
from jax import lax
from jax.experimental import pallas as pl
from jax.experimental.pallas import tpu as pltpu
from jax.sharding import Mesh, NamedSharding, PartitionSpec as P

HDIM = 128
GRID_W = 32


def shifted(array, axis, by):
    length = lax.axis_size(axis)
    pairs = [(i, i + by) for i in range(length) if 0 <= i + by < length]
    return lax.ppermute(array, axis, pairs)


def broadcast(value, axis, source):
    kept = jnp.where(lax.axis_index(axis) == source, value, 0).astype(value.dtype)
    return lax.psum(kept, axis)


def pair_angles(frame_value, count):
    half = HDIM // 2
    tdim = HDIM - 4 * (HDIM // 6)
    sdim = 2 * (HDIM // 6)
    tcount = tdim // 2
    scount = sdim // 2
    index = jnp.arange(half)
    findex = index.astype(jnp.float32)
    freq = jnp.where(
        index < tcount,
        jnp.power(10000.0, -2.0 * findex / tdim),
        jnp.where(
            index < tcount + scount,
            jnp.power(10000.0, -2.0 * (findex - tcount) / sdim),
            jnp.power(10000.0, -2.0 * (findex - tcount - scount) / sdim),
        ),
    )
    token = jnp.arange(count)
    row_pos = (token // GRID_W).astype(jnp.float32)[:, None]
    col_pos = (token % GRID_W).astype(jnp.float32)[:, None]
    frame_f = jnp.zeros((count, 1), jnp.float32) + frame_value.astype(jnp.float32)
    pos = jnp.where(
        index[None, :] < tcount,
        frame_f,
        jnp.where(index[None, :] < tcount + scount, row_pos, col_pos),
    )
    return pos * freq[None, :]


def rotate(block, angle):
    count = block.shape[0]
    heads_here = block.shape[1] // HDIM
    parts = block.astype(jnp.float32).reshape(count, heads_here, HDIM // 2, 2)
    cosine = jnp.cos(angle)[:, None, :]
    sine = jnp.sin(angle)[:, None, :]
    first = parts[..., 0] * cosine - parts[..., 1] * sine
    second = parts[..., 0] * sine + parts[..., 1] * cosine
    return (
        jnp.stack([first, second], axis=-1).reshape(count, heads_here * HDIM).astype(jnp.bfloat16)
    )


def attend_block(query, key_block, value_block):
    count = query.shape[0]
    heads_here = query.shape[1] // HDIM
    qh = query.reshape(count, heads_here, HDIM)
    kh = key_block.reshape(-1, heads_here, HDIM)
    vh = value_block.reshape(-1, heads_here, HDIM)
    scores = jnp.einsum("qhd,khd->hqk", qh, kh, preferred_element_type=jnp.float32) / jnp.sqrt(
        jnp.float32(HDIM)
    )
    peak = jnp.max(scores, axis=-1)
    weights = jnp.exp(scores - peak[..., None]).astype(jnp.bfloat16)
    total = jnp.sum(weights.astype(jnp.float32), axis=-1)
    partial_value = jnp.einsum("hqk,khd->hqd", weights, vh, preferred_element_type=jnp.float32)
    return (peak, total, partial_value)


FRAME_AXES = ("z", "xh", "y")
HEAD_AXES = ("xl", "c")


def frame_index():
    return (lax.axis_index("z") * lax.axis_size("xh") + lax.axis_index("xh")) * lax.axis_size("y") + lax.axis_index(
        "y"
    )


def cyclic(array, axis, by):
    length = lax.axis_size(axis)
    return lax.ppermute(array, axis, [(i, (i + by) % length) for i in range(length)])


def ring_stage(data, axis, source):
    length = lax.axis_size(axis)
    if length == 1:
        return data
    rel = (lax.axis_index(axis) - source) % length
    if length == 2:
        got = cyclic(data, axis, 1)
        return jnp.where(rel == 0, data, got)
    assert length == 4
    half = data.shape[0] // 2
    h0, h1 = data[:half], data[half:]
    g0 = cyclic(h0, axis, 1)
    g1 = cyclic(h1, axis, -1)
    a0 = jnp.where(rel == 1, g0, h0)
    a1 = jnp.where(rel == 3, g1, h1)
    r_p = cyclic(jnp.where(rel == 0, h1, a0), axis, 1)
    r_m = cyclic(jnp.where(rel == 0, h0, a1), axis, -1)
    out0 = jnp.where(rel == 0, h0, jnp.where(rel == 1, g0, jnp.where(rel == 2, r_p, r_m)))
    out1 = jnp.where(rel == 0, h1, jnp.where(rel == 1, r_p, jnp.where(rel == 2, r_m, g1)))
    return jnp.concatenate([out0, out1], axis=0)


def sink_broadcast(data, sink):
    n_frame = lax.axis_size(FRAME_AXES)
    piece = data.shape[0] // n_frame
    spread = lax.all_to_all(data, FRAME_AXES, 0, 0, tiled=True)
    mine = lax.dynamic_slice_in_dim(spread, sink * piece, piece, axis=0)
    return lax.all_gather(mine, FRAME_AXES, axis=0, tiled=True)


def rope_tables(frame_value, count):
    angle = pair_angles(frame_value, count)
    cosine = jnp.cos(angle)
    sine = jnp.sin(angle)
    cos_full = jnp.stack([cosine, cosine], axis=-1).reshape(count, HDIM)
    sin_signed = jnp.stack([-sine, sine], axis=-1).reshape(count, HDIM)
    return cos_full, sin_signed


def attention_kernel(flags, q_ref, ks_ref, vs_ref, kp_ref, vp_ref, kk_ref, vk_ref, swap_ref, *rest):
    tables, out_ref = rest[:6], rest[6]
    swap = swap_ref[...]

    def rot(x_ref, cos_ref, sin_ref):
        x = x_ref[...]
        partner = jnp.dot(x, swap, preferred_element_type=jnp.float32)
        return (x.astype(jnp.float32) * cos_ref[...] + partner * sin_ref[...]).astype(jnp.bfloat16)

    q = rot(q_ref, tables[0], tables[1])
    scale = jnp.sqrt(jnp.float32(HDIM))

    def block(k_ref, v_ref, cos_ref, sin_ref):
        k = rot(k_ref, cos_ref, sin_ref)
        scores = lax.dot_general(q, k, (((1,), (1,)), ((), ())), preferred_element_type=jnp.float32) / scale
        peak = jnp.max(scores, axis=-1, keepdims=True)
        weights = jnp.exp(scores - peak).astype(jnp.bfloat16)
        total = jnp.sum(weights.astype(jnp.float32), axis=-1, keepdims=True)
        partial_value = jnp.dot(weights, v_ref[...], preferred_element_type=jnp.float32)
        return peak, total, partial_value

    m_self, l_self, o_self = block(ks_ref, vs_ref, tables[0], tables[1])
    m_prev, l_prev, o_prev = block(kp_ref, vp_ref, tables[2], tables[3])
    m_sink, l_sink, o_sink = block(kk_ref, vk_ref, tables[4], tables[5])
    prev_used = flags[0] != 0
    sink_used = flags[1] != 0
    top = jnp.maximum(m_self, jnp.where(prev_used, m_prev, m_self))
    top = jnp.maximum(top, jnp.where(sink_used, m_sink, m_self))
    c_self = jnp.exp(m_self - top)
    c_prev = jnp.where(prev_used, jnp.exp(m_prev - top), 0.0)
    c_sink = jnp.where(sink_used, jnp.exp(m_sink - top), 0.0)
    numer = o_self * c_self + o_prev * c_prev + o_sink * c_sink
    denom = l_self * c_self + l_prev * c_prev + l_sink * c_sink
    out_ref[...] = (numer / denom).astype(out_ref.dtype)


def attention(flags, queries, blocks, tables):
    count, width = queries.shape
    heads_here = width // HDIM
    lane = jnp.arange(HDIM)
    swap = (lane[:, None] == (lane[None, :] ^ 1)).astype(jnp.bfloat16)
    head_spec = pl.BlockSpec((count, HDIM), lambda h, flags: (0, h))
    whole_spec = pl.BlockSpec((count, HDIM), lambda h, flags: (0, 0))
    swap_spec = pl.BlockSpec((HDIM, HDIM), lambda h, flags: (0, 0))
    grid_spec = pltpu.PrefetchScalarGridSpec(
        num_scalar_prefetch=1,
        grid=(heads_here,),
        in_specs=[head_spec] * 7 + [swap_spec] + [whole_spec] * 6,
        out_specs=head_spec,
    )
    flops = heads_here * 3 * 4 * count * count * HDIM
    cost = pl.CostEstimate(
        flops=flops,
        transcendentals=heads_here * 3 * count * count,
        bytes_accessed=8 * count * width * 2 + 6 * count * HDIM * 4,
    )
    return pl.pallas_call(
        attention_kernel,
        grid_spec=grid_spec,
        out_shape=jax.ShapeDtypeStruct((count, width), jnp.bfloat16),
        cost_estimate=cost,
    )(flags, queries, *blocks, swap, *tables)


def shards(queries, keys, values, out_weight, sink_owner, frame_pos):
    count = queries.shape[0]
    place = frame_index()
    n_frame = lax.axis_size(FRAME_AXES)
    sink = sink_owner[0] % (n_frame // 2)
    sink_kv = sink_broadcast(jnp.concatenate([keys, values], axis=0), sink)
    prev_k, prev_v = shifted((keys, values), FRAME_AXES, 1)
    positions = lax.all_gather(frame_pos, FRAME_AXES, axis=0, tiled=True)
    prev_used = (place >= 1) & (place - 1 != sink)
    sink_used = sink < place
    flags = jnp.stack([prev_used, sink_used]).astype(jnp.int32)
    tables = (
        rope_tables(frame_pos[0], count)
        + rope_tables(positions[jnp.maximum(place - 1, 0)], count)
        + rope_tables(positions[sink], count)
    )
    blocks = (keys, values, prev_k, prev_v, sink_kv[:count], sink_kv[count:])
    attended = attention(flags, queries, blocks, tables)
    terms = jnp.dot(attended, out_weight, preferred_element_type=jnp.float32)
    mixed = lax.psum_scatter(terms.astype(jnp.bfloat16), HEAD_AXES, scatter_dimension=1, tiled=True)
    return mixed


def solution(mesh):
    frame_phys = {"z": 4, "xh": 2, "y": 4}
    head_phys = {"xl": 2, "c": 2}
    assert mesh.shape["frame"] == 32 and mesh.shape["head"] == 4
    devices = mesh.devices.reshape(tuple(frame_phys.values()) + tuple(head_phys.values()))
    fine = Mesh(devices, FRAME_AXES + HEAD_AXES)
    in_specs = (
        P(FRAME_AXES, HEAD_AXES),
        P(FRAME_AXES, HEAD_AXES),
        P(FRAME_AXES, HEAD_AXES),
        P(HEAD_AXES, None),
        P(),
        P(FRAME_AXES),
    )
    out_specs = P(FRAME_AXES, HEAD_AXES)
    inner = jax.shard_map(shards, mesh=fine, in_specs=in_specs, out_specs=out_specs, check_vma=False)

    def run(*args):
        out = inner(*args)
        return jax.lax.with_sharding_constraint(out, NamedSharding(mesh, P("frame", "head")))

    return run
```

```python
import jax
import jax.numpy as jnp
from jax import lax
from jax.experimental import pallas as pl
from jax.experimental.pallas import tpu as pltpu
from jax.sharding import Mesh, NamedSharding, PartitionSpec as P

HDIM = 128
GRID_W = 32


def shifted(array, axis, by):
    length = lax.axis_size(axis)
    pairs = [(i, i + by) for i in range(length) if 0 <= i + by < length]
    return lax.ppermute(array, axis, pairs)


def broadcast(value, axis, source):
    kept = jnp.where(lax.axis_index(axis) == source, value, 0).astype(value.dtype)
    return lax.psum(kept, axis)


def pair_angles(frame_value, count):
    half = HDIM // 2
    tdim = HDIM - 4 * (HDIM // 6)
    sdim = 2 * (HDIM // 6)
    tcount = tdim // 2
    scount = sdim // 2
    index = jnp.arange(half)
    findex = index.astype(jnp.float32)
    freq = jnp.where(
        index < tcount,
        jnp.power(10000.0, -2.0 * findex / tdim),
        jnp.where(
            index < tcount + scount,
            jnp.power(10000.0, -2.0 * (findex - tcount) / sdim),
            jnp.power(10000.0, -2.0 * (findex - tcount - scount) / sdim),
        ),
    )
    token = jnp.arange(count)
    row_pos = (token // GRID_W).astype(jnp.float32)[:, None]
    col_pos = (token % GRID_W).astype(jnp.float32)[:, None]
    frame_f = jnp.zeros((count, 1), jnp.float32) + frame_value.astype(jnp.float32)
    pos = jnp.where(
        index[None, :] < tcount,
        frame_f,
        jnp.where(index[None, :] < tcount + scount, row_pos, col_pos),
    )
    return pos * freq[None, :]


def rotate(block, angle):
    count = block.shape[0]
    heads_here = block.shape[1] // HDIM
    parts = block.astype(jnp.float32).reshape(count, heads_here, HDIM // 2, 2)
    cosine = jnp.cos(angle)[:, None, :]
    sine = jnp.sin(angle)[:, None, :]
    first = parts[..., 0] * cosine - parts[..., 1] * sine
    second = parts[..., 0] * sine + parts[..., 1] * cosine
    return (
        jnp.stack([first, second], axis=-1).reshape(count, heads_here * HDIM).astype(jnp.bfloat16)
    )


def attend_block(query, key_block, value_block):
    count = query.shape[0]
    heads_here = query.shape[1] // HDIM
    qh = query.reshape(count, heads_here, HDIM)
    kh = key_block.reshape(-1, heads_here, HDIM)
    vh = value_block.reshape(-1, heads_here, HDIM)
    scores = jnp.einsum("qhd,khd->hqk", qh, kh, preferred_element_type=jnp.float32) / jnp.sqrt(
        jnp.float32(HDIM)
    )
    peak = jnp.max(scores, axis=-1)
    weights = jnp.exp(scores - peak[..., None]).astype(jnp.bfloat16)
    total = jnp.sum(weights.astype(jnp.float32), axis=-1)
    partial_value = jnp.einsum("hqk,khd->hqd", weights, vh, preferred_element_type=jnp.float32)
    return (peak, total, partial_value)


FRAME_AXES = ("z", "xh", "y")
HEAD_AXES = ("xl", "c")


def frame_index():
    return (lax.axis_index("z") * lax.axis_size("xh") + lax.axis_index("xh")) * lax.axis_size("y") + lax.axis_index(
        "y"
    )


def cyclic(array, axis, by):
    length = lax.axis_size(axis)
    return lax.ppermute(array, axis, [(i, (i + by) % length) for i in range(length)])


def ring_stage(data, axis, source):
    length = lax.axis_size(axis)
    if length == 1:
        return data
    rel = (lax.axis_index(axis) - source) % length
    if length == 2:
        got = cyclic(data, axis, 1)
        return jnp.where(rel == 0, data, got)
    assert length == 4
    half = data.shape[0] // 2
    h0, h1 = data[:half], data[half:]
    g0 = cyclic(h0, axis, 1)
    g1 = cyclic(h1, axis, -1)
    a0 = jnp.where(rel == 1, g0, h0)
    a1 = jnp.where(rel == 3, g1, h1)
    r_p = cyclic(jnp.where(rel == 0, h1, a0), axis, 1)
    r_m = cyclic(jnp.where(rel == 0, h0, a1), axis, -1)
    out0 = jnp.where(rel == 0, h0, jnp.where(rel == 1, g0, jnp.where(rel == 2, r_p, r_m)))
    out1 = jnp.where(rel == 0, h1, jnp.where(rel == 1, r_p, jnp.where(rel == 2, r_m, g1)))
    return jnp.concatenate([out0, out1], axis=0)


def sink_broadcast(data, sink):
    n_frame = lax.axis_size(FRAME_AXES)
    piece = data.shape[0] // n_frame
    spread = lax.all_to_all(data, FRAME_AXES, 0, 0, tiled=True)
    mine = lax.dynamic_slice_in_dim(spread, sink * piece, piece, axis=0)
    copies = jnp.broadcast_to(mine[None], (n_frame,) + mine.shape).reshape(data.shape)
    return lax.all_to_all(copies, FRAME_AXES, 0, 0, tiled=True)


def rope_tables(frame_value, count):
    angle = pair_angles(frame_value, count)
    cosine = jnp.cos(angle)
    sine = jnp.sin(angle)
    cos_full = jnp.stack([cosine, cosine], axis=-1).reshape(count, HDIM)
    sin_signed = jnp.stack([-sine, sine], axis=-1).reshape(count, HDIM)
    return cos_full, sin_signed


def attention_kernel(flags, q_ref, ks_ref, vs_ref, kp_ref, vp_ref, kk_ref, vk_ref, swap_ref, *rest):
    tables, out_ref = rest[:6], rest[6]
    swap = swap_ref[...]

    def rot(x_ref, cos_ref, sin_ref):
        x = x_ref[...]
        partner = jnp.dot(x, swap, preferred_element_type=jnp.float32)
        return (x.astype(jnp.float32) * cos_ref[...] + partner * sin_ref[...]).astype(jnp.bfloat16)

    q = rot(q_ref, tables[0], tables[1])
    scale = jnp.sqrt(jnp.float32(HDIM))

    def block(k_ref, v_ref, cos_ref, sin_ref):
        k = rot(k_ref, cos_ref, sin_ref)
        scores = lax.dot_general(q, k, (((1,), (1,)), ((), ())), preferred_element_type=jnp.float32) / scale
        peak = jnp.max(scores, axis=-1, keepdims=True)
        weights = jnp.exp(scores - peak).astype(jnp.bfloat16)
        total = jnp.sum(weights.astype(jnp.float32), axis=-1, keepdims=True)
        partial_value = jnp.dot(weights, v_ref[...], preferred_element_type=jnp.float32)
        return peak, total, partial_value

    m_self, l_self, o_self = block(ks_ref, vs_ref, tables[0], tables[1])
    m_prev, l_prev, o_prev = block(kp_ref, vp_ref, tables[2], tables[3])
    m_sink, l_sink, o_sink = block(kk_ref, vk_ref, tables[4], tables[5])
    prev_used = flags[0] != 0
    sink_used = flags[1] != 0
    top = jnp.maximum(m_self, jnp.where(prev_used, m_prev, m_self))
    top = jnp.maximum(top, jnp.where(sink_used, m_sink, m_self))
    c_self = jnp.exp(m_self - top)
    c_prev = jnp.where(prev_used, jnp.exp(m_prev - top), 0.0)
    c_sink = jnp.where(sink_used, jnp.exp(m_sink - top), 0.0)
    numer = o_self * c_self + o_prev * c_prev + o_sink * c_sink
    denom = l_self * c_self + l_prev * c_prev + l_sink * c_sink
    out_ref[...] = (numer / denom).astype(out_ref.dtype)


def attention(flags, queries, blocks, tables):
    count, width = queries.shape
    heads_here = width // HDIM
    lane = jnp.arange(HDIM)
    swap = (lane[:, None] == (lane[None, :] ^ 1)).astype(jnp.bfloat16)
    head_spec = pl.BlockSpec((count, HDIM), lambda h, flags: (0, h))
    whole_spec = pl.BlockSpec((count, HDIM), lambda h, flags: (0, 0))
    swap_spec = pl.BlockSpec((HDIM, HDIM), lambda h, flags: (0, 0))
    grid_spec = pltpu.PrefetchScalarGridSpec(
        num_scalar_prefetch=1,
        grid=(heads_here,),
        in_specs=[head_spec] * 7 + [swap_spec] + [whole_spec] * 6,
        out_specs=head_spec,
    )
    flops = heads_here * 3 * 4 * count * count * HDIM
    cost = pl.CostEstimate(
        flops=flops,
        transcendentals=heads_here * 3 * count * count,
        bytes_accessed=8 * count * width * 2 + 6 * count * HDIM * 4,
    )
    return pl.pallas_call(
        attention_kernel,
        grid_spec=grid_spec,
        out_shape=jax.ShapeDtypeStruct((count, width), jnp.bfloat16),
        cost_estimate=cost,
    )(flags, queries, *blocks, swap, *tables)


def shards(queries, keys, values, out_weight, sink_owner, frame_pos):
    count = queries.shape[0]
    place = frame_index()
    n_frame = lax.axis_size(FRAME_AXES)
    sink = sink_owner[0] % (n_frame // 2)
    sink_kv = sink_broadcast(jnp.concatenate([keys, values], axis=0), sink)
    prev_k, prev_v = shifted((keys, values), FRAME_AXES, 1)
    own_pos = jnp.broadcast_to(frame_pos[:1, None], (n_frame, 128))
    positions = lax.all_to_all(own_pos, FRAME_AXES, 0, 0, tiled=True)[:, 0]
    prev_used = (place >= 1) & (place - 1 != sink)
    sink_used = sink < place
    flags = jnp.stack([prev_used, sink_used]).astype(jnp.int32)
    tables = (
        rope_tables(frame_pos[0], count)
        + rope_tables(positions[jnp.maximum(place - 1, 0)], count)
        + rope_tables(positions[sink], count)
    )
    blocks = (keys, values, prev_k, prev_v, sink_kv[:count], sink_kv[count:])
    attended = attention(flags, queries, blocks, tables)
    terms = jnp.dot(attended, out_weight, preferred_element_type=jnp.float32)
    mixed = lax.psum_scatter(terms.astype(jnp.bfloat16), HEAD_AXES, scatter_dimension=1, tiled=True)
    return mixed


def solution(mesh):
    frame_phys = {"z": 4, "xh": 2, "y": 4}
    head_phys = {"xl": 2, "c": 2}
    assert mesh.shape["frame"] == 32 and mesh.shape["head"] == 4
    devices = mesh.devices.reshape(tuple(frame_phys.values()) + tuple(head_phys.values()))
    fine = Mesh(devices, FRAME_AXES + HEAD_AXES)
    in_specs = (
        P(FRAME_AXES, HEAD_AXES),
        P(FRAME_AXES, HEAD_AXES),
        P(FRAME_AXES, HEAD_AXES),
        P(HEAD_AXES, None),
        P(),
        P(FRAME_AXES),
    )
    out_specs = P(FRAME_AXES, HEAD_AXES)
    inner = jax.shard_map(shards, mesh=fine, in_specs=in_specs, out_specs=out_specs, check_vma=False)

    def run(*args):
        out = inner(*args)
        return jax.lax.with_sharding_constraint(out, NamedSharding(mesh, P("frame", "head")))

    return run
```

```python
import jax
import jax.numpy as jnp
from jax import lax
from jax.experimental import pallas as pl
from jax.experimental.pallas import tpu as pltpu
from jax.sharding import Mesh, NamedSharding, PartitionSpec as P

HDIM = 128
GRID_W = 32


def shifted(array, axis, by):
    length = lax.axis_size(axis)
    pairs = [(i, i + by) for i in range(length) if 0 <= i + by < length]
    return lax.ppermute(array, axis, pairs)


def broadcast(value, axis, source):
    kept = jnp.where(lax.axis_index(axis) == source, value, 0).astype(value.dtype)
    return lax.psum(kept, axis)


def pair_angles(frame_value, count):
    half = HDIM // 2
    tdim = HDIM - 4 * (HDIM // 6)
    sdim = 2 * (HDIM // 6)
    tcount = tdim // 2
    scount = sdim // 2
    index = jnp.arange(half)
    findex = index.astype(jnp.float32)
    freq = jnp.where(
        index < tcount,
        jnp.power(10000.0, -2.0 * findex / tdim),
        jnp.where(
            index < tcount + scount,
            jnp.power(10000.0, -2.0 * (findex - tcount) / sdim),
            jnp.power(10000.0, -2.0 * (findex - tcount - scount) / sdim),
        ),
    )
    token = jnp.arange(count)
    row_pos = (token // GRID_W).astype(jnp.float32)[:, None]
    col_pos = (token % GRID_W).astype(jnp.float32)[:, None]
    frame_f = jnp.zeros((count, 1), jnp.float32) + frame_value.astype(jnp.float32)
    pos = jnp.where(
        index[None, :] < tcount,
        frame_f,
        jnp.where(index[None, :] < tcount + scount, row_pos, col_pos),
    )
    return pos * freq[None, :]


def rotate(block, angle):
    count = block.shape[0]
    heads_here = block.shape[1] // HDIM
    parts = block.astype(jnp.float32).reshape(count, heads_here, HDIM // 2, 2)
    cosine = jnp.cos(angle)[:, None, :]
    sine = jnp.sin(angle)[:, None, :]
    first = parts[..., 0] * cosine - parts[..., 1] * sine
    second = parts[..., 0] * sine + parts[..., 1] * cosine
    return (
        jnp.stack([first, second], axis=-1).reshape(count, heads_here * HDIM).astype(jnp.bfloat16)
    )


def attend_block(query, key_block, value_block):
    count = query.shape[0]
    heads_here = query.shape[1] // HDIM
    qh = query.reshape(count, heads_here, HDIM)
    kh = key_block.reshape(-1, heads_here, HDIM)
    vh = value_block.reshape(-1, heads_here, HDIM)
    scores = jnp.einsum("qhd,khd->hqk", qh, kh, preferred_element_type=jnp.float32) / jnp.sqrt(
        jnp.float32(HDIM)
    )
    peak = jnp.max(scores, axis=-1)
    weights = jnp.exp(scores - peak[..., None]).astype(jnp.bfloat16)
    total = jnp.sum(weights.astype(jnp.float32), axis=-1)
    partial_value = jnp.einsum("hqk,khd->hqd", weights, vh, preferred_element_type=jnp.float32)
    return (peak, total, partial_value)


FRAME_AXES = ("z", "xh", "y")
HEAD_AXES = ("xl", "c")


def frame_index():
    return (lax.axis_index("z") * lax.axis_size("xh") + lax.axis_index("xh")) * lax.axis_size("y") + lax.axis_index(
        "y"
    )


def cyclic(array, axis, by):
    length = lax.axis_size(axis)
    return lax.ppermute(array, axis, [(i, (i + by) % length) for i in range(length)])


def ring_stage(data, axis, source):
    length = lax.axis_size(axis)
    if length == 1:
        return data
    rel = (lax.axis_index(axis) - source) % length
    if length == 2:
        got = cyclic(data, axis, 1)
        return jnp.where(rel == 0, data, got)
    assert length == 4
    half = data.shape[0] // 2
    h0, h1 = data[:half], data[half:]
    g0 = cyclic(h0, axis, 1)
    g1 = cyclic(h1, axis, -1)
    a0 = jnp.where(rel == 1, g0, h0)
    a1 = jnp.where(rel == 3, g1, h1)
    r_p = cyclic(jnp.where(rel == 0, h1, a0), axis, 1)
    r_m = cyclic(jnp.where(rel == 0, h0, a1), axis, -1)
    out0 = jnp.where(rel == 0, h0, jnp.where(rel == 1, g0, jnp.where(rel == 2, r_p, r_m)))
    out1 = jnp.where(rel == 0, h1, jnp.where(rel == 1, r_p, jnp.where(rel == 2, r_m, g1)))
    return jnp.concatenate([out0, out1], axis=0)


def sink_broadcast(data, sink):
    n_frame = lax.axis_size(FRAME_AXES)
    piece = data.shape[0] // n_frame
    spread = lax.all_to_all(data, FRAME_AXES, 0, 0, tiled=True)
    mine = lax.dynamic_slice_in_dim(spread, sink * piece, piece, axis=0)
    copies = jnp.broadcast_to(mine[None], (n_frame,) + mine.shape).reshape(data.shape)
    return lax.all_to_all(copies, FRAME_AXES, 0, 0, tiled=True)


def rope_tables(frame_value, count):
    angle = pair_angles(frame_value, count)
    cosine = jnp.cos(angle)
    sine = jnp.sin(angle)
    cos_full = jnp.stack([cosine, cosine], axis=-1).reshape(count, HDIM)
    sin_signed = jnp.stack([-sine, sine], axis=-1).reshape(count, HDIM)
    return cos_full, sin_signed


def rotate_ref(x_ref, cos_ref, sin_ref, swap):
    x = x_ref[...]
    partner = jnp.dot(x, swap, preferred_element_type=jnp.float32)
    return (x.astype(jnp.float32) * cos_ref[...] + partner * sin_ref[...]).astype(jnp.bfloat16)


def attend_ref(q, k, v_ref):
    scale = jnp.sqrt(jnp.float32(HDIM))
    scores = lax.dot_general(q, k, (((1,), (1,)), ((), ())), preferred_element_type=jnp.float32) / scale
    peak = jnp.max(scores, axis=-1, keepdims=True)
    weights = jnp.exp(scores - peak).astype(jnp.bfloat16)
    total = jnp.sum(weights.astype(jnp.float32), axis=-1, keepdims=True)
    partial_value = jnp.dot(weights, v_ref[...], preferred_element_type=jnp.float32)
    return peak, total, partial_value


def near_kernel(flags, q_ref, ks_ref, vs_ref, kp_ref, vp_ref, swap_ref, cq, sq, cp, sp, m_ref, l_ref, o_ref):
    swap = swap_ref[...]
    q = rotate_ref(q_ref, cq, sq, swap)
    m_self, l_self, o_self = attend_ref(q, rotate_ref(ks_ref, cq, sq, swap), vs_ref)
    m_prev, l_prev, o_prev = attend_ref(q, rotate_ref(kp_ref, cp, sp, swap), vp_ref)
    prev_used = flags[0] != 0
    top = jnp.maximum(m_self, jnp.where(prev_used, m_prev, m_self))
    c_self = jnp.exp(m_self - top)
    c_prev = jnp.where(prev_used, jnp.exp(m_prev - top), 0.0)
    m_ref[...] = jnp.broadcast_to(top, m_ref.shape)
    l_ref[...] = jnp.broadcast_to(l_self * c_self + l_prev * c_prev, l_ref.shape)
    o_ref[...] = o_self * c_self + o_prev * c_prev


def sink_kernel(flags, q_ref, kk_ref, vk_ref, swap_ref, cq, sq, ck, sk, m_ref, l_ref, o_ref, out_ref):
    swap = swap_ref[...]
    q = rotate_ref(q_ref, cq, sq, swap)
    m_sink, l_sink, o_sink = attend_ref(q, rotate_ref(kk_ref, ck, sk, swap), vk_ref)
    sink_used = flags[1] != 0
    m_near = m_ref[:, :1]
    top = jnp.maximum(m_near, jnp.where(sink_used, m_sink, m_near))
    c_near = jnp.exp(m_near - top)
    c_sink = jnp.where(sink_used, jnp.exp(m_sink - top), 0.0)
    numer = o_ref[...] * c_near + o_sink * c_sink
    denom = l_ref[:, :1] * c_near + l_sink * c_sink
    out_ref[...] = (numer / denom).astype(out_ref.dtype)


def specs(count):
    head = pl.BlockSpec((count, HDIM), lambda h, flags: (0, h))
    whole = pl.BlockSpec((count, HDIM), lambda h, flags: (0, 0))
    swap = pl.BlockSpec((HDIM, HDIM), lambda h, flags: (0, 0))
    return head, whole, swap


def swap_matrix():
    lane = jnp.arange(HDIM)
    return (lane[:, None] == (lane[None, :] ^ 1)).astype(jnp.bfloat16)


def near_attention(flags, queries, blocks, tables):
    count, width = queries.shape
    heads_here = width // HDIM
    head, whole, swap = specs(count)
    grid_spec = pltpu.PrefetchScalarGridSpec(
        num_scalar_prefetch=1,
        grid=(heads_here,),
        in_specs=[head] * 5 + [swap] + [whole] * 4,
        out_specs=[head] * 3,
    )
    cost = pl.CostEstimate(
        flops=heads_here * 2 * 4 * count * count * HDIM,
        transcendentals=heads_here * 2 * count * count,
        bytes_accessed=5 * count * width * 2 + 3 * count * width * 4,
    )
    f32 = jax.ShapeDtypeStruct((count, width), jnp.float32)
    return pl.pallas_call(
        near_kernel, grid_spec=grid_spec, out_shape=[f32] * 3, cost_estimate=cost
    )(flags, queries, *blocks, swap_matrix(), *tables)


def sink_attention(flags, queries, blocks, tables, near):
    count, width = queries.shape
    heads_here = width // HDIM
    head, whole, swap = specs(count)
    grid_spec = pltpu.PrefetchScalarGridSpec(
        num_scalar_prefetch=1,
        grid=(heads_here,),
        in_specs=[head] * 3 + [swap] + [whole] * 4 + [head] * 3,
        out_specs=head,
    )
    cost = pl.CostEstimate(
        flops=heads_here * 4 * count * count * HDIM,
        transcendentals=heads_here * count * count,
        bytes_accessed=4 * count * width * 2 + 3 * count * width * 4,
    )
    return pl.pallas_call(
        sink_kernel,
        grid_spec=grid_spec,
        out_shape=jax.ShapeDtypeStruct((count, width), jnp.bfloat16),
        cost_estimate=cost,
    )(flags, queries, *blocks, swap_matrix(), *tables, *near)


def shards(queries, keys, values, out_weight, sink_owner, frame_pos):
    count = queries.shape[0]
    place = frame_index()
    n_frame = lax.axis_size(FRAME_AXES)
    sink = sink_owner[0] % (n_frame // 2)
    prev_k, prev_v = shifted((keys, values), FRAME_AXES, 1)
    payload, prev_k, prev_v = lax.optimization_barrier((jnp.concatenate([keys, values], axis=0), prev_k, prev_v))
    sink_kv = sink_broadcast(payload, sink)
    own_pos = jnp.broadcast_to(frame_pos[:1, None], (n_frame, 128))
    positions = lax.all_to_all(own_pos, FRAME_AXES, 0, 0, tiled=True)[:, 0]
    prev_used = (place >= 1) & (place - 1 != sink)
    sink_used = sink < place
    flags = jnp.stack([prev_used, sink_used]).astype(jnp.int32)
    own_tables = rope_tables(frame_pos[0], count)
    prev_tables = rope_tables(positions[jnp.maximum(place - 1, 0)], count)
    sink_tables = rope_tables(positions[sink], count)
    near = near_attention(flags, queries, (keys, values, prev_k, prev_v), own_tables + prev_tables)
    attended = sink_attention(flags, queries, (sink_kv[:count], sink_kv[count:]), own_tables + sink_tables, near)
    terms = jnp.dot(attended, out_weight, preferred_element_type=jnp.float32)
    mixed = lax.psum_scatter(terms.astype(jnp.bfloat16), HEAD_AXES, scatter_dimension=1, tiled=True)
    return mixed


def solution(mesh):
    frame_phys = {"z": 4, "xh": 2, "y": 4}
    head_phys = {"xl": 2, "c": 2}
    assert mesh.shape["frame"] == 32 and mesh.shape["head"] == 4
    devices = mesh.devices.reshape(tuple(frame_phys.values()) + tuple(head_phys.values()))
    fine = Mesh(devices, FRAME_AXES + HEAD_AXES)
    in_specs = (
        P(FRAME_AXES, HEAD_AXES),
        P(FRAME_AXES, HEAD_AXES),
        P(FRAME_AXES, HEAD_AXES),
        P(HEAD_AXES, None),
        P(),
        P(FRAME_AXES),
    )
    out_specs = P(FRAME_AXES, HEAD_AXES)
    inner = jax.shard_map(shards, mesh=fine, in_specs=in_specs, out_specs=out_specs, check_vma=False)

    def run(*args):
        out = inner(*args)
        return jax.lax.with_sharding_constraint(out, NamedSharding(mesh, P("frame", "head")))

    return run
```

```python
import jax
import jax.numpy as jnp
from jax import lax
from jax.experimental import pallas as pl
from jax.experimental.pallas import tpu as pltpu
from jax.sharding import Mesh, NamedSharding, PartitionSpec as P

HDIM = 128
GRID_W = 32


def shifted(array, axis, by):
    length = lax.axis_size(axis)
    pairs = [(i, i + by) for i in range(length) if 0 <= i + by < length]
    return lax.ppermute(array, axis, pairs)


def broadcast(value, axis, source):
    kept = jnp.where(lax.axis_index(axis) == source, value, 0).astype(value.dtype)
    return lax.psum(kept, axis)


def pair_angles(frame_value, count):
    half = HDIM // 2
    tdim = HDIM - 4 * (HDIM // 6)
    sdim = 2 * (HDIM // 6)
    tcount = tdim // 2
    scount = sdim // 2
    index = jnp.arange(half)
    findex = index.astype(jnp.float32)
    freq = jnp.where(
        index < tcount,
        jnp.power(10000.0, -2.0 * findex / tdim),
        jnp.where(
            index < tcount + scount,
            jnp.power(10000.0, -2.0 * (findex - tcount) / sdim),
            jnp.power(10000.0, -2.0 * (findex - tcount - scount) / sdim),
        ),
    )
    token = jnp.arange(count)
    row_pos = (token // GRID_W).astype(jnp.float32)[:, None]
    col_pos = (token % GRID_W).astype(jnp.float32)[:, None]
    frame_f = jnp.zeros((count, 1), jnp.float32) + frame_value.astype(jnp.float32)
    pos = jnp.where(
        index[None, :] < tcount,
        frame_f,
        jnp.where(index[None, :] < tcount + scount, row_pos, col_pos),
    )
    return pos * freq[None, :]


def rotate(block, angle):
    count = block.shape[0]
    heads_here = block.shape[1] // HDIM
    parts = block.astype(jnp.float32).reshape(count, heads_here, HDIM // 2, 2)
    cosine = jnp.cos(angle)[:, None, :]
    sine = jnp.sin(angle)[:, None, :]
    first = parts[..., 0] * cosine - parts[..., 1] * sine
    second = parts[..., 0] * sine + parts[..., 1] * cosine
    return (
        jnp.stack([first, second], axis=-1).reshape(count, heads_here * HDIM).astype(jnp.bfloat16)
    )


def attend_block(query, key_block, value_block):
    count = query.shape[0]
    heads_here = query.shape[1] // HDIM
    qh = query.reshape(count, heads_here, HDIM)
    kh = key_block.reshape(-1, heads_here, HDIM)
    vh = value_block.reshape(-1, heads_here, HDIM)
    scores = jnp.einsum("qhd,khd->hqk", qh, kh, preferred_element_type=jnp.float32) / jnp.sqrt(
        jnp.float32(HDIM)
    )
    peak = jnp.max(scores, axis=-1)
    weights = jnp.exp(scores - peak[..., None]).astype(jnp.bfloat16)
    total = jnp.sum(weights.astype(jnp.float32), axis=-1)
    partial_value = jnp.einsum("hqk,khd->hqd", weights, vh, preferred_element_type=jnp.float32)
    return (peak, total, partial_value)


FRAME_AXES = ("z", "xh", "y")
HEAD_AXES = ("xl", "c")


def frame_index():
    return (lax.axis_index("z") * lax.axis_size("xh") + lax.axis_index("xh")) * lax.axis_size("y") + lax.axis_index(
        "y"
    )


def cyclic(array, axis, by):
    length = lax.axis_size(axis)
    return lax.ppermute(array, axis, [(i, (i + by) % length) for i in range(length)])


def ring_stage(data, axis, source):
    length = lax.axis_size(axis)
    if length == 1:
        return data
    rel = (lax.axis_index(axis) - source) % length
    if length == 2:
        got = cyclic(data, axis, 1)
        return jnp.where(rel == 0, data, got)
    assert length == 4
    half = data.shape[0] // 2
    h0, h1 = data[:half], data[half:]
    g0 = cyclic(h0, axis, 1)
    g1 = cyclic(h1, axis, -1)
    a0 = jnp.where(rel == 1, g0, h0)
    a1 = jnp.where(rel == 3, g1, h1)
    r_p = cyclic(jnp.where(rel == 0, h1, a0), axis, 1)
    r_m = cyclic(jnp.where(rel == 0, h0, a1), axis, -1)
    out0 = jnp.where(rel == 0, h0, jnp.where(rel == 1, g0, jnp.where(rel == 2, r_p, r_m)))
    out1 = jnp.where(rel == 0, h1, jnp.where(rel == 1, r_p, jnp.where(rel == 2, r_m, g1)))
    return jnp.concatenate([out0, out1], axis=0)


def sink_broadcast(data, sink):
    n_frame = lax.axis_size(FRAME_AXES)
    piece = data.shape[0] // n_frame
    spread = lax.all_to_all(data, FRAME_AXES, 0, 0, tiled=True)
    mine = lax.dynamic_slice_in_dim(spread, sink * piece, piece, axis=0)
    copies = jnp.broadcast_to(mine[None], (n_frame,) + mine.shape).reshape(data.shape)
    return lax.all_to_all(copies, FRAME_AXES, 0, 0, tiled=True)


def rope_tables(frame_value, count):
    angle = pair_angles(frame_value, count)
    cosine = jnp.cos(angle)
    sine = jnp.sin(angle)
    cos_full = jnp.stack([cosine, cosine], axis=-1).reshape(count, HDIM)
    sin_signed = jnp.stack([-sine, sine], axis=-1).reshape(count, HDIM)
    return cos_full, sin_signed


def rotate_ref(x_ref, cos_ref, sin_ref, swap):
    x = x_ref[...]
    partner = jnp.dot(x, swap, preferred_element_type=jnp.float32)
    return (x.astype(jnp.float32) * cos_ref[...] + partner * sin_ref[...]).astype(jnp.bfloat16)


def attend_ref(q, k, v_ref):
    scale = 1.0 / jnp.sqrt(jnp.float32(HDIM))
    raw = lax.dot_general(q, k, (((1,), (1,)), ((), ())), preferred_element_type=jnp.float32)
    raw_peak = jnp.max(raw, axis=-1, keepdims=True)
    peak = raw_peak * scale
    weights = jnp.exp((raw - raw_peak) * scale).astype(jnp.bfloat16)
    total = jnp.sum(weights.astype(jnp.float32), axis=-1, keepdims=True)
    partial_value = jnp.dot(weights, v_ref[...], preferred_element_type=jnp.float32)
    return peak, total, partial_value


def near_kernel(flags, q_ref, ks_ref, vs_ref, kp_ref, vp_ref, swap_ref, cq, sq, cp, sp, m_ref, l_ref, o_ref):
    swap = swap_ref[...]
    q = rotate_ref(q_ref, cq, sq, swap)
    m_self, l_self, o_self = attend_ref(q, rotate_ref(ks_ref, cq, sq, swap), vs_ref)
    m_prev, l_prev, o_prev = attend_ref(q, rotate_ref(kp_ref, cp, sp, swap), vp_ref)
    prev_used = flags[0] != 0
    top = jnp.maximum(m_self, jnp.where(prev_used, m_prev, m_self))
    c_self = jnp.exp(m_self - top)
    c_prev = jnp.where(prev_used, jnp.exp(m_prev - top), 0.0)
    m_ref[...] = jnp.broadcast_to(top, m_ref.shape)
    l_ref[...] = jnp.broadcast_to(l_self * c_self + l_prev * c_prev, l_ref.shape)
    o_ref[...] = o_self * c_self + o_prev * c_prev


def rope_kernel(x_ref, swap_ref, cos_ref, sin_ref, out_ref):
    out_ref[...] = rotate_ref(x_ref, cos_ref, sin_ref, swap_ref[...])


def rope(x, tables):
    count, width = x.shape
    head = pl.BlockSpec((count, HDIM), lambda h: (0, h))
    whole = pl.BlockSpec((count, HDIM), lambda h: (0, 0))
    swap = pl.BlockSpec((HDIM, HDIM), lambda h: (0, 0))
    return pl.pallas_call(
        rope_kernel,
        grid=(width // HDIM,),
        in_specs=[head, swap, whole, whole],
        out_specs=head,
        out_shape=jax.ShapeDtypeStruct((count, width), jnp.bfloat16),
        cost_estimate=pl.CostEstimate(flops=2 * count * width * HDIM, transcendentals=0, bytes_accessed=4 * count * width),
    )(x, swap_matrix(), *tables)


def sink_kernel(flags, q_ref, kk_ref, vk_ref, swap_ref, cq, sq, m_ref, l_ref, o_ref, out_ref):
    swap = swap_ref[...]
    q = rotate_ref(q_ref, cq, sq, swap)
    m_sink, l_sink, o_sink = attend_ref(q, kk_ref[...], vk_ref)
    sink_used = flags[1] != 0
    m_near = m_ref[:, :1]
    top = jnp.maximum(m_near, jnp.where(sink_used, m_sink, m_near))
    c_near = jnp.exp(m_near - top)
    c_sink = jnp.where(sink_used, jnp.exp(m_sink - top), 0.0)
    numer = o_ref[...] * c_near + o_sink * c_sink
    denom = l_ref[:, :1] * c_near + l_sink * c_sink
    out_ref[...] = (numer / denom).astype(out_ref.dtype)


def specs(count):
    head = pl.BlockSpec((count, HDIM), lambda h, flags: (0, h))
    whole = pl.BlockSpec((count, HDIM), lambda h, flags: (0, 0))
    swap = pl.BlockSpec((HDIM, HDIM), lambda h, flags: (0, 0))
    return head, whole, swap


def swap_matrix():
    lane = jnp.arange(HDIM)
    return (lane[:, None] == (lane[None, :] ^ 1)).astype(jnp.bfloat16)


def near_attention(flags, queries, blocks, tables):
    count, width = queries.shape
    heads_here = width // HDIM
    head, whole, swap = specs(count)
    grid_spec = pltpu.PrefetchScalarGridSpec(
        num_scalar_prefetch=1,
        grid=(heads_here,),
        in_specs=[head] * 5 + [swap] + [whole] * 4,
        out_specs=[head] * 3,
    )
    cost = pl.CostEstimate(
        flops=heads_here * 2 * 4 * count * count * HDIM,
        transcendentals=heads_here * 2 * count * count,
        bytes_accessed=5 * count * width * 2 + 3 * count * width * 4,
    )
    f32 = jax.ShapeDtypeStruct((count, width), jnp.float32)
    return pl.pallas_call(
        near_kernel, grid_spec=grid_spec, out_shape=[f32] * 3, cost_estimate=cost
    )(flags, queries, *blocks, swap_matrix(), *tables)


def sink_attention(flags, queries, blocks, tables, near):
    count, width = queries.shape
    heads_here = width // HDIM
    head, whole, swap = specs(count)
    grid_spec = pltpu.PrefetchScalarGridSpec(
        num_scalar_prefetch=1,
        grid=(heads_here,),
        in_specs=[head] * 3 + [swap] + [whole] * 2 + [head] * 3,
        out_specs=head,
    )
    cost = pl.CostEstimate(
        flops=heads_here * 4 * count * count * HDIM,
        transcendentals=heads_here * count * count,
        bytes_accessed=4 * count * width * 2 + 3 * count * width * 4,
    )
    return pl.pallas_call(
        sink_kernel,
        grid_spec=grid_spec,
        out_shape=jax.ShapeDtypeStruct((count, width), jnp.bfloat16),
        cost_estimate=cost,
    )(flags, queries, *blocks, swap_matrix(), *tables, *near)


def shards(queries, keys, values, out_weight, sink_owner, frame_pos):
    count = queries.shape[0]
    place = frame_index()
    n_frame = lax.axis_size(FRAME_AXES)
    sink = sink_owner[0] % (n_frame // 2)
    prev_k, prev_v, prev_pos = shifted((keys, values, frame_pos), FRAME_AXES, 1)
    own_tables = rope_tables(frame_pos[0], count)
    prev_tables = rope_tables(prev_pos[0], count)
    rot_k = rope(keys, own_tables)
    payload, prev_k, prev_v = lax.optimization_barrier((jnp.concatenate([rot_k, values], axis=0), prev_k, prev_v))
    sink_kv = sink_broadcast(payload, sink)
    prev_used = (place >= 1) & (place - 1 != sink)
    sink_used = sink < place
    flags = jnp.stack([prev_used, sink_used]).astype(jnp.int32)
    near = near_attention(flags, queries, (keys, values, prev_k, prev_v), own_tables + prev_tables)
    attended = sink_attention(flags, queries, (sink_kv[:count], sink_kv[count:]), own_tables, near)
    terms = jnp.dot(attended, out_weight, preferred_element_type=jnp.float32)
    mixed = lax.psum_scatter(terms.astype(jnp.bfloat16), HEAD_AXES, scatter_dimension=1, tiled=True)
    return mixed


def solution(mesh):
    frame_phys = {"z": 4, "xh": 2, "y": 4}
    head_phys = {"xl": 2, "c": 2}
    assert mesh.shape["frame"] == 32 and mesh.shape["head"] == 4
    devices = mesh.devices.reshape(tuple(frame_phys.values()) + tuple(head_phys.values()))
    fine = Mesh(devices, FRAME_AXES + HEAD_AXES)
    in_specs = (
        P(FRAME_AXES, HEAD_AXES),
        P(FRAME_AXES, HEAD_AXES),
        P(FRAME_AXES, HEAD_AXES),
        P(HEAD_AXES, None),
        P(),
        P(FRAME_AXES),
    )
    out_specs = P(FRAME_AXES, HEAD_AXES)
    inner = jax.shard_map(shards, mesh=fine, in_specs=in_specs, out_specs=out_specs, check_vma=False)

    def run(*args):
        out = inner(*args)
        return jax.lax.with_sharding_constraint(out, NamedSharding(mesh, P("frame", "head")))

    return run
```

```python
import jax
import jax.numpy as jnp
from jax import lax
from jax.experimental import pallas as pl
from jax.experimental.pallas import tpu as pltpu
from jax.sharding import Mesh, NamedSharding, PartitionSpec as P

HDIM = 128
GRID_W = 32


def shifted(array, axis, by):
    length = lax.axis_size(axis)
    pairs = [(i, i + by) for i in range(length) if 0 <= i + by < length]
    return lax.ppermute(array, axis, pairs)


def broadcast(value, axis, source):
    kept = jnp.where(lax.axis_index(axis) == source, value, 0).astype(value.dtype)
    return lax.psum(kept, axis)


def pair_angles(frame_value, count):
    half = HDIM // 2
    tdim = HDIM - 4 * (HDIM // 6)
    sdim = 2 * (HDIM // 6)
    tcount = tdim // 2
    scount = sdim // 2
    index = jnp.arange(half)
    findex = index.astype(jnp.float32)
    freq = jnp.where(
        index < tcount,
        jnp.power(10000.0, -2.0 * findex / tdim),
        jnp.where(
            index < tcount + scount,
            jnp.power(10000.0, -2.0 * (findex - tcount) / sdim),
            jnp.power(10000.0, -2.0 * (findex - tcount - scount) / sdim),
        ),
    )
    token = jnp.arange(count)
    row_pos = (token // GRID_W).astype(jnp.float32)[:, None]
    col_pos = (token % GRID_W).astype(jnp.float32)[:, None]
    frame_f = jnp.zeros((count, 1), jnp.float32) + frame_value.astype(jnp.float32)
    pos = jnp.where(
        index[None, :] < tcount,
        frame_f,
        jnp.where(index[None, :] < tcount + scount, row_pos, col_pos),
    )
    return pos * freq[None, :]


def rotate(block, angle):
    count = block.shape[0]
    heads_here = block.shape[1] // HDIM
    parts = block.astype(jnp.float32).reshape(count, heads_here, HDIM // 2, 2)
    cosine = jnp.cos(angle)[:, None, :]
    sine = jnp.sin(angle)[:, None, :]
    first = parts[..., 0] * cosine - parts[..., 1] * sine
    second = parts[..., 0] * sine + parts[..., 1] * cosine
    return (
        jnp.stack([first, second], axis=-1).reshape(count, heads_here * HDIM).astype(jnp.bfloat16)
    )


def attend_block(query, key_block, value_block):
    count = query.shape[0]
    heads_here = query.shape[1] // HDIM
    qh = query.reshape(count, heads_here, HDIM)
    kh = key_block.reshape(-1, heads_here, HDIM)
    vh = value_block.reshape(-1, heads_here, HDIM)
    scores = jnp.einsum("qhd,khd->hqk", qh, kh, preferred_element_type=jnp.float32) / jnp.sqrt(
        jnp.float32(HDIM)
    )
    peak = jnp.max(scores, axis=-1)
    weights = jnp.exp(scores - peak[..., None]).astype(jnp.bfloat16)
    total = jnp.sum(weights.astype(jnp.float32), axis=-1)
    partial_value = jnp.einsum("hqk,khd->hqd", weights, vh, preferred_element_type=jnp.float32)
    return (peak, total, partial_value)


FRAME_AXES = ("z", "xh", "y")
HEAD_AXES = ("xl", "c")


def frame_index():
    return (lax.axis_index("z") * lax.axis_size("xh") + lax.axis_index("xh")) * lax.axis_size("y") + lax.axis_index(
        "y"
    )


def cyclic(array, axis, by):
    length = lax.axis_size(axis)
    return lax.ppermute(array, axis, [(i, (i + by) % length) for i in range(length)])


def ring_stage(data, axis, source):
    length = lax.axis_size(axis)
    if length == 1:
        return data
    rel = (lax.axis_index(axis) - source) % length
    if length == 2:
        got = cyclic(data, axis, 1)
        return jnp.where(rel == 0, data, got)
    assert length == 4
    half = data.shape[0] // 2
    h0, h1 = data[:half], data[half:]
    g0 = cyclic(h0, axis, 1)
    g1 = cyclic(h1, axis, -1)
    a0 = jnp.where(rel == 1, g0, h0)
    a1 = jnp.where(rel == 3, g1, h1)
    r_p = cyclic(jnp.where(rel == 0, h1, a0), axis, 1)
    r_m = cyclic(jnp.where(rel == 0, h0, a1), axis, -1)
    out0 = jnp.where(rel == 0, h0, jnp.where(rel == 1, g0, jnp.where(rel == 2, r_p, r_m)))
    out1 = jnp.where(rel == 0, h1, jnp.where(rel == 1, r_p, jnp.where(rel == 2, r_m, g1)))
    return jnp.concatenate([out0, out1], axis=0)


def sink_broadcast(data, sink):
    n_frame = lax.axis_size(FRAME_AXES)
    piece = data.shape[0] // n_frame
    spread = lax.all_to_all(data, FRAME_AXES, 0, 0, tiled=True)
    mine = lax.dynamic_slice_in_dim(spread, sink * piece, piece, axis=0)
    copies = jnp.broadcast_to(mine[None], (n_frame,) + mine.shape).reshape(data.shape)
    return lax.all_to_all(copies, FRAME_AXES, 0, 0, tiled=True)


def rope_tables(frame_value, count):
    angle = pair_angles(frame_value, count)
    cosine = jnp.cos(angle)
    sine = jnp.sin(angle)
    cos_full = jnp.stack([cosine, cosine], axis=-1).reshape(count, HDIM)
    sin_signed = jnp.stack([-sine, sine], axis=-1).reshape(count, HDIM)
    return cos_full, sin_signed


def rotate_ref(x_ref, cos_ref, sin_ref, swap):
    x = x_ref[...]
    partner = jnp.dot(x, swap, preferred_element_type=jnp.float32)
    return (x.astype(jnp.float32) * cos_ref[...] + partner * sin_ref[...]).astype(jnp.bfloat16)


def attend_ref(q, k, v_ref):
    scale = 1.0 / jnp.sqrt(jnp.float32(HDIM))
    raw = lax.dot_general(q, k, (((1,), (1,)), ((), ())), preferred_element_type=jnp.float32)
    raw_peak = jnp.max(raw, axis=-1, keepdims=True)
    peak = raw_peak * scale
    weights = jnp.exp((raw - raw_peak) * scale).astype(jnp.bfloat16)
    total = jnp.sum(weights.astype(jnp.float32), axis=-1, keepdims=True)
    partial_value = jnp.dot(weights, v_ref[...], preferred_element_type=jnp.float32)
    return peak, total, partial_value


def near_kernel(flags, q_ref, ks_ref, vs_ref, kp_ref, vp_ref, swap_ref, cq, sq, cp, sp, m_ref, l_ref, o_ref):
    swap = swap_ref[...]
    q = rotate_ref(q_ref, cq, sq, swap)
    m_self, l_self, o_self = attend_ref(q, rotate_ref(ks_ref, cq, sq, swap), vs_ref)
    m_prev, l_prev, o_prev = attend_ref(q, rotate_ref(kp_ref, cp, sp, swap), vp_ref)
    prev_used = flags[0] != 0
    top = jnp.maximum(m_self, jnp.where(prev_used, m_prev, m_self))
    c_self = jnp.exp(m_self - top)
    c_prev = jnp.where(prev_used, jnp.exp(m_prev - top), 0.0)
    m_ref[...] = jnp.broadcast_to(top, m_ref.shape)
    l_ref[...] = jnp.broadcast_to(l_self * c_self + l_prev * c_prev, l_ref.shape)
    o_ref[...] = o_self * c_self + o_prev * c_prev


def rope_kernel(x_ref, swap_ref, cos_ref, sin_ref, out_ref):
    out_ref[...] = rotate_ref(x_ref, cos_ref, sin_ref, swap_ref[...])


def rope(x, tables):
    count, width = x.shape
    head = pl.BlockSpec((count, HDIM), lambda h: (0, h))
    whole = pl.BlockSpec((count, HDIM), lambda h: (0, 0))
    swap = pl.BlockSpec((HDIM, HDIM), lambda h: (0, 0))
    return pl.pallas_call(
        rope_kernel,
        grid=(width // HDIM,),
        in_specs=[head, swap, whole, whole],
        out_specs=head,
        out_shape=jax.ShapeDtypeStruct((count, width), jnp.bfloat16),
        cost_estimate=pl.CostEstimate(flops=2 * count * width * HDIM, transcendentals=0, bytes_accessed=4 * count * width),
    )(x, swap_matrix(), *tables)


def sink_kernel(flags, q_ref, kk_ref, vk_ref, swap_ref, cq, sq, m_ref, l_ref, o_ref, out_ref):
    swap = swap_ref[...]
    q = rotate_ref(q_ref, cq, sq, swap)
    m_sink, l_sink, o_sink = attend_ref(q, kk_ref[...], vk_ref)
    sink_used = flags[1] != 0
    m_near = m_ref[:, :1]
    top = jnp.maximum(m_near, jnp.where(sink_used, m_sink, m_near))
    c_near = jnp.exp(m_near - top)
    c_sink = jnp.where(sink_used, jnp.exp(m_sink - top), 0.0)
    numer = o_ref[...] * c_near + o_sink * c_sink
    denom = l_ref[:, :1] * c_near + l_sink * c_sink
    out_ref[...] = (numer / denom).astype(out_ref.dtype)


def specs(count):
    head = pl.BlockSpec((count, HDIM), lambda h, flags: (0, h))
    whole = pl.BlockSpec((count, HDIM), lambda h, flags: (0, 0))
    swap = pl.BlockSpec((HDIM, HDIM), lambda h, flags: (0, 0))
    return head, whole, swap


def swap_matrix():
    lane = jnp.arange(HDIM)
    return (lane[:, None] == (lane[None, :] ^ 1)).astype(jnp.bfloat16)


def near_attention(flags, queries, blocks, tables):
    count, width = queries.shape
    heads_here = width // HDIM
    head, whole, swap = specs(count)
    grid_spec = pltpu.PrefetchScalarGridSpec(
        num_scalar_prefetch=1,
        grid=(heads_here,),
        in_specs=[head] * 5 + [swap] + [whole] * 4,
        out_specs=[head] * 3,
    )
    cost = pl.CostEstimate(
        flops=heads_here * 2 * 4 * count * count * HDIM,
        transcendentals=heads_here * 2 * count * count,
        bytes_accessed=5 * count * width * 2 + 3 * count * width * 4,
    )
    f32 = jax.ShapeDtypeStruct((count, width), jnp.float32)
    return pl.pallas_call(
        near_kernel, grid_spec=grid_spec, out_shape=[f32] * 3, cost_estimate=cost
    )(flags, queries, *blocks, swap_matrix(), *tables)


def sink_attention(flags, queries, blocks, tables, near, half, halves):
    count, width = queries.shape
    heads_here = width // HDIM
    rows = count // halves
    part = pl.BlockSpec((rows, HDIM), lambda h, flags: (half, h))
    part_table = pl.BlockSpec((rows, HDIM), lambda h, flags: (half, 0))
    head = pl.BlockSpec((count, HDIM), lambda h, flags: (0, h))
    swap = pl.BlockSpec((HDIM, HDIM), lambda h, flags: (0, 0))
    grid_spec = pltpu.PrefetchScalarGridSpec(
        num_scalar_prefetch=1,
        grid=(heads_here,),
        in_specs=[part] + [head] * 2 + [swap] + [part_table] * 2 + [part] * 3,
        out_specs=pl.BlockSpec((rows, HDIM), lambda h, flags: (0, h)),
    )
    cost = pl.CostEstimate(
        flops=heads_here * 4 * rows * count * HDIM,
        transcendentals=heads_here * rows * count,
        bytes_accessed=(rows + 2 * count) * width * 2 + 3 * rows * width * 4,
    )
    return pl.pallas_call(
        sink_kernel,
        grid_spec=grid_spec,
        out_shape=jax.ShapeDtypeStruct((rows, width), jnp.bfloat16),
        cost_estimate=cost,
    )(flags, queries, *blocks, swap_matrix(), *tables, *near)


def shards(queries, keys, values, out_weight, sink_owner, frame_pos):
    count = queries.shape[0]
    place = frame_index()
    n_frame = lax.axis_size(FRAME_AXES)
    sink = sink_owner[0] % (n_frame // 2)
    prev_k, prev_v, prev_pos = shifted((keys, values, frame_pos), FRAME_AXES, 1)
    own_tables = rope_tables(frame_pos[0], count)
    prev_tables = rope_tables(prev_pos[0], count)
    rot_k = rope(keys, own_tables)
    payload, prev_k, prev_v = lax.optimization_barrier((jnp.concatenate([rot_k, values], axis=0), prev_k, prev_v))
    sink_kv = sink_broadcast(payload, sink)
    prev_used = (place >= 1) & (place - 1 != sink)
    sink_used = sink < place
    flags = jnp.stack([prev_used, sink_used]).astype(jnp.int32)
    near = near_attention(flags, queries, (keys, values, prev_k, prev_v), own_tables + prev_tables)
    halves = 2
    outs = []
    for half in range(halves):
        attended = sink_attention(flags, queries, (sink_kv[:count], sink_kv[count:]), own_tables, near, half, halves)
        terms = jnp.dot(attended, out_weight, preferred_element_type=jnp.float32)
        outs.append(lax.psum_scatter(terms.astype(jnp.bfloat16), HEAD_AXES, scatter_dimension=1, tiled=True))
    mixed = jnp.concatenate(outs, axis=0)
    return mixed


def solution(mesh):
    frame_phys = {"z": 4, "xh": 2, "y": 4}
    head_phys = {"xl": 2, "c": 2}
    assert mesh.shape["frame"] == 32 and mesh.shape["head"] == 4
    devices = mesh.devices.reshape(tuple(frame_phys.values()) + tuple(head_phys.values()))
    fine = Mesh(devices, FRAME_AXES + HEAD_AXES)
    in_specs = (
        P(FRAME_AXES, HEAD_AXES),
        P(FRAME_AXES, HEAD_AXES),
        P(FRAME_AXES, HEAD_AXES),
        P(HEAD_AXES, None),
        P(),
        P(FRAME_AXES),
    )
    out_specs = P(FRAME_AXES, HEAD_AXES)
    inner = jax.shard_map(shards, mesh=fine, in_specs=in_specs, out_specs=out_specs, check_vma=False)

    def run(*args):
        out = inner(*args)
        return jax.lax.with_sharding_constraint(out, NamedSharding(mesh, P("frame", "head")))

    return run
```

```python
import jax
import jax.numpy as jnp
from jax import lax
from jax.experimental import pallas as pl
from jax.experimental.pallas import tpu as pltpu
from jax.sharding import Mesh, NamedSharding, PartitionSpec as P

HDIM = 128
GRID_W = 32


def shifted(array, axis, by):
    length = lax.axis_size(axis)
    pairs = [(i, i + by) for i in range(length) if 0 <= i + by < length]
    return lax.ppermute(array, axis, pairs)


def broadcast(value, axis, source):
    kept = jnp.where(lax.axis_index(axis) == source, value, 0).astype(value.dtype)
    return lax.psum(kept, axis)


def pair_angles(frame_value, count):
    half = HDIM // 2
    tdim = HDIM - 4 * (HDIM // 6)
    sdim = 2 * (HDIM // 6)
    tcount = tdim // 2
    scount = sdim // 2
    index = jnp.arange(half)
    findex = index.astype(jnp.float32)
    freq = jnp.where(
        index < tcount,
        jnp.power(10000.0, -2.0 * findex / tdim),
        jnp.where(
            index < tcount + scount,
            jnp.power(10000.0, -2.0 * (findex - tcount) / sdim),
            jnp.power(10000.0, -2.0 * (findex - tcount - scount) / sdim),
        ),
    )
    token = jnp.arange(count)
    row_pos = (token // GRID_W).astype(jnp.float32)[:, None]
    col_pos = (token % GRID_W).astype(jnp.float32)[:, None]
    frame_f = jnp.zeros((count, 1), jnp.float32) + frame_value.astype(jnp.float32)
    pos = jnp.where(
        index[None, :] < tcount,
        frame_f,
        jnp.where(index[None, :] < tcount + scount, row_pos, col_pos),
    )
    return pos * freq[None, :]


def rotate(block, angle):
    count = block.shape[0]
    heads_here = block.shape[1] // HDIM
    parts = block.astype(jnp.float32).reshape(count, heads_here, HDIM // 2, 2)
    cosine = jnp.cos(angle)[:, None, :]
    sine = jnp.sin(angle)[:, None, :]
    first = parts[..., 0] * cosine - parts[..., 1] * sine
    second = parts[..., 0] * sine + parts[..., 1] * cosine
    return (
        jnp.stack([first, second], axis=-1).reshape(count, heads_here * HDIM).astype(jnp.bfloat16)
    )


def attend_block(query, key_block, value_block):
    count = query.shape[0]
    heads_here = query.shape[1] // HDIM
    qh = query.reshape(count, heads_here, HDIM)
    kh = key_block.reshape(-1, heads_here, HDIM)
    vh = value_block.reshape(-1, heads_here, HDIM)
    scores = jnp.einsum("qhd,khd->hqk", qh, kh, preferred_element_type=jnp.float32) / jnp.sqrt(
        jnp.float32(HDIM)
    )
    peak = jnp.max(scores, axis=-1)
    weights = jnp.exp(scores - peak[..., None]).astype(jnp.bfloat16)
    total = jnp.sum(weights.astype(jnp.float32), axis=-1)
    partial_value = jnp.einsum("hqk,khd->hqd", weights, vh, preferred_element_type=jnp.float32)
    return (peak, total, partial_value)


FRAME_AXES = ("z", "xh", "y")
HEAD_AXES = ("xl", "c")


def frame_index():
    return (lax.axis_index("z") * lax.axis_size("xh") + lax.axis_index("xh")) * lax.axis_size("y") + lax.axis_index(
        "y"
    )


def cyclic(array, axis, by):
    length = lax.axis_size(axis)
    return lax.ppermute(array, axis, [(i, (i + by) % length) for i in range(length)])


def ring_stage(data, axis, source):
    length = lax.axis_size(axis)
    if length == 1:
        return data
    rel = (lax.axis_index(axis) - source) % length
    if length == 2:
        got = cyclic(data, axis, 1)
        return jnp.where(rel == 0, data, got)
    assert length == 4
    half = data.shape[0] // 2
    h0, h1 = data[:half], data[half:]
    g0 = cyclic(h0, axis, 1)
    g1 = cyclic(h1, axis, -1)
    a0 = jnp.where(rel == 1, g0, h0)
    a1 = jnp.where(rel == 3, g1, h1)
    r_p = cyclic(jnp.where(rel == 0, h1, a0), axis, 1)
    r_m = cyclic(jnp.where(rel == 0, h0, a1), axis, -1)
    out0 = jnp.where(rel == 0, h0, jnp.where(rel == 1, g0, jnp.where(rel == 2, r_p, r_m)))
    out1 = jnp.where(rel == 0, h1, jnp.where(rel == 1, r_p, jnp.where(rel == 2, r_m, g1)))
    return jnp.concatenate([out0, out1], axis=0)


def exchange(data, sink):
    n_frame = lax.axis_size(FRAME_AXES)
    piece = data.shape[0] // n_frame
    spread = lax.all_to_all(data, FRAME_AXES, 0, 0, tiled=True)
    pieces = spread.reshape((n_frame, piece) + data.shape[1:])
    before = jnp.concatenate([pieces[-1:], pieces[:-1]], axis=0).reshape(data.shape)
    prev_full = lax.all_to_all(before, FRAME_AXES, 0, 0, tiled=True)
    mine = lax.dynamic_slice_in_dim(spread, sink * piece, piece, axis=0)
    copies = jnp.broadcast_to(mine[None], (n_frame,) + mine.shape).reshape(data.shape)
    copies, prev_full = lax.optimization_barrier((copies, prev_full))
    return prev_full, lax.all_to_all(copies, FRAME_AXES, 0, 0, tiled=True)


def rope_tables(frame_value, count):
    angle = pair_angles(frame_value, count)
    cosine = jnp.cos(angle)
    sine = jnp.sin(angle)
    cos_full = jnp.stack([cosine, cosine], axis=-1).reshape(count, HDIM)
    sin_signed = jnp.stack([-sine, sine], axis=-1).reshape(count, HDIM)
    return cos_full, sin_signed


def rotate_ref(x_ref, cos_ref, sin_ref, swap):
    x = x_ref[...]
    partner = jnp.dot(x, swap, preferred_element_type=jnp.float32)
    return (x.astype(jnp.float32) * cos_ref[...] + partner * sin_ref[...]).astype(jnp.bfloat16)


def attend_ref(q, k, v_ref):
    scale = 1.0 / jnp.sqrt(jnp.float32(HDIM))
    raw = lax.dot_general(q, k, (((1,), (1,)), ((), ())), preferred_element_type=jnp.float32)
    raw_peak = jnp.max(raw, axis=-1, keepdims=True)
    peak = raw_peak * scale
    weights = jnp.exp((raw - raw_peak) * scale).astype(jnp.bfloat16)
    total = jnp.sum(weights.astype(jnp.float32), axis=-1, keepdims=True)
    partial_value = jnp.dot(weights, v_ref[...], preferred_element_type=jnp.float32)
    return peak, total, partial_value


def near_kernel(flags, q_ref, ks_ref, vs_ref, kp_ref, vp_ref, swap_ref, cq, sq, m_ref, l_ref, o_ref):
    swap = swap_ref[...]
    q = rotate_ref(q_ref, cq, sq, swap)
    m_self, l_self, o_self = attend_ref(q, ks_ref[...], vs_ref)
    m_prev, l_prev, o_prev = attend_ref(q, kp_ref[...], vp_ref)
    prev_used = flags[0] != 0
    top = jnp.maximum(m_self, jnp.where(prev_used, m_prev, m_self))
    c_self = jnp.exp(m_self - top)
    c_prev = jnp.where(prev_used, jnp.exp(m_prev - top), 0.0)
    m_ref[...] = jnp.broadcast_to(top, m_ref.shape)
    l_ref[...] = jnp.broadcast_to(l_self * c_self + l_prev * c_prev, l_ref.shape)
    o_ref[...] = o_self * c_self + o_prev * c_prev


def rope_kernel(x_ref, swap_ref, cos_ref, sin_ref, out_ref):
    out_ref[...] = rotate_ref(x_ref, cos_ref, sin_ref, swap_ref[...])


def rope(x, tables):
    count, width = x.shape
    head = pl.BlockSpec((count, HDIM), lambda h: (0, h))
    whole = pl.BlockSpec((count, HDIM), lambda h: (0, 0))
    swap = pl.BlockSpec((HDIM, HDIM), lambda h: (0, 0))
    return pl.pallas_call(
        rope_kernel,
        grid=(width // HDIM,),
        in_specs=[head, swap, whole, whole],
        out_specs=head,
        out_shape=jax.ShapeDtypeStruct((count, width), jnp.bfloat16),
        cost_estimate=pl.CostEstimate(flops=2 * count * width * HDIM, transcendentals=0, bytes_accessed=4 * count * width),
    )(x, swap_matrix(), *tables)


def sink_kernel(flags, q_ref, kk_ref, vk_ref, swap_ref, cq, sq, m_ref, l_ref, o_ref, out_ref):
    swap = swap_ref[...]
    q = rotate_ref(q_ref, cq, sq, swap)
    m_sink, l_sink, o_sink = attend_ref(q, kk_ref[...], vk_ref)
    sink_used = flags[1] != 0
    m_near = m_ref[:, :1]
    top = jnp.maximum(m_near, jnp.where(sink_used, m_sink, m_near))
    c_near = jnp.exp(m_near - top)
    c_sink = jnp.where(sink_used, jnp.exp(m_sink - top), 0.0)
    numer = o_ref[...] * c_near + o_sink * c_sink
    denom = l_ref[:, :1] * c_near + l_sink * c_sink
    out_ref[...] = (numer / denom).astype(out_ref.dtype)


def specs(count):
    head = pl.BlockSpec((count, HDIM), lambda h, flags: (0, h))
    whole = pl.BlockSpec((count, HDIM), lambda h, flags: (0, 0))
    swap = pl.BlockSpec((HDIM, HDIM), lambda h, flags: (0, 0))
    return head, whole, swap


def swap_matrix():
    lane = jnp.arange(HDIM)
    return (lane[:, None] == (lane[None, :] ^ 1)).astype(jnp.bfloat16)


def near_attention(flags, queries, blocks, tables):
    count, width = queries.shape
    heads_here = width // HDIM
    head, whole, swap = specs(count)
    grid_spec = pltpu.PrefetchScalarGridSpec(
        num_scalar_prefetch=1,
        grid=(heads_here,),
        in_specs=[head] * 5 + [swap] + [whole] * 2,
        out_specs=[head] * 3,
    )
    cost = pl.CostEstimate(
        flops=heads_here * 2 * 4 * count * count * HDIM,
        transcendentals=heads_here * 2 * count * count,
        bytes_accessed=5 * count * width * 2 + 3 * count * width * 4,
    )
    f32 = jax.ShapeDtypeStruct((count, width), jnp.float32)
    return pl.pallas_call(
        near_kernel, grid_spec=grid_spec, out_shape=[f32] * 3, cost_estimate=cost
    )(flags, queries, *blocks, swap_matrix(), *tables)


def sink_attention(flags, queries, blocks, tables, near, half, halves):
    count, width = queries.shape
    heads_here = width // HDIM
    rows = count // halves
    part = pl.BlockSpec((rows, HDIM), lambda h, flags: (half, h))
    part_table = pl.BlockSpec((rows, HDIM), lambda h, flags: (half, 0))
    head = pl.BlockSpec((count, HDIM), lambda h, flags: (0, h))
    swap = pl.BlockSpec((HDIM, HDIM), lambda h, flags: (0, 0))
    grid_spec = pltpu.PrefetchScalarGridSpec(
        num_scalar_prefetch=1,
        grid=(heads_here,),
        in_specs=[part] + [head] * 2 + [swap] + [part_table] * 2 + [part] * 3,
        out_specs=pl.BlockSpec((rows, HDIM), lambda h, flags: (0, h)),
    )
    cost = pl.CostEstimate(
        flops=heads_here * 4 * rows * count * HDIM,
        transcendentals=heads_here * rows * count,
        bytes_accessed=(rows + 2 * count) * width * 2 + 3 * rows * width * 4,
    )
    return pl.pallas_call(
        sink_kernel,
        grid_spec=grid_spec,
        out_shape=jax.ShapeDtypeStruct((rows, width), jnp.bfloat16),
        cost_estimate=cost,
    )(flags, queries, *blocks, swap_matrix(), *tables, *near)


def shards(queries, keys, values, out_weight, sink_owner, frame_pos):
    count = queries.shape[0]
    place = frame_index()
    n_frame = lax.axis_size(FRAME_AXES)
    sink = sink_owner[0] % (n_frame // 2)
    own_tables = rope_tables(frame_pos[0], count)
    rot_k = rope(keys, own_tables)
    prev_kv, sink_kv = exchange(jnp.concatenate([rot_k, values], axis=0), sink)
    prev_used = (place >= 1) & (place - 1 != sink)
    sink_used = sink < place
    flags = jnp.stack([prev_used, sink_used]).astype(jnp.int32)
    near = near_attention(flags, queries, (rot_k, values, prev_kv[:count], prev_kv[count:]), own_tables)
    halves = 2
    outs = []
    for half in range(halves):
        attended = sink_attention(flags, queries, (sink_kv[:count], sink_kv[count:]), own_tables, near, half, halves)
        terms = jnp.dot(attended, out_weight, preferred_element_type=jnp.float32)
        outs.append(lax.psum_scatter(terms.astype(jnp.bfloat16), HEAD_AXES, scatter_dimension=1, tiled=True))
    mixed = jnp.concatenate(outs, axis=0)
    return mixed


def solution(mesh):
    frame_phys = {"z": 4, "xh": 2, "y": 4}
    head_phys = {"xl": 2, "c": 2}
    assert mesh.shape["frame"] == 32 and mesh.shape["head"] == 4
    devices = mesh.devices.reshape(tuple(frame_phys.values()) + tuple(head_phys.values()))
    fine = Mesh(devices, FRAME_AXES + HEAD_AXES)
    in_specs = (
        P(FRAME_AXES, HEAD_AXES),
        P(FRAME_AXES, HEAD_AXES),
        P(FRAME_AXES, HEAD_AXES),
        P(HEAD_AXES, None),
        P(),
        P(FRAME_AXES),
    )
    out_specs = P(FRAME_AXES, HEAD_AXES)
    inner = jax.shard_map(shards, mesh=fine, in_specs=in_specs, out_specs=out_specs, check_vma=False)

    def run(*args):
        out = inner(*args)
        return jax.lax.with_sharding_constraint(out, NamedSharding(mesh, P("frame", "head")))

    return run
```

```python
import jax
import jax.numpy as jnp
from jax import lax
from jax.experimental import pallas as pl
from jax.experimental.pallas import tpu as pltpu
from jax.sharding import Mesh, NamedSharding, PartitionSpec as P

HDIM = 128
GRID_W = 32


def shifted(array, axis, by):
    length = lax.axis_size(axis)
    pairs = [(i, i + by) for i in range(length) if 0 <= i + by < length]
    return lax.ppermute(array, axis, pairs)


def broadcast(value, axis, source):
    kept = jnp.where(lax.axis_index(axis) == source, value, 0).astype(value.dtype)
    return lax.psum(kept, axis)


def pair_angles(frame_value, count):
    half = HDIM // 2
    tdim = HDIM - 4 * (HDIM // 6)
    sdim = 2 * (HDIM // 6)
    tcount = tdim // 2
    scount = sdim // 2
    index = jnp.arange(half)
    findex = index.astype(jnp.float32)
    freq = jnp.where(
        index < tcount,
        jnp.power(10000.0, -2.0 * findex / tdim),
        jnp.where(
            index < tcount + scount,
            jnp.power(10000.0, -2.0 * (findex - tcount) / sdim),
            jnp.power(10000.0, -2.0 * (findex - tcount - scount) / sdim),
        ),
    )
    token = jnp.arange(count)
    row_pos = (token // GRID_W).astype(jnp.float32)[:, None]
    col_pos = (token % GRID_W).astype(jnp.float32)[:, None]
    frame_f = jnp.zeros((count, 1), jnp.float32) + frame_value.astype(jnp.float32)
    pos = jnp.where(
        index[None, :] < tcount,
        frame_f,
        jnp.where(index[None, :] < tcount + scount, row_pos, col_pos),
    )
    return pos * freq[None, :]


def rotate(block, angle):
    count = block.shape[0]
    heads_here = block.shape[1] // HDIM
    parts = block.astype(jnp.float32).reshape(count, heads_here, HDIM // 2, 2)
    cosine = jnp.cos(angle)[:, None, :]
    sine = jnp.sin(angle)[:, None, :]
    first = parts[..., 0] * cosine - parts[..., 1] * sine
    second = parts[..., 0] * sine + parts[..., 1] * cosine
    return (
        jnp.stack([first, second], axis=-1).reshape(count, heads_here * HDIM).astype(jnp.bfloat16)
    )


def attend_block(query, key_block, value_block):
    count = query.shape[0]
    heads_here = query.shape[1] // HDIM
    qh = query.reshape(count, heads_here, HDIM)
    kh = key_block.reshape(-1, heads_here, HDIM)
    vh = value_block.reshape(-1, heads_here, HDIM)
    scores = jnp.einsum("qhd,khd->hqk", qh, kh, preferred_element_type=jnp.float32) / jnp.sqrt(
        jnp.float32(HDIM)
    )
    peak = jnp.max(scores, axis=-1)
    weights = jnp.exp(scores - peak[..., None]).astype(jnp.bfloat16)
    total = jnp.sum(weights.astype(jnp.float32), axis=-1)
    partial_value = jnp.einsum("hqk,khd->hqd", weights, vh, preferred_element_type=jnp.float32)
    return (peak, total, partial_value)


FRAME_AXES = ("z", "xh", "y")
HEAD_AXES = ("xl", "c")


def frame_index():
    return (lax.axis_index("z") * lax.axis_size("xh") + lax.axis_index("xh")) * lax.axis_size("y") + lax.axis_index(
        "y"
    )


def cyclic(array, axis, by):
    length = lax.axis_size(axis)
    return lax.ppermute(array, axis, [(i, (i + by) % length) for i in range(length)])


def ring_stage(data, axis, source):
    length = lax.axis_size(axis)
    if length == 1:
        return data
    rel = (lax.axis_index(axis) - source) % length
    if length == 2:
        got = cyclic(data, axis, 1)
        return jnp.where(rel == 0, data, got)
    assert length == 4
    half = data.shape[0] // 2
    h0, h1 = data[:half], data[half:]
    g0 = cyclic(h0, axis, 1)
    g1 = cyclic(h1, axis, -1)
    a0 = jnp.where(rel == 1, g0, h0)
    a1 = jnp.where(rel == 3, g1, h1)
    r_p = cyclic(jnp.where(rel == 0, h1, a0), axis, 1)
    r_m = cyclic(jnp.where(rel == 0, h0, a1), axis, -1)
    out0 = jnp.where(rel == 0, h0, jnp.where(rel == 1, g0, jnp.where(rel == 2, r_p, r_m)))
    out1 = jnp.where(rel == 0, h1, jnp.where(rel == 1, r_p, jnp.where(rel == 2, r_m, g1)))
    return jnp.concatenate([out0, out1], axis=0)


def exchange(data, sink):
    n_frame = lax.axis_size(FRAME_AXES)
    piece = data.shape[0] // n_frame
    spread = lax.all_to_all(data, FRAME_AXES, 0, 0, tiled=True)
    pieces = spread.reshape((n_frame, piece) + data.shape[1:])
    before = jnp.concatenate([pieces[-1:], pieces[:-1]], axis=0).reshape(data.shape)
    prev_full = lax.all_to_all(before, FRAME_AXES, 0, 0, tiled=True)
    mine = lax.dynamic_slice_in_dim(spread, sink * piece, piece, axis=0)
    copies = jnp.broadcast_to(mine[None], (n_frame,) + mine.shape).reshape(data.shape)
    copies, prev_full = lax.optimization_barrier((copies, prev_full))
    return prev_full, lax.all_to_all(copies, FRAME_AXES, 0, 0, tiled=True)


def rope_tables(frame_value, count):
    angle = pair_angles(frame_value, count)
    cosine = jnp.cos(angle)
    sine = jnp.sin(angle)
    cos_full = jnp.stack([cosine, cosine], axis=-1).reshape(count, HDIM)
    sin_signed = jnp.stack([-sine, sine], axis=-1).reshape(count, HDIM)
    return cos_full, sin_signed


def rotate_ref(x_ref, cos_ref, sin_ref, swap):
    x = x_ref[...]
    partner = jnp.dot(x, swap, preferred_element_type=jnp.float32)
    return (x.astype(jnp.float32) * cos_ref[...] + partner * sin_ref[...]).astype(jnp.bfloat16)


def attend_ref(q, k, v_ref):
    scale = 1.0 / jnp.sqrt(jnp.float32(HDIM))
    raw = lax.dot_general(q, k, (((1,), (1,)), ((), ())), preferred_element_type=jnp.float32)
    raw_peak = jnp.max(raw, axis=-1, keepdims=True)
    peak = raw_peak * scale
    weights = jnp.exp((raw - raw_peak) * scale).astype(jnp.bfloat16)
    total = jnp.sum(weights.astype(jnp.float32), axis=-1, keepdims=True)
    partial_value = jnp.dot(weights, v_ref[...], preferred_element_type=jnp.float32)
    return peak, total, partial_value


def near_kernel(flags, q_ref, ks_ref, vs_ref, kp_ref, vp_ref, swap_ref, cq, sq, m_ref, l_ref, o_ref):
    swap = swap_ref[...]
    q = rotate_ref(q_ref, cq, sq, swap)
    m_self, l_self, o_self = attend_ref(q, ks_ref[...], vs_ref)
    m_prev, l_prev, o_prev = attend_ref(q, kp_ref[...], vp_ref)
    prev_used = flags[0] != 0
    top = jnp.maximum(m_self, jnp.where(prev_used, m_prev, m_self))
    c_self = jnp.exp(m_self - top)
    c_prev = jnp.where(prev_used, jnp.exp(m_prev - top), 0.0)
    m_ref[...] = jnp.broadcast_to(top, m_ref.shape)
    l_ref[...] = jnp.broadcast_to(l_self * c_self + l_prev * c_prev, l_ref.shape)
    o_ref[...] = o_self * c_self + o_prev * c_prev


def rope_kernel(x_ref, swap_ref, cos_ref, sin_ref, out_ref):
    out_ref[...] = rotate_ref(x_ref, cos_ref, sin_ref, swap_ref[...])


def rope(x, tables):
    count, width = x.shape
    head = pl.BlockSpec((count, HDIM), lambda h: (0, h))
    whole = pl.BlockSpec((count, HDIM), lambda h: (0, 0))
    swap = pl.BlockSpec((HDIM, HDIM), lambda h: (0, 0))
    return pl.pallas_call(
        rope_kernel,
        grid=(width // HDIM,),
        in_specs=[head, swap, whole, whole],
        out_specs=head,
        out_shape=jax.ShapeDtypeStruct((count, width), jnp.bfloat16),
        cost_estimate=pl.CostEstimate(flops=2 * count * width * HDIM, transcendentals=0, bytes_accessed=4 * count * width),
    )(x, swap_matrix(), *tables)


def sink_kernel(flags, q_ref, kk_ref, vk_ref, swap_ref, cq, sq, m_ref, l_ref, o_ref, out_ref):
    swap = swap_ref[...]
    q = rotate_ref(q_ref, cq, sq, swap)
    m_sink, l_sink, o_sink = attend_ref(q, kk_ref[...], vk_ref)
    sink_used = flags[1] != 0
    m_near = m_ref[:, :1]
    top = jnp.maximum(m_near, jnp.where(sink_used, m_sink, m_near))
    c_near = jnp.exp(m_near - top)
    c_sink = jnp.where(sink_used, jnp.exp(m_sink - top), 0.0)
    numer = o_ref[...] * c_near + o_sink * c_sink
    denom = l_ref[:, :1] * c_near + l_sink * c_sink
    out_ref[...] = (numer / denom).astype(out_ref.dtype)


def specs(count):
    head = pl.BlockSpec((count, HDIM), lambda h, flags: (0, h))
    whole = pl.BlockSpec((count, HDIM), lambda h, flags: (0, 0))
    swap = pl.BlockSpec((HDIM, HDIM), lambda h, flags: (0, 0))
    return head, whole, swap


def swap_matrix():
    lane = jnp.arange(HDIM)
    return (lane[:, None] == (lane[None, :] ^ 1)).astype(jnp.bfloat16)


def near_attention(flags, queries, blocks, tables):
    count, width = queries.shape
    heads_here = width // HDIM
    head, whole, swap = specs(count)
    grid_spec = pltpu.PrefetchScalarGridSpec(
        num_scalar_prefetch=1,
        grid=(heads_here,),
        in_specs=[head] * 5 + [swap] + [whole] * 2,
        out_specs=[head] * 3,
    )
    cost = pl.CostEstimate(
        flops=heads_here * 2 * 4 * count * count * HDIM,
        transcendentals=heads_here * 2 * count * count,
        bytes_accessed=5 * count * width * 2 + 3 * count * width * 4,
    )
    f32 = jax.ShapeDtypeStruct((count, width), jnp.float32)
    return pl.pallas_call(
        near_kernel, grid_spec=grid_spec, out_shape=[f32] * 3, cost_estimate=cost
    )(flags, queries, *blocks, swap_matrix(), *tables)


def sink_attention(flags, queries, blocks, tables, near, half, halves):
    count, width = queries.shape
    heads_here = width // HDIM
    rows = count // halves
    part = pl.BlockSpec((rows, HDIM), lambda h, flags: (half, h))
    part_table = pl.BlockSpec((rows, HDIM), lambda h, flags: (half, 0))
    head = pl.BlockSpec((count, HDIM), lambda h, flags: (0, h))
    swap = pl.BlockSpec((HDIM, HDIM), lambda h, flags: (0, 0))
    grid_spec = pltpu.PrefetchScalarGridSpec(
        num_scalar_prefetch=1,
        grid=(heads_here,),
        in_specs=[part] + [head] * 2 + [swap] + [part_table] * 2 + [part] * 3,
        out_specs=pl.BlockSpec((rows, HDIM), lambda h, flags: (0, h)),
    )
    cost = pl.CostEstimate(
        flops=heads_here * 4 * rows * count * HDIM,
        transcendentals=heads_here * rows * count,
        bytes_accessed=(rows + 2 * count) * width * 2 + 3 * rows * width * 4,
    )
    return pl.pallas_call(
        sink_kernel,
        grid_spec=grid_spec,
        out_shape=jax.ShapeDtypeStruct((rows, width), jnp.bfloat16),
        cost_estimate=cost,
    )(flags, queries, *blocks, swap_matrix(), *tables, *near)


def head_reduce(terms):
    rows, width = terms.shape
    n_xl, n_c = lax.axis_size("xl"), lax.axis_size("c")
    block = width // (n_xl * n_c)
    xl, c = lax.axis_index("xl"), lax.axis_index("c")
    grid = terms.reshape(rows, n_xl, n_c, block)
    mine = lax.dynamic_slice_in_dim(grid, c, 1, axis=2)
    other = lax.dynamic_slice_in_dim(grid, 1 - c, 1, axis=2)
    got = lax.ppermute(other, "c", [(0, 1), (1, 0)])
    chip = (mine.astype(jnp.float32) + got.astype(jnp.float32)).astype(jnp.bfloat16)
    keep = lax.dynamic_slice_in_dim(chip, xl, 1, axis=1)
    send = lax.dynamic_slice_in_dim(chip, 1 - xl, 1, axis=1)
    got = lax.ppermute(send, "xl", [(0, 1), (1, 0)])
    total = keep.astype(jnp.float32) + got.astype(jnp.float32)
    return total.astype(jnp.bfloat16).reshape(rows, block)


def shards(queries, keys, values, out_weight, sink_owner, frame_pos):
    count = queries.shape[0]
    place = frame_index()
    n_frame = lax.axis_size(FRAME_AXES)
    sink = sink_owner[0] % (n_frame // 2)
    own_tables = rope_tables(frame_pos[0], count)
    rot_k = rope(keys, own_tables)
    prev_kv, sink_kv = exchange(jnp.concatenate([rot_k, values], axis=0), sink)
    prev_used = (place >= 1) & (place - 1 != sink)
    sink_used = sink < place
    flags = jnp.stack([prev_used, sink_used]).astype(jnp.int32)
    near = near_attention(flags, queries, (rot_k, values, prev_kv[:count], prev_kv[count:]), own_tables)
    halves = 2
    outs = []
    for half in range(halves):
        attended = sink_attention(flags, queries, (sink_kv[:count], sink_kv[count:]), own_tables, near, half, halves)
        terms = jnp.dot(attended, out_weight, preferred_element_type=jnp.float32)
        outs.append(head_reduce(terms.astype(jnp.bfloat16)))
    mixed = jnp.concatenate(outs, axis=0)
    return mixed


def solution(mesh):
    frame_phys = {"z": 4, "xh": 2, "y": 4}
    head_phys = {"xl": 2, "c": 2}
    assert mesh.shape["frame"] == 32 and mesh.shape["head"] == 4
    devices = mesh.devices.reshape(tuple(frame_phys.values()) + tuple(head_phys.values()))
    fine = Mesh(devices, FRAME_AXES + HEAD_AXES)
    in_specs = (
        P(FRAME_AXES, HEAD_AXES),
        P(FRAME_AXES, HEAD_AXES),
        P(FRAME_AXES, HEAD_AXES),
        P(HEAD_AXES, None),
        P(),
        P(FRAME_AXES),
    )
    out_specs = P(FRAME_AXES, HEAD_AXES)
    inner = jax.shard_map(shards, mesh=fine, in_specs=in_specs, out_specs=out_specs, check_vma=False)

    def run(*args):
        out = inner(*args)
        return jax.lax.with_sharding_constraint(out, NamedSharding(mesh, P("frame", "head")))

    return run
```

```python
import jax
import jax.numpy as jnp
from jax import lax
from jax.experimental import pallas as pl
from jax.experimental.pallas import tpu as pltpu
from jax.sharding import Mesh, NamedSharding, PartitionSpec as P

HDIM = 128
GRID_W = 32


def shifted(array, axis, by):
    length = lax.axis_size(axis)
    pairs = [(i, i + by) for i in range(length) if 0 <= i + by < length]
    return lax.ppermute(array, axis, pairs)


def broadcast(value, axis, source):
    kept = jnp.where(lax.axis_index(axis) == source, value, 0).astype(value.dtype)
    return lax.psum(kept, axis)


def pair_angles(frame_value, count):
    half = HDIM // 2
    tdim = HDIM - 4 * (HDIM // 6)
    sdim = 2 * (HDIM // 6)
    tcount = tdim // 2
    scount = sdim // 2
    index = jnp.arange(half)
    findex = index.astype(jnp.float32)
    freq = jnp.where(
        index < tcount,
        jnp.power(10000.0, -2.0 * findex / tdim),
        jnp.where(
            index < tcount + scount,
            jnp.power(10000.0, -2.0 * (findex - tcount) / sdim),
            jnp.power(10000.0, -2.0 * (findex - tcount - scount) / sdim),
        ),
    )
    token = jnp.arange(count)
    row_pos = (token // GRID_W).astype(jnp.float32)[:, None]
    col_pos = (token % GRID_W).astype(jnp.float32)[:, None]
    frame_f = jnp.zeros((count, 1), jnp.float32) + frame_value.astype(jnp.float32)
    pos = jnp.where(
        index[None, :] < tcount,
        frame_f,
        jnp.where(index[None, :] < tcount + scount, row_pos, col_pos),
    )
    return pos * freq[None, :]


def rotate(block, angle):
    count = block.shape[0]
    heads_here = block.shape[1] // HDIM
    parts = block.astype(jnp.float32).reshape(count, heads_here, HDIM // 2, 2)
    cosine = jnp.cos(angle)[:, None, :]
    sine = jnp.sin(angle)[:, None, :]
    first = parts[..., 0] * cosine - parts[..., 1] * sine
    second = parts[..., 0] * sine + parts[..., 1] * cosine
    return (
        jnp.stack([first, second], axis=-1).reshape(count, heads_here * HDIM).astype(jnp.bfloat16)
    )


def attend_block(query, key_block, value_block):
    count = query.shape[0]
    heads_here = query.shape[1] // HDIM
    qh = query.reshape(count, heads_here, HDIM)
    kh = key_block.reshape(-1, heads_here, HDIM)
    vh = value_block.reshape(-1, heads_here, HDIM)
    scores = jnp.einsum("qhd,khd->hqk", qh, kh, preferred_element_type=jnp.float32) / jnp.sqrt(
        jnp.float32(HDIM)
    )
    peak = jnp.max(scores, axis=-1)
    weights = jnp.exp(scores - peak[..., None]).astype(jnp.bfloat16)
    total = jnp.sum(weights.astype(jnp.float32), axis=-1)
    partial_value = jnp.einsum("hqk,khd->hqd", weights, vh, preferred_element_type=jnp.float32)
    return (peak, total, partial_value)


FRAME_AXES = ("z", "xh", "y")
HEAD_AXES = ("xl", "c")


def frame_index():
    return (lax.axis_index("z") * lax.axis_size("xh") + lax.axis_index("xh")) * lax.axis_size("y") + lax.axis_index(
        "y"
    )


def cyclic(array, axis, by):
    length = lax.axis_size(axis)
    return lax.ppermute(array, axis, [(i, (i + by) % length) for i in range(length)])


def ring_stage(data, axis, source):
    length = lax.axis_size(axis)
    if length == 1:
        return data
    rel = (lax.axis_index(axis) - source) % length
    if length == 2:
        got = cyclic(data, axis, 1)
        return jnp.where(rel == 0, data, got)
    assert length == 4
    half = data.shape[0] // 2
    h0, h1 = data[:half], data[half:]
    g0 = cyclic(h0, axis, 1)
    g1 = cyclic(h1, axis, -1)
    a0 = jnp.where(rel == 1, g0, h0)
    a1 = jnp.where(rel == 3, g1, h1)
    r_p = cyclic(jnp.where(rel == 0, h1, a0), axis, 1)
    r_m = cyclic(jnp.where(rel == 0, h0, a1), axis, -1)
    out0 = jnp.where(rel == 0, h0, jnp.where(rel == 1, g0, jnp.where(rel == 2, r_p, r_m)))
    out1 = jnp.where(rel == 0, h1, jnp.where(rel == 1, r_p, jnp.where(rel == 2, r_m, g1)))
    return jnp.concatenate([out0, out1], axis=0)


def exchange(data, sink):
    n_frame = lax.axis_size(FRAME_AXES)
    piece = data.shape[0] // n_frame
    spread = lax.all_to_all(data, FRAME_AXES, 0, 0, tiled=True)
    pieces = spread.reshape((n_frame, piece) + data.shape[1:])
    before = jnp.concatenate([pieces[-1:], pieces[:-1]], axis=0).reshape(data.shape)
    prev_full = lax.all_to_all(before, FRAME_AXES, 0, 0, tiled=True)
    mine = lax.dynamic_slice_in_dim(spread, sink * piece, piece, axis=0)
    copies = jnp.broadcast_to(mine[None], (n_frame,) + mine.shape).reshape(data.shape)
    copies, prev_full = lax.optimization_barrier((copies, prev_full))
    return prev_full, lax.all_to_all(copies, FRAME_AXES, 0, 0, tiled=True)


def rope_tables(frame_value, count):
    angle = pair_angles(frame_value, count)
    cosine = jnp.cos(angle)
    sine = jnp.sin(angle)
    cos_full = jnp.stack([cosine, cosine], axis=-1).reshape(count, HDIM)
    sin_signed = jnp.stack([-sine, sine], axis=-1).reshape(count, HDIM)
    return cos_full, sin_signed


def rotate_ref(x_ref, cos_ref, sin_ref, swap):
    x = x_ref[...]
    partner = jnp.dot(x, swap, preferred_element_type=jnp.float32)
    return (x.astype(jnp.float32) * cos_ref[...] + partner * sin_ref[...]).astype(jnp.bfloat16)


def attend_ref(q, k, v_ref):
    scale = 1.0 / jnp.sqrt(jnp.float32(HDIM))
    raw = lax.dot_general(q, k, (((1,), (1,)), ((), ())), preferred_element_type=jnp.float32)
    raw_peak = jnp.max(raw, axis=-1, keepdims=True)
    peak = raw_peak * scale
    weights = jnp.exp((raw - raw_peak) * scale).astype(jnp.bfloat16)
    total = jnp.sum(weights.astype(jnp.float32), axis=-1, keepdims=True)
    partial_value = jnp.dot(weights, v_ref[...], preferred_element_type=jnp.float32)
    return peak, total, partial_value


def near_kernel(flags, q_ref, ks_ref, vs_ref, kp_ref, vp_ref, swap_ref, cq, sq, m_ref, l_ref, o_ref):
    swap = swap_ref[...]
    q = rotate_ref(q_ref, cq, sq, swap)
    m_self, l_self, o_self = attend_ref(q, ks_ref[...], vs_ref)
    m_prev, l_prev, o_prev = attend_ref(q, kp_ref[...], vp_ref)
    prev_used = flags[0] != 0
    top = jnp.maximum(m_self, jnp.where(prev_used, m_prev, m_self))
    c_self = jnp.exp(m_self - top)
    c_prev = jnp.where(prev_used, jnp.exp(m_prev - top), 0.0)
    m_ref[...] = jnp.broadcast_to(top, m_ref.shape)
    l_ref[...] = jnp.broadcast_to(l_self * c_self + l_prev * c_prev, l_ref.shape)
    o_ref[...] = o_self * c_self + o_prev * c_prev


def rope_kernel(x_ref, swap_ref, cos_ref, sin_ref, out_ref):
    out_ref[...] = rotate_ref(x_ref, cos_ref, sin_ref, swap_ref[...])


def rope(x, tables):
    count, width = x.shape
    head = pl.BlockSpec((count, HDIM), lambda h: (0, h))
    whole = pl.BlockSpec((count, HDIM), lambda h: (0, 0))
    swap = pl.BlockSpec((HDIM, HDIM), lambda h: (0, 0))
    return pl.pallas_call(
        rope_kernel,
        grid=(width // HDIM,),
        in_specs=[head, swap, whole, whole],
        out_specs=head,
        out_shape=jax.ShapeDtypeStruct((count, width), jnp.bfloat16),
        cost_estimate=pl.CostEstimate(flops=2 * count * width * HDIM, transcendentals=0, bytes_accessed=4 * count * width),
    )(x, swap_matrix(), *tables)


def sink_kernel(flags, q_ref, kk_ref, vk_ref, swap_ref, cq, sq, m_ref, l_ref, o_ref, out_ref):
    swap = swap_ref[...]
    q = rotate_ref(q_ref, cq, sq, swap)
    m_sink, l_sink, o_sink = attend_ref(q, kk_ref[...], vk_ref)
    sink_used = flags[1] != 0
    m_near = m_ref[:, :1]
    top = jnp.maximum(m_near, jnp.where(sink_used, m_sink, m_near))
    c_near = jnp.exp(m_near - top)
    c_sink = jnp.where(sink_used, jnp.exp(m_sink - top), 0.0)
    numer = o_ref[...] * c_near + o_sink * c_sink
    denom = l_ref[:, :1] * c_near + l_sink * c_sink
    out_ref[...] = (numer / denom).astype(out_ref.dtype)


def specs(count):
    head = pl.BlockSpec((count, HDIM), lambda h, flags: (0, h))
    whole = pl.BlockSpec((count, HDIM), lambda h, flags: (0, 0))
    swap = pl.BlockSpec((HDIM, HDIM), lambda h, flags: (0, 0))
    return head, whole, swap


def swap_matrix():
    lane = jnp.arange(HDIM)
    return (lane[:, None] == (lane[None, :] ^ 1)).astype(jnp.bfloat16)


def near_attention(flags, queries, blocks, tables):
    count, width = queries.shape
    heads_here = width // HDIM
    head, whole, swap = specs(count)
    grid_spec = pltpu.PrefetchScalarGridSpec(
        num_scalar_prefetch=1,
        grid=(heads_here,),
        in_specs=[head] * 5 + [swap] + [whole] * 2,
        out_specs=[head] * 3,
    )
    cost = pl.CostEstimate(
        flops=heads_here * 2 * 4 * count * count * HDIM,
        transcendentals=heads_here * 2 * count * count,
        bytes_accessed=5 * count * width * 2 + 3 * count * width * 4,
    )
    f32 = jax.ShapeDtypeStruct((count, width), jnp.float32)
    return pl.pallas_call(
        near_kernel, grid_spec=grid_spec, out_shape=[f32] * 3, cost_estimate=cost
    )(flags, queries, *blocks, swap_matrix(), *tables)


def sink_attention(flags, queries, blocks, tables, near, half, halves):
    count, width = queries.shape
    heads_here = width // HDIM
    rows = count // halves
    part = pl.BlockSpec((rows, HDIM), lambda h, flags: (half, h))
    part_table = pl.BlockSpec((rows, HDIM), lambda h, flags: (half, 0))
    head = pl.BlockSpec((count, HDIM), lambda h, flags: (0, h))
    swap = pl.BlockSpec((HDIM, HDIM), lambda h, flags: (0, 0))
    grid_spec = pltpu.PrefetchScalarGridSpec(
        num_scalar_prefetch=1,
        grid=(heads_here,),
        in_specs=[part] + [head] * 2 + [swap] + [part_table] * 2 + [part] * 3,
        out_specs=pl.BlockSpec((rows, HDIM), lambda h, flags: (0, h)),
    )
    cost = pl.CostEstimate(
        flops=heads_here * 4 * rows * count * HDIM,
        transcendentals=heads_here * rows * count,
        bytes_accessed=(rows + 2 * count) * width * 2 + 3 * rows * width * 4,
    )
    return pl.pallas_call(
        sink_kernel,
        grid_spec=grid_spec,
        out_shape=jax.ShapeDtypeStruct((rows, width), jnp.bfloat16),
        cost_estimate=cost,
    )(flags, queries, *blocks, swap_matrix(), *tables, *near)


def weight_blocks(out_weight):
    n_xl, n_c = lax.axis_size("xl"), lax.axis_size("c")
    block = out_weight.shape[1] // (n_xl * n_c)
    c = lax.axis_index("c")

    def columns(core):
        return jnp.stack(
            [lax.dynamic_slice_in_dim(out_weight, (x * n_c + core) * block, block, axis=1) for x in range(n_xl)]
        )

    return columns(c), columns(1 - c)


def head_reduce(attended, mine_w, other_w):
    xl = lax.axis_index("xl")
    mine = jnp.einsum("rk,xkn->xrn", attended, mine_w, preferred_element_type=jnp.float32).astype(jnp.bfloat16)
    other = jnp.einsum("rk,xkn->xrn", attended, other_w, preferred_element_type=jnp.float32).astype(jnp.bfloat16)
    got = lax.ppermute(other, "c", [(0, 1), (1, 0)])
    chip = (mine.astype(jnp.float32) + got.astype(jnp.float32)).astype(jnp.bfloat16)
    keep = lax.dynamic_index_in_dim(chip, xl, axis=0, keepdims=False)
    send = lax.dynamic_index_in_dim(chip, 1 - xl, axis=0, keepdims=False)
    got = lax.ppermute(send, "xl", [(0, 1), (1, 0)])
    return (keep.astype(jnp.float32) + got.astype(jnp.float32)).astype(jnp.bfloat16)


def shards(queries, keys, values, out_weight, sink_owner, frame_pos):
    count = queries.shape[0]
    place = frame_index()
    n_frame = lax.axis_size(FRAME_AXES)
    sink = sink_owner[0] % (n_frame // 2)
    own_tables = rope_tables(frame_pos[0], count)
    rot_k = rope(keys, own_tables)
    prev_kv, sink_kv = exchange(jnp.concatenate([rot_k, values], axis=0), sink)
    prev_used = (place >= 1) & (place - 1 != sink)
    sink_used = sink < place
    flags = jnp.stack([prev_used, sink_used]).astype(jnp.int32)
    near = near_attention(flags, queries, (rot_k, values, prev_kv[:count], prev_kv[count:]), own_tables)
    halves = 2
    mine_w, other_w = weight_blocks(out_weight)
    outs = []
    for half in range(halves):
        attended = sink_attention(flags, queries, (sink_kv[:count], sink_kv[count:]), own_tables, near, half, halves)
        outs.append(head_reduce(attended, mine_w, other_w))
    mixed = jnp.concatenate(outs, axis=0)
    return mixed


def solution(mesh):
    frame_phys = {"z": 4, "xh": 2, "y": 4}
    head_phys = {"xl": 2, "c": 2}
    assert mesh.shape["frame"] == 32 and mesh.shape["head"] == 4
    devices = mesh.devices.reshape(tuple(frame_phys.values()) + tuple(head_phys.values()))
    fine = Mesh(devices, FRAME_AXES + HEAD_AXES)
    in_specs = (
        P(FRAME_AXES, HEAD_AXES),
        P(FRAME_AXES, HEAD_AXES),
        P(FRAME_AXES, HEAD_AXES),
        P(HEAD_AXES, None),
        P(),
        P(FRAME_AXES),
    )
    out_specs = P(FRAME_AXES, HEAD_AXES)
    inner = jax.shard_map(shards, mesh=fine, in_specs=in_specs, out_specs=out_specs, check_vma=False)

    def run(*args):
        out = inner(*args)
        return jax.lax.with_sharding_constraint(out, NamedSharding(mesh, P("frame", "head")))

    return run
```

```python
import jax
import jax.numpy as jnp
from jax import lax
from jax.experimental import pallas as pl
from jax.experimental.pallas import tpu as pltpu
from jax.sharding import Mesh, NamedSharding, PartitionSpec as P

HDIM = 128
GRID_W = 32


def shifted(array, axis, by):
    length = lax.axis_size(axis)
    pairs = [(i, i + by) for i in range(length) if 0 <= i + by < length]
    return lax.ppermute(array, axis, pairs)


def broadcast(value, axis, source):
    kept = jnp.where(lax.axis_index(axis) == source, value, 0).astype(value.dtype)
    return lax.psum(kept, axis)


def pair_angles(frame_value, count):
    half = HDIM // 2
    tdim = HDIM - 4 * (HDIM // 6)
    sdim = 2 * (HDIM // 6)
    tcount = tdim // 2
    scount = sdim // 2
    index = jnp.arange(half)
    findex = index.astype(jnp.float32)
    freq = jnp.where(
        index < tcount,
        jnp.power(10000.0, -2.0 * findex / tdim),
        jnp.where(
            index < tcount + scount,
            jnp.power(10000.0, -2.0 * (findex - tcount) / sdim),
            jnp.power(10000.0, -2.0 * (findex - tcount - scount) / sdim),
        ),
    )
    token = jnp.arange(count)
    row_pos = (token // GRID_W).astype(jnp.float32)[:, None]
    col_pos = (token % GRID_W).astype(jnp.float32)[:, None]
    frame_f = jnp.zeros((count, 1), jnp.float32) + frame_value.astype(jnp.float32)
    pos = jnp.where(
        index[None, :] < tcount,
        frame_f,
        jnp.where(index[None, :] < tcount + scount, row_pos, col_pos),
    )
    return pos * freq[None, :]


def rotate(block, angle):
    count = block.shape[0]
    heads_here = block.shape[1] // HDIM
    parts = block.astype(jnp.float32).reshape(count, heads_here, HDIM // 2, 2)
    cosine = jnp.cos(angle)[:, None, :]
    sine = jnp.sin(angle)[:, None, :]
    first = parts[..., 0] * cosine - parts[..., 1] * sine
    second = parts[..., 0] * sine + parts[..., 1] * cosine
    return (
        jnp.stack([first, second], axis=-1).reshape(count, heads_here * HDIM).astype(jnp.bfloat16)
    )


def attend_block(query, key_block, value_block):
    count = query.shape[0]
    heads_here = query.shape[1] // HDIM
    qh = query.reshape(count, heads_here, HDIM)
    kh = key_block.reshape(-1, heads_here, HDIM)
    vh = value_block.reshape(-1, heads_here, HDIM)
    scores = jnp.einsum("qhd,khd->hqk", qh, kh, preferred_element_type=jnp.float32) / jnp.sqrt(
        jnp.float32(HDIM)
    )
    peak = jnp.max(scores, axis=-1)
    weights = jnp.exp(scores - peak[..., None]).astype(jnp.bfloat16)
    total = jnp.sum(weights.astype(jnp.float32), axis=-1)
    partial_value = jnp.einsum("hqk,khd->hqd", weights, vh, preferred_element_type=jnp.float32)
    return (peak, total, partial_value)


FRAME_AXES = ("z", "xh", "y")
HEAD_AXES = ("xl", "c")


def frame_index():
    return (lax.axis_index("z") * lax.axis_size("xh") + lax.axis_index("xh")) * lax.axis_size("y") + lax.axis_index(
        "y"
    )


def cyclic(array, axis, by):
    length = lax.axis_size(axis)
    return lax.ppermute(array, axis, [(i, (i + by) % length) for i in range(length)])


def ring_stage(data, axis, source):
    length = lax.axis_size(axis)
    if length == 1:
        return data
    rel = (lax.axis_index(axis) - source) % length
    if length == 2:
        got = cyclic(data, axis, 1)
        return jnp.where(rel == 0, data, got)
    assert length == 4
    half = data.shape[0] // 2
    h0, h1 = data[:half], data[half:]
    g0 = cyclic(h0, axis, 1)
    g1 = cyclic(h1, axis, -1)
    a0 = jnp.where(rel == 1, g0, h0)
    a1 = jnp.where(rel == 3, g1, h1)
    r_p = cyclic(jnp.where(rel == 0, h1, a0), axis, 1)
    r_m = cyclic(jnp.where(rel == 0, h0, a1), axis, -1)
    out0 = jnp.where(rel == 0, h0, jnp.where(rel == 1, g0, jnp.where(rel == 2, r_p, r_m)))
    out1 = jnp.where(rel == 0, h1, jnp.where(rel == 1, r_p, jnp.where(rel == 2, r_m, g1)))
    return jnp.concatenate([out0, out1], axis=0)


def exchange(data, sink):
    n_frame = lax.axis_size(FRAME_AXES)
    piece = data.shape[0] // n_frame
    spread = lax.all_to_all(data, FRAME_AXES, 0, 0, tiled=True)
    pieces = spread.reshape((n_frame, piece) + data.shape[1:])
    before = jnp.concatenate([pieces[-1:], pieces[:-1]], axis=0).reshape(data.shape)
    prev_full = lax.all_to_all(before, FRAME_AXES, 0, 0, tiled=True)
    mine = lax.dynamic_slice_in_dim(spread, sink * piece, piece, axis=0)
    copies = jnp.broadcast_to(mine[None], (n_frame,) + mine.shape).reshape(data.shape)
    copies, prev_full = lax.optimization_barrier((copies, prev_full))
    return prev_full, lax.all_to_all(copies, FRAME_AXES, 0, 0, tiled=True)


def rope_tables(frame_value, count):
    angle = pair_angles(frame_value, count)
    cosine = jnp.cos(angle)
    sine = jnp.sin(angle)
    cos_full = jnp.stack([cosine, cosine], axis=-1).reshape(count, HDIM)
    sin_signed = jnp.stack([-sine, sine], axis=-1).reshape(count, HDIM)
    return cos_full, sin_signed


def rotate_ref(x_ref, cos_ref, sin_ref, swap):
    x = x_ref[...]
    partner = jnp.dot(x, swap, preferred_element_type=jnp.float32)
    return (x.astype(jnp.float32) * cos_ref[...] + partner * sin_ref[...]).astype(jnp.bfloat16)


def attend_ref(q, k, v_ref):
    scale = 1.0 / jnp.sqrt(jnp.float32(HDIM))
    raw = lax.dot_general(q, k, (((1,), (1,)), ((), ())), preferred_element_type=jnp.float32)
    raw_peak = jnp.max(raw, axis=-1, keepdims=True)
    peak = raw_peak * scale
    weights = jnp.exp((raw - raw_peak) * scale).astype(jnp.bfloat16)
    total = jnp.sum(weights.astype(jnp.float32), axis=-1, keepdims=True)
    partial_value = jnp.dot(weights, v_ref[...], preferred_element_type=jnp.float32)
    return peak, total, partial_value


def near_kernel(flags, q_ref, ks_ref, vs_ref, kp_ref, vp_ref, swap_ref, cq, sq, m_ref, l_ref, o_ref):
    swap = swap_ref[...]
    q = rotate_ref(q_ref, cq, sq, swap)
    m_self, l_self, o_self = attend_ref(q, ks_ref[...], vs_ref)
    m_prev, l_prev, o_prev = attend_ref(q, kp_ref[...], vp_ref)
    prev_used = flags[0] != 0
    top = jnp.maximum(m_self, jnp.where(prev_used, m_prev, m_self))
    c_self = jnp.exp(m_self - top)
    c_prev = jnp.where(prev_used, jnp.exp(m_prev - top), 0.0)
    m_ref[...] = jnp.broadcast_to(top, m_ref.shape)
    l_ref[...] = jnp.broadcast_to(l_self * c_self + l_prev * c_prev, l_ref.shape)
    o_ref[...] = o_self * c_self + o_prev * c_prev


def rope_kernel(x_ref, swap_ref, cos_ref, sin_ref, out_ref):
    out_ref[...] = rotate_ref(x_ref, cos_ref, sin_ref, swap_ref[...])


def rope(x, tables):
    count, width = x.shape
    head = pl.BlockSpec((count, HDIM), lambda h: (0, h))
    whole = pl.BlockSpec((count, HDIM), lambda h: (0, 0))
    swap = pl.BlockSpec((HDIM, HDIM), lambda h: (0, 0))
    return pl.pallas_call(
        rope_kernel,
        grid=(width // HDIM,),
        in_specs=[head, swap, whole, whole],
        out_specs=head,
        out_shape=jax.ShapeDtypeStruct((count, width), jnp.bfloat16),
        cost_estimate=pl.CostEstimate(flops=2 * count * width * HDIM, transcendentals=0, bytes_accessed=4 * count * width),
    )(x, swap_matrix(), *tables)


def sink_kernel(flags, q_ref, kk_ref, vk_ref, swap_ref, cq, sq, m_ref, l_ref, o_ref, out_ref):
    swap = swap_ref[...]
    q = rotate_ref(q_ref, cq, sq, swap)
    m_sink, l_sink, o_sink = attend_ref(q, kk_ref[...], vk_ref)
    sink_used = flags[1] != 0
    m_near = m_ref[:, :1]
    top = jnp.maximum(m_near, jnp.where(sink_used, m_sink, m_near))
    c_near = jnp.exp(m_near - top)
    c_sink = jnp.where(sink_used, jnp.exp(m_sink - top), 0.0)
    numer = o_ref[...] * c_near + o_sink * c_sink
    denom = l_ref[:, :1] * c_near + l_sink * c_sink
    out_ref[...] = (numer / denom).astype(out_ref.dtype)


def specs(count):
    head = pl.BlockSpec((count, HDIM), lambda h, flags: (0, h))
    whole = pl.BlockSpec((count, HDIM), lambda h, flags: (0, 0))
    swap = pl.BlockSpec((HDIM, HDIM), lambda h, flags: (0, 0))
    return head, whole, swap


def swap_matrix():
    lane = jnp.arange(HDIM)
    return (lane[:, None] == (lane[None, :] ^ 1)).astype(jnp.bfloat16)


def near_attention(flags, queries, blocks, tables):
    count, width = queries.shape
    heads_here = width // HDIM
    head, whole, swap = specs(count)
    grid_spec = pltpu.PrefetchScalarGridSpec(
        num_scalar_prefetch=1,
        grid=(heads_here,),
        in_specs=[head] * 5 + [swap] + [whole] * 2,
        out_specs=[head] * 3,
    )
    cost = pl.CostEstimate(
        flops=heads_here * 2 * 4 * count * count * HDIM,
        transcendentals=heads_here * 2 * count * count,
        bytes_accessed=5 * count * width * 2 + 3 * count * width * 4,
    )
    f32 = jax.ShapeDtypeStruct((count, width), jnp.float32)
    return pl.pallas_call(
        near_kernel, grid_spec=grid_spec, out_shape=[f32] * 3, cost_estimate=cost
    )(flags, queries, *blocks, swap_matrix(), *tables)


def sink_attention(flags, queries, blocks, tables, near, half, halves):
    count, width = queries.shape
    heads_here = width // HDIM
    rows = count // halves
    part = pl.BlockSpec((rows, HDIM), lambda h, flags: (half, h))
    part_table = pl.BlockSpec((rows, HDIM), lambda h, flags: (half, 0))
    head = pl.BlockSpec((count, HDIM), lambda h, flags: (0, h))
    swap = pl.BlockSpec((HDIM, HDIM), lambda h, flags: (0, 0))
    grid_spec = pltpu.PrefetchScalarGridSpec(
        num_scalar_prefetch=1,
        grid=(heads_here,),
        in_specs=[part] + [head] * 2 + [swap] + [part_table] * 2 + [part] * 3,
        out_specs=pl.BlockSpec((rows, HDIM), lambda h, flags: (0, h)),
    )
    cost = pl.CostEstimate(
        flops=heads_here * 4 * rows * count * HDIM,
        transcendentals=heads_here * rows * count,
        bytes_accessed=(rows + 2 * count) * width * 2 + 3 * rows * width * 4,
    )
    return pl.pallas_call(
        sink_kernel,
        grid_spec=grid_spec,
        out_shape=jax.ShapeDtypeStruct((rows, width), jnp.bfloat16),
        cost_estimate=cost,
    )(flags, queries, *blocks, swap_matrix(), *tables, *near)


def weight_blocks(out_weight):
    n_xl, n_c = lax.axis_size("xl"), lax.axis_size("c")
    block = out_weight.shape[1] // (n_xl * n_c)
    c = lax.axis_index("c")

    def columns(core):
        return jnp.stack(
            [lax.dynamic_slice_in_dim(out_weight, (x * n_c + core) * block, block, axis=1) for x in range(n_xl)]
        )

    return columns(c), columns(1 - c)


def head_reduce(attended, mine_w, other_w):
    xl = lax.axis_index("xl")
    mine = jnp.einsum("rk,xkn->xrn", attended, mine_w, preferred_element_type=jnp.float32).astype(jnp.bfloat16)
    other = jnp.einsum("rk,xkn->xrn", attended, other_w, preferred_element_type=jnp.float32).astype(jnp.bfloat16)
    got = lax.ppermute(other, "c", [(0, 1), (1, 0)])
    chip = (mine.astype(jnp.float32) + got.astype(jnp.float32)).astype(jnp.bfloat16)
    keep = lax.dynamic_index_in_dim(chip, xl, axis=0, keepdims=False)
    send = lax.dynamic_index_in_dim(chip, 1 - xl, axis=0, keepdims=False)
    got = lax.ppermute(send, "xl", [(0, 1), (1, 0)])
    return (keep.astype(jnp.float32) + got.astype(jnp.float32)).astype(jnp.bfloat16)


def shards(queries, keys, values, out_weight, sink_owner, frame_pos):
    count = queries.shape[0]
    place = frame_index()
    n_frame = lax.axis_size(FRAME_AXES)
    sink = sink_owner[0] % (n_frame // 2)
    own_tables = rope_tables(frame_pos[0], count)
    rot_k = rope(keys, own_tables)
    prev_kv, sink_kv = exchange(jnp.concatenate([rot_k, values], axis=0), sink)
    prev_used = (place >= 1) & (place - 1 != sink)
    sink_used = sink < place
    flags = jnp.stack([prev_used, sink_used]).astype(jnp.int32)
    near = near_attention(flags, queries, (rot_k, values, prev_kv[:count], prev_kv[count:]), own_tables)
    halves = 4
    mine_w, other_w = weight_blocks(out_weight)
    outs = []
    for half in range(halves):
        attended = sink_attention(flags, queries, (sink_kv[:count], sink_kv[count:]), own_tables, near, half, halves)
        outs.append(head_reduce(attended, mine_w, other_w))
    mixed = jnp.concatenate(outs, axis=0)
    return mixed


def solution(mesh):
    frame_phys = {"z": 4, "xh": 2, "y": 4}
    head_phys = {"xl": 2, "c": 2}
    assert mesh.shape["frame"] == 32 and mesh.shape["head"] == 4
    devices = mesh.devices.reshape(tuple(frame_phys.values()) + tuple(head_phys.values()))
    fine = Mesh(devices, FRAME_AXES + HEAD_AXES)
    in_specs = (
        P(FRAME_AXES, HEAD_AXES),
        P(FRAME_AXES, HEAD_AXES),
        P(FRAME_AXES, HEAD_AXES),
        P(HEAD_AXES, None),
        P(),
        P(FRAME_AXES),
    )
    out_specs = P(FRAME_AXES, HEAD_AXES)
    inner = jax.shard_map(shards, mesh=fine, in_specs=in_specs, out_specs=out_specs, check_vma=False)

    def run(*args):
        out = inner(*args)
        return jax.lax.with_sharding_constraint(out, NamedSharding(mesh, P("frame", "head")))

    return run
```

```python
import jax
import jax.numpy as jnp
from jax import lax
from jax.experimental import pallas as pl
from jax.experimental.pallas import tpu as pltpu
from jax.sharding import Mesh, NamedSharding, PartitionSpec as P

HDIM = 128
GRID_W = 32


def shifted(array, axis, by):
    length = lax.axis_size(axis)
    pairs = [(i, i + by) for i in range(length) if 0 <= i + by < length]
    return lax.ppermute(array, axis, pairs)


def broadcast(value, axis, source):
    kept = jnp.where(lax.axis_index(axis) == source, value, 0).astype(value.dtype)
    return lax.psum(kept, axis)


def pair_angles(frame_value, count):
    half = HDIM // 2
    tdim = HDIM - 4 * (HDIM // 6)
    sdim = 2 * (HDIM // 6)
    tcount = tdim // 2
    scount = sdim // 2
    index = jnp.arange(half)
    findex = index.astype(jnp.float32)
    freq = jnp.where(
        index < tcount,
        jnp.power(10000.0, -2.0 * findex / tdim),
        jnp.where(
            index < tcount + scount,
            jnp.power(10000.0, -2.0 * (findex - tcount) / sdim),
            jnp.power(10000.0, -2.0 * (findex - tcount - scount) / sdim),
        ),
    )
    token = jnp.arange(count)
    row_pos = (token // GRID_W).astype(jnp.float32)[:, None]
    col_pos = (token % GRID_W).astype(jnp.float32)[:, None]
    frame_f = jnp.zeros((count, 1), jnp.float32) + frame_value.astype(jnp.float32)
    pos = jnp.where(
        index[None, :] < tcount,
        frame_f,
        jnp.where(index[None, :] < tcount + scount, row_pos, col_pos),
    )
    return pos * freq[None, :]


def rotate(block, angle):
    count = block.shape[0]
    heads_here = block.shape[1] // HDIM
    parts = block.astype(jnp.float32).reshape(count, heads_here, HDIM // 2, 2)
    cosine = jnp.cos(angle)[:, None, :]
    sine = jnp.sin(angle)[:, None, :]
    first = parts[..., 0] * cosine - parts[..., 1] * sine
    second = parts[..., 0] * sine + parts[..., 1] * cosine
    return (
        jnp.stack([first, second], axis=-1).reshape(count, heads_here * HDIM).astype(jnp.bfloat16)
    )


def attend_block(query, key_block, value_block):
    count = query.shape[0]
    heads_here = query.shape[1] // HDIM
    qh = query.reshape(count, heads_here, HDIM)
    kh = key_block.reshape(-1, heads_here, HDIM)
    vh = value_block.reshape(-1, heads_here, HDIM)
    scores = jnp.einsum("qhd,khd->hqk", qh, kh, preferred_element_type=jnp.float32) / jnp.sqrt(
        jnp.float32(HDIM)
    )
    peak = jnp.max(scores, axis=-1)
    weights = jnp.exp(scores - peak[..., None]).astype(jnp.bfloat16)
    total = jnp.sum(weights.astype(jnp.float32), axis=-1)
    partial_value = jnp.einsum("hqk,khd->hqd", weights, vh, preferred_element_type=jnp.float32)
    return (peak, total, partial_value)


FRAME_AXES = ("z", "xh", "y")
HEAD_AXES = ("xl", "c")


def frame_index():
    return (lax.axis_index("z") * lax.axis_size("xh") + lax.axis_index("xh")) * lax.axis_size("y") + lax.axis_index(
        "y"
    )


def cyclic(array, axis, by):
    length = lax.axis_size(axis)
    return lax.ppermute(array, axis, [(i, (i + by) % length) for i in range(length)])


def ring_stage(data, axis, source):
    length = lax.axis_size(axis)
    if length == 1:
        return data
    rel = (lax.axis_index(axis) - source) % length
    if length == 2:
        got = cyclic(data, axis, 1)
        return jnp.where(rel == 0, data, got)
    assert length == 4
    half = data.shape[0] // 2
    h0, h1 = data[:half], data[half:]
    g0 = cyclic(h0, axis, 1)
    g1 = cyclic(h1, axis, -1)
    a0 = jnp.where(rel == 1, g0, h0)
    a1 = jnp.where(rel == 3, g1, h1)
    r_p = cyclic(jnp.where(rel == 0, h1, a0), axis, 1)
    r_m = cyclic(jnp.where(rel == 0, h0, a1), axis, -1)
    out0 = jnp.where(rel == 0, h0, jnp.where(rel == 1, g0, jnp.where(rel == 2, r_p, r_m)))
    out1 = jnp.where(rel == 0, h1, jnp.where(rel == 1, r_p, jnp.where(rel == 2, r_m, g1)))
    return jnp.concatenate([out0, out1], axis=0)


def exchange(data, sink):
    n_frame = lax.axis_size(FRAME_AXES)
    piece = data.shape[0] // n_frame
    spread = lax.all_to_all(data, FRAME_AXES, 0, 0, tiled=True)
    pieces = spread.reshape((n_frame, piece) + data.shape[1:])
    before = jnp.concatenate([pieces[-1:], pieces[:-1]], axis=0).reshape(data.shape)
    prev_full = lax.all_to_all(before, FRAME_AXES, 0, 0, tiled=True)
    mine = lax.dynamic_slice_in_dim(spread, sink * piece, piece, axis=0)
    copies = jnp.broadcast_to(mine[None], (n_frame,) + mine.shape).reshape(data.shape)
    copies, prev_full = lax.optimization_barrier((copies, prev_full))
    return prev_full, lax.all_to_all(copies, FRAME_AXES, 0, 0, tiled=True)


def rope_tables(frame_value, count):
    angle = pair_angles(frame_value, count)
    cosine = jnp.cos(angle)
    sine = jnp.sin(angle)
    cos_full = jnp.stack([cosine, cosine], axis=-1).reshape(count, HDIM)
    sin_signed = jnp.stack([-sine, sine], axis=-1).reshape(count, HDIM)
    return cos_full, sin_signed


def rotate_ref(x_ref, cos_ref, sin_ref, swap):
    x = x_ref[...]
    partner = jnp.dot(x, swap, preferred_element_type=jnp.float32)
    return (x.astype(jnp.float32) * cos_ref[...] + partner * sin_ref[...]).astype(jnp.bfloat16)


def attend_ref(q, k, v_ref):
    scale = 1.0 / jnp.sqrt(jnp.float32(HDIM))
    raw = lax.dot_general(q, k, (((1,), (1,)), ((), ())), preferred_element_type=jnp.float32)
    raw_peak = jnp.max(raw, axis=-1, keepdims=True)
    peak = raw_peak * scale
    weights = jnp.exp((raw - raw_peak) * scale).astype(jnp.bfloat16)
    total = jnp.sum(weights.astype(jnp.float32), axis=-1, keepdims=True)
    partial_value = jnp.dot(weights, v_ref[...], preferred_element_type=jnp.float32)
    return peak, total, partial_value


def near_kernel(flags, q_ref, ks_ref, vs_ref, kp_ref, vp_ref, swap_ref, cq, sq, m_ref, l_ref, o_ref):
    swap = swap_ref[...]
    q = rotate_ref(q_ref, cq, sq, swap)
    m_self, l_self, o_self = attend_ref(q, ks_ref[...], vs_ref)
    m_prev, l_prev, o_prev = attend_ref(q, kp_ref[...], vp_ref)
    prev_used = flags[0] != 0
    top = jnp.maximum(m_self, jnp.where(prev_used, m_prev, m_self))
    c_self = jnp.exp(m_self - top)
    c_prev = jnp.where(prev_used, jnp.exp(m_prev - top), 0.0)
    m_ref[...] = jnp.broadcast_to(top, m_ref.shape)
    l_ref[...] = jnp.broadcast_to(l_self * c_self + l_prev * c_prev, l_ref.shape)
    o_ref[...] = o_self * c_self + o_prev * c_prev


def rope_kernel(x_ref, swap_ref, cos_ref, sin_ref, out_ref):
    out_ref[...] = rotate_ref(x_ref, cos_ref, sin_ref, swap_ref[...])


def rope(x, tables):
    count, width = x.shape
    head = pl.BlockSpec((count, HDIM), lambda h: (0, h))
    whole = pl.BlockSpec((count, HDIM), lambda h: (0, 0))
    swap = pl.BlockSpec((HDIM, HDIM), lambda h: (0, 0))
    return pl.pallas_call(
        rope_kernel,
        grid=(width // HDIM,),
        in_specs=[head, swap, whole, whole],
        out_specs=head,
        out_shape=jax.ShapeDtypeStruct((count, width), jnp.bfloat16),
        cost_estimate=pl.CostEstimate(flops=2 * count * width * HDIM, transcendentals=0, bytes_accessed=4 * count * width),
    )(x, swap_matrix(), *tables)


def sink_kernel(flags, q_ref, kk_ref, vk_ref, swap_ref, cq, sq, m_ref, l_ref, o_ref, out_ref):
    swap = swap_ref[...]
    q = rotate_ref(q_ref, cq, sq, swap)
    m_sink, l_sink, o_sink = attend_ref(q, kk_ref[...], vk_ref)
    sink_used = flags[1] != 0
    m_near = m_ref[:, :1]
    top = jnp.maximum(m_near, jnp.where(sink_used, m_sink, m_near))
    c_near = jnp.exp(m_near - top)
    c_sink = jnp.where(sink_used, jnp.exp(m_sink - top), 0.0)
    numer = o_ref[...] * c_near + o_sink * c_sink
    denom = l_ref[:, :1] * c_near + l_sink * c_sink
    out_ref[...] = (numer / denom).astype(out_ref.dtype)


def specs(count):
    head = pl.BlockSpec((count, HDIM), lambda h, flags: (0, h))
    whole = pl.BlockSpec((count, HDIM), lambda h, flags: (0, 0))
    swap = pl.BlockSpec((HDIM, HDIM), lambda h, flags: (0, 0))
    return head, whole, swap


def swap_matrix():
    lane = jnp.arange(HDIM)
    return (lane[:, None] == (lane[None, :] ^ 1)).astype(jnp.bfloat16)


def near_attention(flags, queries, blocks, tables):
    count, width = queries.shape
    heads_here = width // HDIM
    head, whole, swap = specs(count)
    value_spec = pl.BlockSpec((count, HDIM), lambda h, flags: (1, h))
    grid_spec = pltpu.PrefetchScalarGridSpec(
        num_scalar_prefetch=1,
        grid=(heads_here,),
        in_specs=[head] * 4 + [value_spec, swap] + [whole] * 2,
        out_specs=[head] * 3,
    )
    cost = pl.CostEstimate(
        flops=heads_here * 2 * 4 * count * count * HDIM,
        transcendentals=heads_here * 2 * count * count,
        bytes_accessed=5 * count * width * 2 + 3 * count * width * 4,
    )
    f32 = jax.ShapeDtypeStruct((count, width), jnp.float32)
    return pl.pallas_call(
        near_kernel, grid_spec=grid_spec, out_shape=[f32] * 3, cost_estimate=cost
    )(flags, queries, *blocks, swap_matrix(), *tables)


def sink_attention(flags, queries, blocks, tables, near, half, halves):
    count, width = queries.shape
    heads_here = width // HDIM
    rows = count // halves
    part = pl.BlockSpec((rows, HDIM), lambda h, flags: (half, h))
    part_table = pl.BlockSpec((rows, HDIM), lambda h, flags: (half, 0))
    key_spec = pl.BlockSpec((count, HDIM), lambda h, flags: (0, h))
    value_spec = pl.BlockSpec((count, HDIM), lambda h, flags: (1, h))
    swap = pl.BlockSpec((HDIM, HDIM), lambda h, flags: (0, 0))
    grid_spec = pltpu.PrefetchScalarGridSpec(
        num_scalar_prefetch=1,
        grid=(heads_here,),
        in_specs=[part, key_spec, value_spec, swap] + [part_table] * 2 + [part] * 3,
        out_specs=pl.BlockSpec((rows, HDIM), lambda h, flags: (0, h)),
    )
    cost = pl.CostEstimate(
        flops=heads_here * 4 * rows * count * HDIM,
        transcendentals=heads_here * rows * count,
        bytes_accessed=(rows + 2 * count) * width * 2 + 3 * rows * width * 4,
    )
    return pl.pallas_call(
        sink_kernel,
        grid_spec=grid_spec,
        out_shape=jax.ShapeDtypeStruct((rows, width), jnp.bfloat16),
        cost_estimate=cost,
    )(flags, queries, *blocks, swap_matrix(), *tables, *near)


def weight_blocks(out_weight):
    n_xl, n_c = lax.axis_size("xl"), lax.axis_size("c")
    block = out_weight.shape[1] // (n_xl * n_c)
    c = lax.axis_index("c")

    def columns(core):
        return jnp.stack(
            [lax.dynamic_slice_in_dim(out_weight, (x * n_c + core) * block, block, axis=1) for x in range(n_xl)]
        )

    return columns(c), columns(1 - c)


def head_reduce(attended, mine_w, other_w):
    xl = lax.axis_index("xl")
    mine = jnp.einsum("rk,xkn->xrn", attended, mine_w, preferred_element_type=jnp.float32).astype(jnp.bfloat16)
    other = jnp.einsum("rk,xkn->xrn", attended, other_w, preferred_element_type=jnp.float32).astype(jnp.bfloat16)
    got = lax.ppermute(other, "c", [(0, 1), (1, 0)])
    chip = (mine.astype(jnp.float32) + got.astype(jnp.float32)).astype(jnp.bfloat16)
    keep = lax.dynamic_index_in_dim(chip, xl, axis=0, keepdims=False)
    send = lax.dynamic_index_in_dim(chip, 1 - xl, axis=0, keepdims=False)
    got = lax.ppermute(send, "xl", [(0, 1), (1, 0)])
    return (keep.astype(jnp.float32) + got.astype(jnp.float32)).astype(jnp.bfloat16)


def shards(queries, keys, values, out_weight, sink_owner, frame_pos):
    count = queries.shape[0]
    place = frame_index()
    n_frame = lax.axis_size(FRAME_AXES)
    sink = sink_owner[0] % (n_frame // 2)
    own_tables = rope_tables(frame_pos[0], count)
    rot_k = rope(keys, own_tables)
    prev_kv, sink_kv = exchange(jnp.concatenate([rot_k, values], axis=0), sink)
    prev_used = (place >= 1) & (place - 1 != sink)
    sink_used = sink < place
    flags = jnp.stack([prev_used, sink_used]).astype(jnp.int32)
    near = near_attention(flags, queries, (rot_k, values, prev_kv, prev_kv), own_tables)
    halves = 2
    mine_w, other_w = weight_blocks(out_weight)
    outs = []
    for half in range(halves):
        attended = sink_attention(flags, queries, (sink_kv, sink_kv), own_tables, near, half, halves)
        outs.append(head_reduce(attended, mine_w, other_w))
    mixed = jnp.concatenate(outs, axis=0)
    return mixed


def solution(mesh):
    frame_phys = {"z": 4, "xh": 2, "y": 4}
    head_phys = {"xl": 2, "c": 2}
    assert mesh.shape["frame"] == 32 and mesh.shape["head"] == 4
    devices = mesh.devices.reshape(tuple(frame_phys.values()) + tuple(head_phys.values()))
    fine = Mesh(devices, FRAME_AXES + HEAD_AXES)
    in_specs = (
        P(FRAME_AXES, HEAD_AXES),
        P(FRAME_AXES, HEAD_AXES),
        P(FRAME_AXES, HEAD_AXES),
        P(HEAD_AXES, None),
        P(),
        P(FRAME_AXES),
    )
    out_specs = P(FRAME_AXES, HEAD_AXES)
    inner = jax.shard_map(shards, mesh=fine, in_specs=in_specs, out_specs=out_specs, check_vma=False)

    def run(*args):
        out = inner(*args)
        return jax.lax.with_sharding_constraint(out, NamedSharding(mesh, P("frame", "head")))

    return run
```

```python
import jax
import jax.numpy as jnp
from jax import lax
from jax.experimental import pallas as pl
from jax.experimental.pallas import tpu as pltpu
from jax.sharding import Mesh, NamedSharding, PartitionSpec as P

HDIM = 128
GRID_W = 32


def shifted(array, axis, by):
    length = lax.axis_size(axis)
    pairs = [(i, i + by) for i in range(length) if 0 <= i + by < length]
    return lax.ppermute(array, axis, pairs)


def broadcast(value, axis, source):
    kept = jnp.where(lax.axis_index(axis) == source, value, 0).astype(value.dtype)
    return lax.psum(kept, axis)


def pair_angles(frame_value, count):
    half = HDIM // 2
    tdim = HDIM - 4 * (HDIM // 6)
    sdim = 2 * (HDIM // 6)
    tcount = tdim // 2
    scount = sdim // 2
    index = jnp.arange(half)
    findex = index.astype(jnp.float32)
    freq = jnp.where(
        index < tcount,
        jnp.power(10000.0, -2.0 * findex / tdim),
        jnp.where(
            index < tcount + scount,
            jnp.power(10000.0, -2.0 * (findex - tcount) / sdim),
            jnp.power(10000.0, -2.0 * (findex - tcount - scount) / sdim),
        ),
    )
    token = jnp.arange(count)
    row_pos = (token // GRID_W).astype(jnp.float32)[:, None]
    col_pos = (token % GRID_W).astype(jnp.float32)[:, None]
    frame_f = jnp.zeros((count, 1), jnp.float32) + frame_value.astype(jnp.float32)
    pos = jnp.where(
        index[None, :] < tcount,
        frame_f,
        jnp.where(index[None, :] < tcount + scount, row_pos, col_pos),
    )
    return pos * freq[None, :]


def rotate(block, angle):
    count = block.shape[0]
    heads_here = block.shape[1] // HDIM
    parts = block.astype(jnp.float32).reshape(count, heads_here, HDIM // 2, 2)
    cosine = jnp.cos(angle)[:, None, :]
    sine = jnp.sin(angle)[:, None, :]
    first = parts[..., 0] * cosine - parts[..., 1] * sine
    second = parts[..., 0] * sine + parts[..., 1] * cosine
    return (
        jnp.stack([first, second], axis=-1).reshape(count, heads_here * HDIM).astype(jnp.bfloat16)
    )


def attend_block(query, key_block, value_block):
    count = query.shape[0]
    heads_here = query.shape[1] // HDIM
    qh = query.reshape(count, heads_here, HDIM)
    kh = key_block.reshape(-1, heads_here, HDIM)
    vh = value_block.reshape(-1, heads_here, HDIM)
    scores = jnp.einsum("qhd,khd->hqk", qh, kh, preferred_element_type=jnp.float32) / jnp.sqrt(
        jnp.float32(HDIM)
    )
    peak = jnp.max(scores, axis=-1)
    weights = jnp.exp(scores - peak[..., None]).astype(jnp.bfloat16)
    total = jnp.sum(weights.astype(jnp.float32), axis=-1)
    partial_value = jnp.einsum("hqk,khd->hqd", weights, vh, preferred_element_type=jnp.float32)
    return (peak, total, partial_value)


FRAME_AXES = ("z", "xh", "y")
HEAD_AXES = ("xl", "c")


def frame_index():
    return (lax.axis_index("z") * lax.axis_size("xh") + lax.axis_index("xh")) * lax.axis_size("y") + lax.axis_index(
        "y"
    )


def cyclic(array, axis, by):
    length = lax.axis_size(axis)
    return lax.ppermute(array, axis, [(i, (i + by) % length) for i in range(length)])


def ring_stage(data, axis, source):
    length = lax.axis_size(axis)
    if length == 1:
        return data
    rel = (lax.axis_index(axis) - source) % length
    if length == 2:
        got = cyclic(data, axis, 1)
        return jnp.where(rel == 0, data, got)
    assert length == 4
    half = data.shape[0] // 2
    h0, h1 = data[:half], data[half:]
    g0 = cyclic(h0, axis, 1)
    g1 = cyclic(h1, axis, -1)
    a0 = jnp.where(rel == 1, g0, h0)
    a1 = jnp.where(rel == 3, g1, h1)
    r_p = cyclic(jnp.where(rel == 0, h1, a0), axis, 1)
    r_m = cyclic(jnp.where(rel == 0, h0, a1), axis, -1)
    out0 = jnp.where(rel == 0, h0, jnp.where(rel == 1, g0, jnp.where(rel == 2, r_p, r_m)))
    out1 = jnp.where(rel == 0, h1, jnp.where(rel == 1, r_p, jnp.where(rel == 2, r_m, g1)))
    return jnp.concatenate([out0, out1], axis=0)


def exchange(data, sink, early):
    n_frame = lax.axis_size(FRAME_AXES)
    piece = data.shape[0] // n_frame
    spread = lax.all_to_all(data, FRAME_AXES, 0, 0, tiled=True)
    pieces = spread.reshape((n_frame, piece) + data.shape[1:])
    before = jnp.concatenate([pieces[-1:], pieces[:-1]], axis=0).reshape(data.shape)
    prev_full = lax.all_to_all(before, FRAME_AXES, 0, 0, tiled=True)
    mine = lax.dynamic_slice_in_dim(spread, sink * piece, piece, axis=0)
    copies = jnp.broadcast_to(mine[None], (n_frame,) + mine.shape).reshape(data.shape)
    copies, prev_full, early = lax.optimization_barrier((copies, prev_full, early))
    return prev_full, lax.all_to_all(copies, FRAME_AXES, 0, 0, tiled=True), early


def rope_tables(frame_value, count):
    angle = pair_angles(frame_value, count)
    cosine = jnp.cos(angle)
    sine = jnp.sin(angle)
    cos_full = jnp.stack([cosine, cosine], axis=-1).reshape(count, HDIM)
    sin_signed = jnp.stack([-sine, sine], axis=-1).reshape(count, HDIM)
    return cos_full, sin_signed


def rotate_ref(x_ref, cos_ref, sin_ref, swap):
    x = x_ref[...]
    partner = jnp.dot(x, swap, preferred_element_type=jnp.float32)
    return (x.astype(jnp.float32) * cos_ref[...] + partner * sin_ref[...]).astype(jnp.bfloat16)


def attend_ref(q, k, v_ref):
    scale = 1.0 / jnp.sqrt(jnp.float32(HDIM))
    raw = lax.dot_general(q, k, (((1,), (1,)), ((), ())), preferred_element_type=jnp.float32)
    raw_peak = jnp.max(raw, axis=-1, keepdims=True)
    peak = raw_peak * scale
    weights = jnp.exp((raw - raw_peak) * scale).astype(jnp.bfloat16)
    total = jnp.sum(weights.astype(jnp.float32), axis=-1, keepdims=True)
    partial_value = jnp.dot(weights, v_ref[...], preferred_element_type=jnp.float32)
    return peak, total, partial_value


def near_kernel(flags, q_ref, ks_ref, vs_ref, kp_ref, vp_ref, swap_ref, cq, sq, m_ref, l_ref, o_ref):
    swap = swap_ref[...]
    q = rotate_ref(q_ref, cq, sq, swap)
    m_self, l_self, o_self = attend_ref(q, ks_ref[...], vs_ref)
    m_prev, l_prev, o_prev = attend_ref(q, kp_ref[...], vp_ref)
    prev_used = flags[0] != 0
    top = jnp.maximum(m_self, jnp.where(prev_used, m_prev, m_self))
    c_self = jnp.exp(m_self - top)
    c_prev = jnp.where(prev_used, jnp.exp(m_prev - top), 0.0)
    m_ref[...] = jnp.broadcast_to(top, m_ref.shape)
    l_ref[...] = jnp.broadcast_to(l_self * c_self + l_prev * c_prev, l_ref.shape)
    o_ref[...] = o_self * c_self + o_prev * c_prev


def rope_kernel(x_ref, swap_ref, cos_ref, sin_ref, out_ref):
    out_ref[...] = rotate_ref(x_ref, cos_ref, sin_ref, swap_ref[...])


def rope(x, tables):
    count, width = x.shape
    head = pl.BlockSpec((count, HDIM), lambda h: (0, h))
    whole = pl.BlockSpec((count, HDIM), lambda h: (0, 0))
    swap = pl.BlockSpec((HDIM, HDIM), lambda h: (0, 0))
    return pl.pallas_call(
        rope_kernel,
        grid=(width // HDIM,),
        in_specs=[head, swap, whole, whole],
        out_specs=head,
        out_shape=jax.ShapeDtypeStruct((count, width), jnp.bfloat16),
        cost_estimate=pl.CostEstimate(flops=2 * count * width * HDIM, transcendentals=0, bytes_accessed=4 * count * width),
    )(x, swap_matrix(), *tables)


def sink_kernel(flags, q_ref, kk_ref, vk_ref, swap_ref, cq, sq, m_ref, l_ref, o_ref, out_ref):
    swap = swap_ref[...]
    q = rotate_ref(q_ref, cq, sq, swap)
    m_sink, l_sink, o_sink = attend_ref(q, kk_ref[...], vk_ref)
    sink_used = flags[1] != 0
    m_near = m_ref[:, :1]
    top = jnp.maximum(m_near, jnp.where(sink_used, m_sink, m_near))
    c_near = jnp.exp(m_near - top)
    c_sink = jnp.where(sink_used, jnp.exp(m_sink - top), 0.0)
    numer = o_ref[...] * c_near + o_sink * c_sink
    denom = l_ref[:, :1] * c_near + l_sink * c_sink
    out_ref[...] = (numer / denom).astype(out_ref.dtype)


def specs(count):
    head = pl.BlockSpec((count, HDIM), lambda h, flags: (0, h))
    whole = pl.BlockSpec((count, HDIM), lambda h, flags: (0, 0))
    swap = pl.BlockSpec((HDIM, HDIM), lambda h, flags: (0, 0))
    return head, whole, swap


def swap_matrix():
    lane = jnp.arange(HDIM)
    return (lane[:, None] == (lane[None, :] ^ 1)).astype(jnp.bfloat16)


def near_attention(flags, queries, blocks, tables):
    count, width = queries.shape
    heads_here = width // HDIM
    head, whole, swap = specs(count)
    value_spec = pl.BlockSpec((count, HDIM), lambda h, flags: (1, h))
    grid_spec = pltpu.PrefetchScalarGridSpec(
        num_scalar_prefetch=1,
        grid=(heads_here,),
        in_specs=[head] * 4 + [value_spec, swap] + [whole] * 2,
        out_specs=[head] * 3,
    )
    cost = pl.CostEstimate(
        flops=heads_here * 2 * 4 * count * count * HDIM,
        transcendentals=heads_here * 2 * count * count,
        bytes_accessed=5 * count * width * 2 + 3 * count * width * 4,
    )
    f32 = jax.ShapeDtypeStruct((count, width), jnp.float32)
    return pl.pallas_call(
        near_kernel, grid_spec=grid_spec, out_shape=[f32] * 3, cost_estimate=cost
    )(flags, queries, *blocks, swap_matrix(), *tables)


def sink_attention(flags, queries, blocks, tables, near, half, halves):
    count, width = queries.shape
    heads_here = width // HDIM
    rows = count // halves
    part = pl.BlockSpec((rows, HDIM), lambda h, flags: (half, h))
    part_table = pl.BlockSpec((rows, HDIM), lambda h, flags: (half, 0))
    key_spec = pl.BlockSpec((count, HDIM), lambda h, flags: (0, h))
    value_spec = pl.BlockSpec((count, HDIM), lambda h, flags: (1, h))
    swap = pl.BlockSpec((HDIM, HDIM), lambda h, flags: (0, 0))
    grid_spec = pltpu.PrefetchScalarGridSpec(
        num_scalar_prefetch=1,
        grid=(heads_here,),
        in_specs=[part, key_spec, value_spec, swap] + [part_table] * 2 + [part] * 3,
        out_specs=pl.BlockSpec((rows, HDIM), lambda h, flags: (0, h)),
    )
    cost = pl.CostEstimate(
        flops=heads_here * 4 * rows * count * HDIM,
        transcendentals=heads_here * rows * count,
        bytes_accessed=(rows + 2 * count) * width * 2 + 3 * rows * width * 4,
    )
    return pl.pallas_call(
        sink_kernel,
        grid_spec=grid_spec,
        out_shape=jax.ShapeDtypeStruct((rows, width), jnp.bfloat16),
        cost_estimate=cost,
    )(flags, queries, *blocks, swap_matrix(), *tables, *near)


def weight_blocks(out_weight):
    n_xl, n_c = lax.axis_size("xl"), lax.axis_size("c")
    block = out_weight.shape[1] // (n_xl * n_c)
    c = lax.axis_index("c")

    def columns(core):
        return jnp.stack(
            [lax.dynamic_slice_in_dim(out_weight, (x * n_c + core) * block, block, axis=1) for x in range(n_xl)]
        )

    return columns(c), columns(1 - c)


def head_reduce(attended, mine_w, other_w):
    xl = lax.axis_index("xl")
    mine = jnp.einsum("rk,xkn->xrn", attended, mine_w, preferred_element_type=jnp.float32).astype(jnp.bfloat16)
    other = jnp.einsum("rk,xkn->xrn", attended, other_w, preferred_element_type=jnp.float32).astype(jnp.bfloat16)
    got = lax.ppermute(other, "c", [(0, 1), (1, 0)])
    chip = (mine.astype(jnp.float32) + got.astype(jnp.float32)).astype(jnp.bfloat16)
    keep = lax.dynamic_index_in_dim(chip, xl, axis=0, keepdims=False)
    send = lax.dynamic_index_in_dim(chip, 1 - xl, axis=0, keepdims=False)
    got = lax.ppermute(send, "xl", [(0, 1), (1, 0)])
    return (keep.astype(jnp.float32) + got.astype(jnp.float32)).astype(jnp.bfloat16)


def shards(queries, keys, values, out_weight, sink_owner, frame_pos):
    count = queries.shape[0]
    place = frame_index()
    n_frame = lax.axis_size(FRAME_AXES)
    sink = sink_owner[0] % (n_frame // 2)
    own_tables = rope_tables(frame_pos[0], count)
    rot_k = rope(keys, own_tables)
    prev_kv, sink_kv, (mine_w, other_w) = exchange(
        jnp.concatenate([rot_k, values], axis=0), sink, weight_blocks(out_weight)
    )
    prev_used = (place >= 1) & (place - 1 != sink)
    sink_used = sink < place
    flags = jnp.stack([prev_used, sink_used]).astype(jnp.int32)
    near = near_attention(flags, queries, (rot_k, values, prev_kv, prev_kv), own_tables)
    halves = 2
    outs = []
    for half in range(halves):
        attended = sink_attention(flags, queries, (sink_kv, sink_kv), own_tables, near, half, halves)
        outs.append(head_reduce(attended, mine_w, other_w))
    mixed = jnp.concatenate(outs, axis=0)
    return mixed


def solution(mesh):
    frame_phys = {"z": 4, "xh": 2, "y": 4}
    head_phys = {"xl": 2, "c": 2}
    assert mesh.shape["frame"] == 32 and mesh.shape["head"] == 4
    devices = mesh.devices.reshape(tuple(frame_phys.values()) + tuple(head_phys.values()))
    fine = Mesh(devices, FRAME_AXES + HEAD_AXES)
    in_specs = (
        P(FRAME_AXES, HEAD_AXES),
        P(FRAME_AXES, HEAD_AXES),
        P(FRAME_AXES, HEAD_AXES),
        P(HEAD_AXES, None),
        P(),
        P(FRAME_AXES),
    )
    out_specs = P(FRAME_AXES, HEAD_AXES)
    inner = jax.shard_map(shards, mesh=fine, in_specs=in_specs, out_specs=out_specs, check_vma=False)

    def run(*args):
        out = inner(*args)
        return jax.lax.with_sharding_constraint(out, NamedSharding(mesh, P("frame", "head")))

    return run
```

```python
import jax
import jax.numpy as jnp
from jax import lax
from jax.experimental import pallas as pl
from jax.experimental.pallas import tpu as pltpu
from jax.sharding import Mesh, NamedSharding, PartitionSpec as P

HDIM = 128
GRID_W = 32


def shifted(array, axis, by):
    length = lax.axis_size(axis)
    pairs = [(i, i + by) for i in range(length) if 0 <= i + by < length]
    return lax.ppermute(array, axis, pairs)


def broadcast(value, axis, source):
    kept = jnp.where(lax.axis_index(axis) == source, value, 0).astype(value.dtype)
    return lax.psum(kept, axis)


def pair_angles(frame_value, count):
    half = HDIM // 2
    tdim = HDIM - 4 * (HDIM // 6)
    sdim = 2 * (HDIM // 6)
    tcount = tdim // 2
    scount = sdim // 2
    index = jnp.arange(half)
    findex = index.astype(jnp.float32)
    freq = jnp.where(
        index < tcount,
        jnp.power(10000.0, -2.0 * findex / tdim),
        jnp.where(
            index < tcount + scount,
            jnp.power(10000.0, -2.0 * (findex - tcount) / sdim),
            jnp.power(10000.0, -2.0 * (findex - tcount - scount) / sdim),
        ),
    )
    token = jnp.arange(count)
    row_pos = (token // GRID_W).astype(jnp.float32)[:, None]
    col_pos = (token % GRID_W).astype(jnp.float32)[:, None]
    frame_f = jnp.zeros((count, 1), jnp.float32) + frame_value.astype(jnp.float32)
    pos = jnp.where(
        index[None, :] < tcount,
        frame_f,
        jnp.where(index[None, :] < tcount + scount, row_pos, col_pos),
    )
    return pos * freq[None, :]


def rotate(block, angle):
    count = block.shape[0]
    heads_here = block.shape[1] // HDIM
    parts = block.astype(jnp.float32).reshape(count, heads_here, HDIM // 2, 2)
    cosine = jnp.cos(angle)[:, None, :]
    sine = jnp.sin(angle)[:, None, :]
    first = parts[..., 0] * cosine - parts[..., 1] * sine
    second = parts[..., 0] * sine + parts[..., 1] * cosine
    return (
        jnp.stack([first, second], axis=-1).reshape(count, heads_here * HDIM).astype(jnp.bfloat16)
    )


def attend_block(query, key_block, value_block):
    count = query.shape[0]
    heads_here = query.shape[1] // HDIM
    qh = query.reshape(count, heads_here, HDIM)
    kh = key_block.reshape(-1, heads_here, HDIM)
    vh = value_block.reshape(-1, heads_here, HDIM)
    scores = jnp.einsum("qhd,khd->hqk", qh, kh, preferred_element_type=jnp.float32) / jnp.sqrt(
        jnp.float32(HDIM)
    )
    peak = jnp.max(scores, axis=-1)
    weights = jnp.exp(scores - peak[..., None]).astype(jnp.bfloat16)
    total = jnp.sum(weights.astype(jnp.float32), axis=-1)
    partial_value = jnp.einsum("hqk,khd->hqd", weights, vh, preferred_element_type=jnp.float32)
    return (peak, total, partial_value)


FRAME_AXES = ("z", "xh", "y")
HEAD_AXES = ("xl", "c")


def frame_index():
    return (lax.axis_index("z") * lax.axis_size("xh") + lax.axis_index("xh")) * lax.axis_size("y") + lax.axis_index(
        "y"
    )


def cyclic(array, axis, by):
    length = lax.axis_size(axis)
    return lax.ppermute(array, axis, [(i, (i + by) % length) for i in range(length)])


def ring_stage(data, axis, source):
    length = lax.axis_size(axis)
    if length == 1:
        return data
    rel = (lax.axis_index(axis) - source) % length
    if length == 2:
        got = cyclic(data, axis, 1)
        return jnp.where(rel == 0, data, got)
    assert length == 4
    half = data.shape[0] // 2
    h0, h1 = data[:half], data[half:]
    g0 = cyclic(h0, axis, 1)
    g1 = cyclic(h1, axis, -1)
    a0 = jnp.where(rel == 1, g0, h0)
    a1 = jnp.where(rel == 3, g1, h1)
    r_p = cyclic(jnp.where(rel == 0, h1, a0), axis, 1)
    r_m = cyclic(jnp.where(rel == 0, h0, a1), axis, -1)
    out0 = jnp.where(rel == 0, h0, jnp.where(rel == 1, g0, jnp.where(rel == 2, r_p, r_m)))
    out1 = jnp.where(rel == 0, h1, jnp.where(rel == 1, r_p, jnp.where(rel == 2, r_m, g1)))
    return jnp.concatenate([out0, out1], axis=0)


def exchange(data, sink):
    n_frame = lax.axis_size(FRAME_AXES)
    piece = data.shape[0] // n_frame
    spread = lax.all_to_all(data, FRAME_AXES, 0, 0, tiled=True)
    pieces = spread.reshape((n_frame, piece) + data.shape[1:])
    before = jnp.concatenate([pieces[-1:], pieces[:-1]], axis=0).reshape(data.shape)
    prev_full = lax.all_to_all(before, FRAME_AXES, 0, 0, tiled=True)
    mine = lax.dynamic_slice_in_dim(spread, sink * piece, piece, axis=0)
    copies = jnp.broadcast_to(mine[None], (n_frame,) + mine.shape).reshape(data.shape)
    copies, prev_full = lax.optimization_barrier((copies, prev_full))
    return prev_full, lax.all_to_all(copies, FRAME_AXES, 0, 0, tiled=True)


def rope_tables(frame_value, count):
    angle = pair_angles(frame_value, count)
    cosine = jnp.cos(angle)
    sine = jnp.sin(angle)
    cos_full = jnp.stack([cosine, cosine], axis=-1).reshape(count, HDIM)
    sin_signed = jnp.stack([-sine, sine], axis=-1).reshape(count, HDIM)
    return cos_full, sin_signed


def rotate_ref(x_ref, cos_ref, sin_ref, swap):
    x = x_ref[...]
    partner = jnp.dot(x, swap, preferred_element_type=jnp.float32)
    return (x.astype(jnp.float32) * cos_ref[...] + partner * sin_ref[...]).astype(jnp.bfloat16)


def attend_ref(q, k, v_ref):
    scale = 1.0 / jnp.sqrt(jnp.float32(HDIM))
    raw = lax.dot_general(q, k, (((1,), (1,)), ((), ())), preferred_element_type=jnp.float32)
    raw_peak = jnp.max(raw, axis=-1, keepdims=True)
    peak = raw_peak * scale
    weights = jnp.exp((raw - raw_peak) * scale).astype(jnp.bfloat16)
    total = jnp.sum(weights.astype(jnp.float32), axis=-1, keepdims=True)
    partial_value = jnp.dot(weights, v_ref[...], preferred_element_type=jnp.float32)
    return peak, total, partial_value


def near_kernel(flags, q_ref, ks_ref, vs_ref, kp_ref, vp_ref, swap_ref, cq, sq, m_ref, l_ref, o_ref):
    swap = swap_ref[...]
    q = rotate_ref(q_ref, cq, sq, swap)
    m_self, l_self, o_self = attend_ref(q, ks_ref[...], vs_ref)
    m_prev, l_prev, o_prev = attend_ref(q, kp_ref[...], vp_ref)
    prev_used = flags[0] != 0
    top = jnp.maximum(m_self, jnp.where(prev_used, m_prev, m_self))
    c_self = jnp.exp(m_self - top)
    c_prev = jnp.where(prev_used, jnp.exp(m_prev - top), 0.0)
    m_ref[...] = jnp.broadcast_to(top, m_ref.shape)
    l_ref[...] = jnp.broadcast_to(l_self * c_self + l_prev * c_prev, l_ref.shape)
    o_ref[...] = o_self * c_self + o_prev * c_prev


def rope_kernel(x_ref, swap_ref, cos_ref, sin_ref, out_ref):
    out_ref[...] = rotate_ref(x_ref, cos_ref, sin_ref, swap_ref[...])


def rope(x, tables):
    count, width = x.shape
    head = pl.BlockSpec((count, HDIM), lambda h: (0, h))
    whole = pl.BlockSpec((count, HDIM), lambda h: (0, 0))
    swap = pl.BlockSpec((HDIM, HDIM), lambda h: (0, 0))
    return pl.pallas_call(
        rope_kernel,
        grid=(width // HDIM,),
        in_specs=[head, swap, whole, whole],
        out_specs=head,
        out_shape=jax.ShapeDtypeStruct((count, width), jnp.bfloat16),
        cost_estimate=pl.CostEstimate(flops=2 * count * width * HDIM, transcendentals=0, bytes_accessed=4 * count * width),
    )(x, swap_matrix(), *tables)


def sink_kernel(flags, q_ref, kk_ref, vk_ref, swap_ref, cq, sq, m_ref, l_ref, o_ref, out_ref):
    swap = swap_ref[...]
    sink_used = flags[1] != 0
    for j in range(q_ref.shape[1] // HDIM):
        cols = slice(j * HDIM, (j + 1) * HDIM)
        q = rotate_ref(q_ref.at[:, cols], cq, sq, swap)
        m_sink, l_sink, o_sink = attend_ref(q, kk_ref[:, cols], vk_ref.at[:, cols])
        m_near = m_ref[:, j * HDIM : j * HDIM + 1]
        top = jnp.maximum(m_near, jnp.where(sink_used, m_sink, m_near))
        c_near = jnp.exp(m_near - top)
        c_sink = jnp.where(sink_used, jnp.exp(m_sink - top), 0.0)
        numer = o_ref[:, cols] * c_near + o_sink * c_sink
        denom = l_ref[:, j * HDIM : j * HDIM + 1] * c_near + l_sink * c_sink
        out_ref[:, cols] = (numer / denom).astype(out_ref.dtype)


def specs(count):
    head = pl.BlockSpec((count, HDIM), lambda h, flags: (0, h))
    whole = pl.BlockSpec((count, HDIM), lambda h, flags: (0, 0))
    swap = pl.BlockSpec((HDIM, HDIM), lambda h, flags: (0, 0))
    return head, whole, swap


def swap_matrix():
    lane = jnp.arange(HDIM)
    return (lane[:, None] == (lane[None, :] ^ 1)).astype(jnp.bfloat16)


def near_attention(flags, queries, blocks, tables):
    count, width = queries.shape
    heads_here = width // HDIM
    head, whole, swap = specs(count)
    value_spec = pl.BlockSpec((count, HDIM), lambda h, flags: (1, h))
    grid_spec = pltpu.PrefetchScalarGridSpec(
        num_scalar_prefetch=1,
        grid=(heads_here,),
        in_specs=[head] * 4 + [value_spec, swap] + [whole] * 2,
        out_specs=[head] * 3,
    )
    cost = pl.CostEstimate(
        flops=heads_here * 2 * 4 * count * count * HDIM,
        transcendentals=heads_here * 2 * count * count,
        bytes_accessed=5 * count * width * 2 + 3 * count * width * 4,
    )
    f32 = jax.ShapeDtypeStruct((count, width), jnp.float32)
    return pl.pallas_call(
        near_kernel, grid_spec=grid_spec, out_shape=[f32] * 3, cost_estimate=cost
    )(flags, queries, *blocks, swap_matrix(), *tables)


def sink_attention(flags, queries, blocks, tables, near, half, halves):
    count, width = queries.shape
    group = 2
    heads_here = width // HDIM // group
    rows = count // halves
    wide = group * HDIM
    part = pl.BlockSpec((rows, wide), lambda h, flags: (half, h))
    part_table = pl.BlockSpec((rows, HDIM), lambda h, flags: (half, 0))
    key_spec = pl.BlockSpec((count, wide), lambda h, flags: (0, h))
    value_spec = pl.BlockSpec((count, wide), lambda h, flags: (1, h))
    swap = pl.BlockSpec((HDIM, HDIM), lambda h, flags: (0, 0))
    grid_spec = pltpu.PrefetchScalarGridSpec(
        num_scalar_prefetch=1,
        grid=(heads_here,),
        in_specs=[part, key_spec, value_spec, swap] + [part_table] * 2 + [part] * 3,
        out_specs=pl.BlockSpec((rows, wide), lambda h, flags: (0, h)),
    )
    cost = pl.CostEstimate(
        flops=heads_here * group * 4 * rows * count * HDIM,
        transcendentals=heads_here * group * rows * count,
        bytes_accessed=(rows + 2 * count) * width * 2 + 3 * rows * width * 4,
    )
    return pl.pallas_call(
        sink_kernel,
        grid_spec=grid_spec,
        out_shape=jax.ShapeDtypeStruct((rows, width), jnp.bfloat16),
        cost_estimate=cost,
    )(flags, queries, *blocks, swap_matrix(), *tables, *near)


def weight_blocks(out_weight):
    n_xl, n_c = lax.axis_size("xl"), lax.axis_size("c")
    block = out_weight.shape[1] // (n_xl * n_c)
    c = lax.axis_index("c")

    def columns(core):
        return jnp.stack(
            [lax.dynamic_slice_in_dim(out_weight, (x * n_c + core) * block, block, axis=1) for x in range(n_xl)]
        )

    return columns(c), columns(1 - c)


def head_reduce(attended, mine_w, other_w):
    xl = lax.axis_index("xl")
    mine = jnp.einsum("rk,xkn->xrn", attended, mine_w, preferred_element_type=jnp.float32).astype(jnp.bfloat16)
    other = jnp.einsum("rk,xkn->xrn", attended, other_w, preferred_element_type=jnp.float32).astype(jnp.bfloat16)
    got = lax.ppermute(other, "c", [(0, 1), (1, 0)])
    chip = (mine.astype(jnp.float32) + got.astype(jnp.float32)).astype(jnp.bfloat16)
    keep = lax.dynamic_index_in_dim(chip, xl, axis=0, keepdims=False)
    send = lax.dynamic_index_in_dim(chip, 1 - xl, axis=0, keepdims=False)
    got = lax.ppermute(send, "xl", [(0, 1), (1, 0)])
    return (keep.astype(jnp.float32) + got.astype(jnp.float32)).astype(jnp.bfloat16)


def shards(queries, keys, values, out_weight, sink_owner, frame_pos):
    count = queries.shape[0]
    place = frame_index()
    n_frame = lax.axis_size(FRAME_AXES)
    sink = sink_owner[0] % (n_frame // 2)
    own_tables = rope_tables(frame_pos[0], count)
    rot_k = rope(keys, own_tables)
    prev_kv, sink_kv = exchange(jnp.concatenate([rot_k, values], axis=0), sink)
    prev_used = (place >= 1) & (place - 1 != sink)
    sink_used = sink < place
    flags = jnp.stack([prev_used, sink_used]).astype(jnp.int32)
    near = near_attention(flags, queries, (rot_k, values, prev_kv, prev_kv), own_tables)
    halves = 2
    mine_w, other_w = weight_blocks(out_weight)
    outs = []
    for half in range(halves):
        attended = sink_attention(flags, queries, (sink_kv, sink_kv), own_tables, near, half, halves)
        outs.append(head_reduce(attended, mine_w, other_w))
    mixed = jnp.concatenate(outs, axis=0)
    return mixed


def solution(mesh):
    frame_phys = {"z": 4, "xh": 2, "y": 4}
    head_phys = {"xl": 2, "c": 2}
    assert mesh.shape["frame"] == 32 and mesh.shape["head"] == 4
    devices = mesh.devices.reshape(tuple(frame_phys.values()) + tuple(head_phys.values()))
    fine = Mesh(devices, FRAME_AXES + HEAD_AXES)
    in_specs = (
        P(FRAME_AXES, HEAD_AXES),
        P(FRAME_AXES, HEAD_AXES),
        P(FRAME_AXES, HEAD_AXES),
        P(HEAD_AXES, None),
        P(),
        P(FRAME_AXES),
    )
    out_specs = P(FRAME_AXES, HEAD_AXES)
    inner = jax.shard_map(shards, mesh=fine, in_specs=in_specs, out_specs=out_specs, check_vma=False)

    def run(*args):
        out = inner(*args)
        return jax.lax.with_sharding_constraint(out, NamedSharding(mesh, P("frame", "head")))

    return run
```

```python
import jax
import jax.numpy as jnp
from jax import lax
from jax.experimental import pallas as pl
from jax.experimental.pallas import tpu as pltpu
from jax.sharding import Mesh, NamedSharding, PartitionSpec as P

HDIM = 128
GRID_W = 32


def shifted(array, axis, by):
    length = lax.axis_size(axis)
    pairs = [(i, i + by) for i in range(length) if 0 <= i + by < length]
    return lax.ppermute(array, axis, pairs)


def broadcast(value, axis, source):
    kept = jnp.where(lax.axis_index(axis) == source, value, 0).astype(value.dtype)
    return lax.psum(kept, axis)


def pair_angles(frame_value, count):
    half = HDIM // 2
    tdim = HDIM - 4 * (HDIM // 6)
    sdim = 2 * (HDIM // 6)
    tcount = tdim // 2
    scount = sdim // 2
    index = jnp.arange(half)
    findex = index.astype(jnp.float32)
    freq = jnp.where(
        index < tcount,
        jnp.power(10000.0, -2.0 * findex / tdim),
        jnp.where(
            index < tcount + scount,
            jnp.power(10000.0, -2.0 * (findex - tcount) / sdim),
            jnp.power(10000.0, -2.0 * (findex - tcount - scount) / sdim),
        ),
    )
    token = jnp.arange(count)
    row_pos = (token // GRID_W).astype(jnp.float32)[:, None]
    col_pos = (token % GRID_W).astype(jnp.float32)[:, None]
    frame_f = jnp.zeros((count, 1), jnp.float32) + frame_value.astype(jnp.float32)
    pos = jnp.where(
        index[None, :] < tcount,
        frame_f,
        jnp.where(index[None, :] < tcount + scount, row_pos, col_pos),
    )
    return pos * freq[None, :]


def rotate(block, angle):
    count = block.shape[0]
    heads_here = block.shape[1] // HDIM
    parts = block.astype(jnp.float32).reshape(count, heads_here, HDIM // 2, 2)
    cosine = jnp.cos(angle)[:, None, :]
    sine = jnp.sin(angle)[:, None, :]
    first = parts[..., 0] * cosine - parts[..., 1] * sine
    second = parts[..., 0] * sine + parts[..., 1] * cosine
    return (
        jnp.stack([first, second], axis=-1).reshape(count, heads_here * HDIM).astype(jnp.bfloat16)
    )


def attend_block(query, key_block, value_block):
    count = query.shape[0]
    heads_here = query.shape[1] // HDIM
    qh = query.reshape(count, heads_here, HDIM)
    kh = key_block.reshape(-1, heads_here, HDIM)
    vh = value_block.reshape(-1, heads_here, HDIM)
    scores = jnp.einsum("qhd,khd->hqk", qh, kh, preferred_element_type=jnp.float32) / jnp.sqrt(
        jnp.float32(HDIM)
    )
    peak = jnp.max(scores, axis=-1)
    weights = jnp.exp(scores - peak[..., None]).astype(jnp.bfloat16)
    total = jnp.sum(weights.astype(jnp.float32), axis=-1)
    partial_value = jnp.einsum("hqk,khd->hqd", weights, vh, preferred_element_type=jnp.float32)
    return (peak, total, partial_value)


FRAME_AXES = ("z", "xh", "y")
HEAD_AXES = ("xl", "c")


def frame_index():
    return (lax.axis_index("z") * lax.axis_size("xh") + lax.axis_index("xh")) * lax.axis_size("y") + lax.axis_index(
        "y"
    )


def cyclic(array, axis, by):
    length = lax.axis_size(axis)
    return lax.ppermute(array, axis, [(i, (i + by) % length) for i in range(length)])


def ring_stage(data, axis, source):
    length = lax.axis_size(axis)
    if length == 1:
        return data
    rel = (lax.axis_index(axis) - source) % length
    if length == 2:
        got = cyclic(data, axis, 1)
        return jnp.where(rel == 0, data, got)
    assert length == 4
    half = data.shape[0] // 2
    h0, h1 = data[:half], data[half:]
    g0 = cyclic(h0, axis, 1)
    g1 = cyclic(h1, axis, -1)
    a0 = jnp.where(rel == 1, g0, h0)
    a1 = jnp.where(rel == 3, g1, h1)
    r_p = cyclic(jnp.where(rel == 0, h1, a0), axis, 1)
    r_m = cyclic(jnp.where(rel == 0, h0, a1), axis, -1)
    out0 = jnp.where(rel == 0, h0, jnp.where(rel == 1, g0, jnp.where(rel == 2, r_p, r_m)))
    out1 = jnp.where(rel == 0, h1, jnp.where(rel == 1, r_p, jnp.where(rel == 2, r_m, g1)))
    return jnp.concatenate([out0, out1], axis=0)


def exchange(data, sink):
    n_frame = lax.axis_size(FRAME_AXES)
    piece = data.shape[0] // n_frame
    spread = lax.all_to_all(data, FRAME_AXES, 0, 0, tiled=True)
    pieces = spread.reshape((n_frame, piece) + data.shape[1:])
    before = jnp.concatenate([pieces[-1:], pieces[:-1]], axis=0).reshape(data.shape)
    prev_full = lax.all_to_all(before, FRAME_AXES, 0, 0, tiled=True)
    mine = lax.dynamic_slice_in_dim(spread, sink * piece, piece, axis=0)
    copies = jnp.broadcast_to(mine[None], (n_frame,) + mine.shape).reshape(data.shape)
    copies, prev_full = lax.optimization_barrier((copies, prev_full))
    return prev_full, lax.all_to_all(copies, FRAME_AXES, 0, 0, tiled=True)


def rope_tables(frame_value, count):
    angle = pair_angles(frame_value, count)
    cosine = jnp.cos(angle)
    sine = jnp.sin(angle)
    cos_full = jnp.stack([cosine, cosine], axis=-1).reshape(count, HDIM)
    sin_signed = jnp.stack([-sine, sine], axis=-1).reshape(count, HDIM)
    return cos_full, sin_signed


def rotate_ref(x_ref, cos_ref, sin_ref, swap):
    x = x_ref[...]
    partner = jnp.dot(x, swap, preferred_element_type=jnp.float32)
    return (x.astype(jnp.float32) * cos_ref[...] + partner * sin_ref[...]).astype(jnp.bfloat16)


def attend_ref(q, k, v_ref):
    scale = 1.0 / jnp.sqrt(jnp.float32(HDIM))
    raw = lax.dot_general(q, k, (((1,), (1,)), ((), ())), preferred_element_type=jnp.float32)
    raw_peak = jnp.max(raw, axis=-1, keepdims=True)
    peak = raw_peak * scale
    weights = jnp.exp((raw - raw_peak) * scale).astype(jnp.bfloat16)
    total = jnp.sum(weights.astype(jnp.float32), axis=-1, keepdims=True)
    partial_value = jnp.dot(weights, v_ref[...], preferred_element_type=jnp.float32)
    return peak, total, partial_value


def near_kernel(flags, q_ref, ks_ref, vs_ref, kp_ref, vp_ref, swap_ref, cq, sq, m_ref, l_ref, o_ref):
    swap = swap_ref[...]
    q = rotate_ref(q_ref, cq, sq, swap)
    m_self, l_self, o_self = attend_ref(q, ks_ref[...], vs_ref)
    m_prev, l_prev, o_prev = attend_ref(q, kp_ref[...], vp_ref)
    prev_used = flags[0] != 0
    top = jnp.maximum(m_self, jnp.where(prev_used, m_prev, m_self))
    c_self = jnp.exp(m_self - top)
    c_prev = jnp.where(prev_used, jnp.exp(m_prev - top), 0.0)
    m_ref[...] = jnp.broadcast_to(top, m_ref.shape)
    l_ref[...] = jnp.broadcast_to(l_self * c_self + l_prev * c_prev, l_ref.shape)
    o_ref[...] = o_self * c_self + o_prev * c_prev


def rope_kernel(x_ref, swap_ref, cos_ref, sin_ref, out_ref):
    out_ref[...] = rotate_ref(x_ref, cos_ref, sin_ref, swap_ref[...])


def rope(x, tables):
    count, width = x.shape
    head = pl.BlockSpec((count, HDIM), lambda h: (0, h))
    whole = pl.BlockSpec((count, HDIM), lambda h: (0, 0))
    swap = pl.BlockSpec((HDIM, HDIM), lambda h: (0, 0))
    return pl.pallas_call(
        rope_kernel,
        grid=(width // HDIM,),
        in_specs=[head, swap, whole, whole],
        out_specs=head,
        out_shape=jax.ShapeDtypeStruct((count, width), jnp.bfloat16),
        cost_estimate=pl.CostEstimate(flops=2 * count * width * HDIM, transcendentals=0, bytes_accessed=4 * count * width),
    )(x, swap_matrix(), *tables)


def sink_kernel(flags, q_ref, kk_ref, vk_ref, swap_ref, cq, sq, m_ref, l_ref, o_ref, out_ref):
    swap = swap_ref[...]
    sink_used = flags[1] != 0
    for j in range(q_ref.shape[1] // HDIM):
        cols = slice(j * HDIM, (j + 1) * HDIM)
        q = rotate_ref(q_ref.at[:, cols], cq, sq, swap)
        m_sink, l_sink, o_sink = attend_ref(q, kk_ref[:, cols], vk_ref.at[:, cols])
        m_near = m_ref[:, j * HDIM : j * HDIM + 1]
        top = jnp.maximum(m_near, jnp.where(sink_used, m_sink, m_near))
        c_near = jnp.exp(m_near - top)
        c_sink = jnp.where(sink_used, jnp.exp(m_sink - top), 0.0)
        numer = o_ref[:, cols] * c_near + o_sink * c_sink
        denom = l_ref[:, j * HDIM : j * HDIM + 1] * c_near + l_sink * c_sink
        out_ref[:, cols] = (numer / denom).astype(out_ref.dtype)


def specs(count):
    head = pl.BlockSpec((count, HDIM), lambda h, flags: (0, h))
    whole = pl.BlockSpec((count, HDIM), lambda h, flags: (0, 0))
    swap = pl.BlockSpec((HDIM, HDIM), lambda h, flags: (0, 0))
    return head, whole, swap


def swap_matrix():
    lane = jnp.arange(HDIM)
    return (lane[:, None] == (lane[None, :] ^ 1)).astype(jnp.bfloat16)


def near_attention(flags, queries, blocks, tables):
    count, width = queries.shape
    heads_here = width // HDIM
    head, whole, swap = specs(count)
    value_spec = pl.BlockSpec((count, HDIM), lambda h, flags: (1, h))
    grid_spec = pltpu.PrefetchScalarGridSpec(
        num_scalar_prefetch=1,
        grid=(heads_here,),
        in_specs=[head] * 4 + [value_spec, swap] + [whole] * 2,
        out_specs=[head] * 3,
    )
    cost = pl.CostEstimate(
        flops=heads_here * 2 * 4 * count * count * HDIM,
        transcendentals=heads_here * 2 * count * count,
        bytes_accessed=5 * count * width * 2 + 3 * count * width * 4,
    )
    f32 = jax.ShapeDtypeStruct((count, width), jnp.float32)
    return pl.pallas_call(
        near_kernel, grid_spec=grid_spec, out_shape=[f32] * 3, cost_estimate=cost
    )(flags, queries, *blocks, swap_matrix(), *tables)


def sink_attention(flags, queries, blocks, tables, near, half, halves):
    count, width = queries.shape
    group = 5
    heads_here = width // HDIM // group
    rows = count // halves
    wide = group * HDIM
    part = pl.BlockSpec((rows, wide), lambda h, flags: (half, h))
    part_table = pl.BlockSpec((rows, HDIM), lambda h, flags: (half, 0))
    key_spec = pl.BlockSpec((count, wide), lambda h, flags: (0, h))
    value_spec = pl.BlockSpec((count, wide), lambda h, flags: (1, h))
    swap = pl.BlockSpec((HDIM, HDIM), lambda h, flags: (0, 0))
    grid_spec = pltpu.PrefetchScalarGridSpec(
        num_scalar_prefetch=1,
        grid=(heads_here,),
        in_specs=[part, key_spec, value_spec, swap] + [part_table] * 2 + [part] * 3,
        out_specs=pl.BlockSpec((rows, wide), lambda h, flags: (0, h)),
    )
    cost = pl.CostEstimate(
        flops=heads_here * group * 4 * rows * count * HDIM,
        transcendentals=heads_here * group * rows * count,
        bytes_accessed=(rows + 2 * count) * width * 2 + 3 * rows * width * 4,
    )
    return pl.pallas_call(
        sink_kernel,
        grid_spec=grid_spec,
        out_shape=jax.ShapeDtypeStruct((rows, width), jnp.bfloat16),
        cost_estimate=cost,
    )(flags, queries, *blocks, swap_matrix(), *tables, *near)


def weight_blocks(out_weight):
    n_xl, n_c = lax.axis_size("xl"), lax.axis_size("c")
    block = out_weight.shape[1] // (n_xl * n_c)
    c = lax.axis_index("c")

    def columns(core):
        return jnp.stack(
            [lax.dynamic_slice_in_dim(out_weight, (x * n_c + core) * block, block, axis=1) for x in range(n_xl)]
        )

    return columns(c), columns(1 - c)


def head_reduce(attended, mine_w, other_w):
    xl = lax.axis_index("xl")
    mine = jnp.einsum("rk,xkn->xrn", attended, mine_w, preferred_element_type=jnp.float32).astype(jnp.bfloat16)
    other = jnp.einsum("rk,xkn->xrn", attended, other_w, preferred_element_type=jnp.float32).astype(jnp.bfloat16)
    got = lax.ppermute(other, "c", [(0, 1), (1, 0)])
    chip = (mine.astype(jnp.float32) + got.astype(jnp.float32)).astype(jnp.bfloat16)
    keep = lax.dynamic_index_in_dim(chip, xl, axis=0, keepdims=False)
    send = lax.dynamic_index_in_dim(chip, 1 - xl, axis=0, keepdims=False)
    got = lax.ppermute(send, "xl", [(0, 1), (1, 0)])
    return (keep.astype(jnp.float32) + got.astype(jnp.float32)).astype(jnp.bfloat16)


def shards(queries, keys, values, out_weight, sink_owner, frame_pos):
    count = queries.shape[0]
    place = frame_index()
    n_frame = lax.axis_size(FRAME_AXES)
    sink = sink_owner[0] % (n_frame // 2)
    own_tables = rope_tables(frame_pos[0], count)
    rot_k = rope(keys, own_tables)
    prev_kv, sink_kv = exchange(jnp.concatenate([rot_k, values], axis=0), sink)
    prev_used = (place >= 1) & (place - 1 != sink)
    sink_used = sink < place
    flags = jnp.stack([prev_used, sink_used]).astype(jnp.int32)
    near = near_attention(flags, queries, (rot_k, values, prev_kv, prev_kv), own_tables)
    halves = 2
    mine_w, other_w = weight_blocks(out_weight)
    outs = []
    for half in range(halves):
        attended = sink_attention(flags, queries, (sink_kv, sink_kv), own_tables, near, half, halves)
        outs.append(head_reduce(attended, mine_w, other_w))
    mixed = jnp.concatenate(outs, axis=0)
    return mixed


def solution(mesh):
    frame_phys = {"z": 4, "xh": 2, "y": 4}
    head_phys = {"xl": 2, "c": 2}
    assert mesh.shape["frame"] == 32 and mesh.shape["head"] == 4
    devices = mesh.devices.reshape(tuple(frame_phys.values()) + tuple(head_phys.values()))
    fine = Mesh(devices, FRAME_AXES + HEAD_AXES)
    in_specs = (
        P(FRAME_AXES, HEAD_AXES),
        P(FRAME_AXES, HEAD_AXES),
        P(FRAME_AXES, HEAD_AXES),
        P(HEAD_AXES, None),
        P(),
        P(FRAME_AXES),
    )
    out_specs = P(FRAME_AXES, HEAD_AXES)
    inner = jax.shard_map(shards, mesh=fine, in_specs=in_specs, out_specs=out_specs, check_vma=False)

    def run(*args):
        out = inner(*args)
        return jax.lax.with_sharding_constraint(out, NamedSharding(mesh, P("frame", "head")))

    return run
```

```python
import jax
import jax.numpy as jnp
from jax import lax
from jax.experimental import pallas as pl
from jax.experimental.pallas import tpu as pltpu
from jax.sharding import Mesh, NamedSharding, PartitionSpec as P

HDIM = 128
GRID_W = 32


def shifted(array, axis, by):
    length = lax.axis_size(axis)
    pairs = [(i, i + by) for i in range(length) if 0 <= i + by < length]
    return lax.ppermute(array, axis, pairs)


def broadcast(value, axis, source):
    kept = jnp.where(lax.axis_index(axis) == source, value, 0).astype(value.dtype)
    return lax.psum(kept, axis)


def pair_angles(frame_value, count):
    half = HDIM // 2
    tdim = HDIM - 4 * (HDIM // 6)
    sdim = 2 * (HDIM // 6)
    tcount = tdim // 2
    scount = sdim // 2
    index = jnp.arange(half)
    findex = index.astype(jnp.float32)
    freq = jnp.where(
        index < tcount,
        jnp.power(10000.0, -2.0 * findex / tdim),
        jnp.where(
            index < tcount + scount,
            jnp.power(10000.0, -2.0 * (findex - tcount) / sdim),
            jnp.power(10000.0, -2.0 * (findex - tcount - scount) / sdim),
        ),
    )
    token = jnp.arange(count)
    row_pos = (token // GRID_W).astype(jnp.float32)[:, None]
    col_pos = (token % GRID_W).astype(jnp.float32)[:, None]
    frame_f = jnp.zeros((count, 1), jnp.float32) + frame_value.astype(jnp.float32)
    pos = jnp.where(
        index[None, :] < tcount,
        frame_f,
        jnp.where(index[None, :] < tcount + scount, row_pos, col_pos),
    )
    return pos * freq[None, :]


def rotate(block, angle):
    count = block.shape[0]
    heads_here = block.shape[1] // HDIM
    parts = block.astype(jnp.float32).reshape(count, heads_here, HDIM // 2, 2)
    cosine = jnp.cos(angle)[:, None, :]
    sine = jnp.sin(angle)[:, None, :]
    first = parts[..., 0] * cosine - parts[..., 1] * sine
    second = parts[..., 0] * sine + parts[..., 1] * cosine
    return (
        jnp.stack([first, second], axis=-1).reshape(count, heads_here * HDIM).astype(jnp.bfloat16)
    )


def attend_block(query, key_block, value_block):
    count = query.shape[0]
    heads_here = query.shape[1] // HDIM
    qh = query.reshape(count, heads_here, HDIM)
    kh = key_block.reshape(-1, heads_here, HDIM)
    vh = value_block.reshape(-1, heads_here, HDIM)
    scores = jnp.einsum("qhd,khd->hqk", qh, kh, preferred_element_type=jnp.float32) / jnp.sqrt(
        jnp.float32(HDIM)
    )
    peak = jnp.max(scores, axis=-1)
    weights = jnp.exp(scores - peak[..., None]).astype(jnp.bfloat16)
    total = jnp.sum(weights.astype(jnp.float32), axis=-1)
    partial_value = jnp.einsum("hqk,khd->hqd", weights, vh, preferred_element_type=jnp.float32)
    return (peak, total, partial_value)


FRAME_AXES = ("z", "xh", "y")
HEAD_AXES = ("xl", "c")


def frame_index():
    return (lax.axis_index("z") * lax.axis_size("xh") + lax.axis_index("xh")) * lax.axis_size("y") + lax.axis_index(
        "y"
    )


def cyclic(array, axis, by):
    length = lax.axis_size(axis)
    return lax.ppermute(array, axis, [(i, (i + by) % length) for i in range(length)])


def ring_stage(data, axis, source):
    length = lax.axis_size(axis)
    if length == 1:
        return data
    rel = (lax.axis_index(axis) - source) % length
    if length == 2:
        got = cyclic(data, axis, 1)
        return jnp.where(rel == 0, data, got)
    assert length == 4
    half = data.shape[0] // 2
    h0, h1 = data[:half], data[half:]
    g0 = cyclic(h0, axis, 1)
    g1 = cyclic(h1, axis, -1)
    a0 = jnp.where(rel == 1, g0, h0)
    a1 = jnp.where(rel == 3, g1, h1)
    r_p = cyclic(jnp.where(rel == 0, h1, a0), axis, 1)
    r_m = cyclic(jnp.where(rel == 0, h0, a1), axis, -1)
    out0 = jnp.where(rel == 0, h0, jnp.where(rel == 1, g0, jnp.where(rel == 2, r_p, r_m)))
    out1 = jnp.where(rel == 0, h1, jnp.where(rel == 1, r_p, jnp.where(rel == 2, r_m, g1)))
    return jnp.concatenate([out0, out1], axis=0)


def exchange(data, sink):
    n_frame = lax.axis_size(FRAME_AXES)
    piece = data.shape[0] // n_frame
    spread = lax.all_to_all(data, FRAME_AXES, 0, 0, tiled=True)
    pieces = spread.reshape((n_frame, piece) + data.shape[1:])
    before = jnp.concatenate([pieces[-1:], pieces[:-1]], axis=0).reshape(data.shape)
    prev_full = lax.all_to_all(before, FRAME_AXES, 0, 0, tiled=True)
    mine = lax.dynamic_slice_in_dim(spread, sink * piece, piece, axis=0)
    copies = jnp.broadcast_to(mine[None], (n_frame,) + mine.shape).reshape(data.shape)
    copies, prev_full = lax.optimization_barrier((copies, prev_full))
    return prev_full, lax.all_to_all(copies, FRAME_AXES, 0, 0, tiled=True)


def rope_tables(frame_value, count):
    angle = pair_angles(frame_value, count)
    cosine = jnp.cos(angle)
    sine = jnp.sin(angle)
    cos_full = jnp.stack([cosine, cosine], axis=-1).reshape(count, HDIM)
    sin_signed = jnp.stack([-sine, sine], axis=-1).reshape(count, HDIM)
    return cos_full, sin_signed


def rotate_ref(x_ref, cos_ref, sin_ref, swap):
    x = x_ref[...]
    partner = jnp.dot(x, swap, preferred_element_type=jnp.float32)
    return (x.astype(jnp.float32) * cos_ref[...] + partner * sin_ref[...]).astype(jnp.bfloat16)


def attend_ref(q, k, v_ref):
    scale = 1.0 / jnp.sqrt(jnp.float32(HDIM))
    raw = lax.dot_general(q, k, (((1,), (1,)), ((), ())), preferred_element_type=jnp.float32)
    raw_peak = jnp.max(raw, axis=-1, keepdims=True)
    peak = raw_peak * scale
    weights = jnp.exp((raw - raw_peak) * scale).astype(jnp.bfloat16)
    total = jnp.sum(weights.astype(jnp.float32), axis=-1, keepdims=True)
    partial_value = jnp.dot(weights, v_ref[...], preferred_element_type=jnp.float32)
    return peak, total, partial_value


def near_kernel(flags, q_ref, ks_ref, vs_ref, kp_ref, vp_ref, swap_ref, cq, sq, m_ref, l_ref, o_ref):
    swap = swap_ref[...]
    q = rotate_ref(q_ref, cq, sq, swap)
    m_self, l_self, o_self = attend_ref(q, ks_ref[...], vs_ref)
    m_prev, l_prev, o_prev = attend_ref(q, kp_ref[...], vp_ref)
    prev_used = flags[0] != 0
    top = jnp.maximum(m_self, jnp.where(prev_used, m_prev, m_self))
    c_self = jnp.exp(m_self - top)
    c_prev = jnp.where(prev_used, jnp.exp(m_prev - top), 0.0)
    m_ref[...] = jnp.broadcast_to(top, m_ref.shape)
    l_ref[...] = jnp.broadcast_to(l_self * c_self + l_prev * c_prev, l_ref.shape)
    o_ref[...] = o_self * c_self + o_prev * c_prev


def rope_kernel(x_ref, swap_ref, cos_ref, sin_ref, out_ref):
    swap = swap_ref[...]
    for j in range(x_ref.shape[1] // HDIM):
        cols = slice(j * HDIM, (j + 1) * HDIM)
        out_ref[:, cols] = rotate_ref(x_ref.at[:, cols], cos_ref, sin_ref, swap)


def rope(x, tables):
    count, width = x.shape
    wide = 5 * HDIM
    head = pl.BlockSpec((count, wide), lambda h: (0, h))
    whole = pl.BlockSpec((count, HDIM), lambda h: (0, 0))
    swap = pl.BlockSpec((HDIM, HDIM), lambda h: (0, 0))
    return pl.pallas_call(
        rope_kernel,
        grid=(width // wide,),
        in_specs=[head, swap, whole, whole],
        out_specs=head,
        out_shape=jax.ShapeDtypeStruct((count, width), jnp.bfloat16),
        cost_estimate=pl.CostEstimate(flops=2 * count * width * HDIM, transcendentals=0, bytes_accessed=4 * count * width),
    )(x, swap_matrix(), *tables)


def sink_kernel(flags, q_ref, kk_ref, vk_ref, swap_ref, cq, sq, m_ref, l_ref, o_ref, out_ref):
    swap = swap_ref[...]
    sink_used = flags[1] != 0
    for j in range(q_ref.shape[1] // HDIM):
        cols = slice(j * HDIM, (j + 1) * HDIM)
        q = rotate_ref(q_ref.at[:, cols], cq, sq, swap)
        m_sink, l_sink, o_sink = attend_ref(q, kk_ref[:, cols], vk_ref.at[:, cols])
        m_near = m_ref[:, j * HDIM : j * HDIM + 1]
        top = jnp.maximum(m_near, jnp.where(sink_used, m_sink, m_near))
        c_near = jnp.exp(m_near - top)
        c_sink = jnp.where(sink_used, jnp.exp(m_sink - top), 0.0)
        numer = o_ref[:, cols] * c_near + o_sink * c_sink
        denom = l_ref[:, j * HDIM : j * HDIM + 1] * c_near + l_sink * c_sink
        out_ref[:, cols] = (numer / denom).astype(out_ref.dtype)


def specs(count):
    head = pl.BlockSpec((count, HDIM), lambda h, flags: (0, h))
    whole = pl.BlockSpec((count, HDIM), lambda h, flags: (0, 0))
    swap = pl.BlockSpec((HDIM, HDIM), lambda h, flags: (0, 0))
    return head, whole, swap


def swap_matrix():
    lane = jnp.arange(HDIM)
    return (lane[:, None] == (lane[None, :] ^ 1)).astype(jnp.bfloat16)


def near_attention(flags, queries, blocks, tables):
    count, width = queries.shape
    heads_here = width // HDIM
    head, whole, swap = specs(count)
    value_spec = pl.BlockSpec((count, HDIM), lambda h, flags: (1, h))
    grid_spec = pltpu.PrefetchScalarGridSpec(
        num_scalar_prefetch=1,
        grid=(heads_here,),
        in_specs=[head] * 4 + [value_spec, swap] + [whole] * 2,
        out_specs=[head] * 3,
    )
    cost = pl.CostEstimate(
        flops=heads_here * 2 * 4 * count * count * HDIM,
        transcendentals=heads_here * 2 * count * count,
        bytes_accessed=5 * count * width * 2 + 3 * count * width * 4,
    )
    f32 = jax.ShapeDtypeStruct((count, width), jnp.float32)
    return pl.pallas_call(
        near_kernel, grid_spec=grid_spec, out_shape=[f32] * 3, cost_estimate=cost
    )(flags, queries, *blocks, swap_matrix(), *tables)


def sink_attention(flags, queries, blocks, tables, near, half, halves):
    count, width = queries.shape
    group = 5
    heads_here = width // HDIM // group
    rows = count // halves
    wide = group * HDIM
    part = pl.BlockSpec((rows, wide), lambda h, flags: (half, h))
    part_table = pl.BlockSpec((rows, HDIM), lambda h, flags: (half, 0))
    key_spec = pl.BlockSpec((count, wide), lambda h, flags: (0, h))
    value_spec = pl.BlockSpec((count, wide), lambda h, flags: (1, h))
    swap = pl.BlockSpec((HDIM, HDIM), lambda h, flags: (0, 0))
    grid_spec = pltpu.PrefetchScalarGridSpec(
        num_scalar_prefetch=1,
        grid=(heads_here,),
        in_specs=[part, key_spec, value_spec, swap] + [part_table] * 2 + [part] * 3,
        out_specs=pl.BlockSpec((rows, wide), lambda h, flags: (0, h)),
    )
    cost = pl.CostEstimate(
        flops=heads_here * group * 4 * rows * count * HDIM,
        transcendentals=heads_here * group * rows * count,
        bytes_accessed=(rows + 2 * count) * width * 2 + 3 * rows * width * 4,
    )
    return pl.pallas_call(
        sink_kernel,
        grid_spec=grid_spec,
        out_shape=jax.ShapeDtypeStruct((rows, width), jnp.bfloat16),
        cost_estimate=cost,
    )(flags, queries, *blocks, swap_matrix(), *tables, *near)


def weight_blocks(out_weight):
    n_xl, n_c = lax.axis_size("xl"), lax.axis_size("c")
    block = out_weight.shape[1] // (n_xl * n_c)
    c = lax.axis_index("c")

    def columns(core):
        return jnp.stack(
            [lax.dynamic_slice_in_dim(out_weight, (x * n_c + core) * block, block, axis=1) for x in range(n_xl)]
        )

    return columns(c), columns(1 - c)


def head_reduce(attended, mine_w, other_w):
    xl = lax.axis_index("xl")
    mine = jnp.einsum("rk,xkn->xrn", attended, mine_w, preferred_element_type=jnp.float32).astype(jnp.bfloat16)
    other = jnp.einsum("rk,xkn->xrn", attended, other_w, preferred_element_type=jnp.float32).astype(jnp.bfloat16)
    got = lax.ppermute(other, "c", [(0, 1), (1, 0)])
    chip = (mine.astype(jnp.float32) + got.astype(jnp.float32)).astype(jnp.bfloat16)
    keep = lax.dynamic_index_in_dim(chip, xl, axis=0, keepdims=False)
    send = lax.dynamic_index_in_dim(chip, 1 - xl, axis=0, keepdims=False)
    got = lax.ppermute(send, "xl", [(0, 1), (1, 0)])
    return (keep.astype(jnp.float32) + got.astype(jnp.float32)).astype(jnp.bfloat16)


def shards(queries, keys, values, out_weight, sink_owner, frame_pos):
    count = queries.shape[0]
    place = frame_index()
    n_frame = lax.axis_size(FRAME_AXES)
    sink = sink_owner[0] % (n_frame // 2)
    own_tables = rope_tables(frame_pos[0], count)
    rot_k = rope(keys, own_tables)
    prev_kv, sink_kv = exchange(jnp.concatenate([rot_k, values], axis=0), sink)
    prev_used = (place >= 1) & (place - 1 != sink)
    sink_used = sink < place
    flags = jnp.stack([prev_used, sink_used]).astype(jnp.int32)
    near = near_attention(flags, queries, (rot_k, values, prev_kv, prev_kv), own_tables)
    halves = 2
    mine_w, other_w = weight_blocks(out_weight)
    outs = []
    for half in range(halves):
        attended = sink_attention(flags, queries, (sink_kv, sink_kv), own_tables, near, half, halves)
        outs.append(head_reduce(attended, mine_w, other_w))
    mixed = jnp.concatenate(outs, axis=0)
    return mixed


def solution(mesh):
    frame_phys = {"z": 4, "xh": 2, "y": 4}
    head_phys = {"xl": 2, "c": 2}
    assert mesh.shape["frame"] == 32 and mesh.shape["head"] == 4
    devices = mesh.devices.reshape(tuple(frame_phys.values()) + tuple(head_phys.values()))
    fine = Mesh(devices, FRAME_AXES + HEAD_AXES)
    in_specs = (
        P(FRAME_AXES, HEAD_AXES),
        P(FRAME_AXES, HEAD_AXES),
        P(FRAME_AXES, HEAD_AXES),
        P(HEAD_AXES, None),
        P(),
        P(FRAME_AXES),
    )
    out_specs = P(FRAME_AXES, HEAD_AXES)
    inner = jax.shard_map(shards, mesh=fine, in_specs=in_specs, out_specs=out_specs, check_vma=False)

    def run(*args):
        out = inner(*args)
        return jax.lax.with_sharding_constraint(out, NamedSharding(mesh, P("frame", "head")))

    return run
```

```python
import jax
import jax.numpy as jnp
from jax import lax
from jax.experimental import pallas as pl
from jax.experimental.pallas import tpu as pltpu
from jax.sharding import Mesh, NamedSharding, PartitionSpec as P

HDIM = 128
GRID_W = 32


def shifted(array, axis, by):
    length = lax.axis_size(axis)
    pairs = [(i, i + by) for i in range(length) if 0 <= i + by < length]
    return lax.ppermute(array, axis, pairs)


def broadcast(value, axis, source):
    kept = jnp.where(lax.axis_index(axis) == source, value, 0).astype(value.dtype)
    return lax.psum(kept, axis)


def pair_angles(frame_value, count):
    half = HDIM // 2
    tdim = HDIM - 4 * (HDIM // 6)
    sdim = 2 * (HDIM // 6)
    tcount = tdim // 2
    scount = sdim // 2
    index = jnp.arange(half)
    findex = index.astype(jnp.float32)
    freq = jnp.where(
        index < tcount,
        jnp.power(10000.0, -2.0 * findex / tdim),
        jnp.where(
            index < tcount + scount,
            jnp.power(10000.0, -2.0 * (findex - tcount) / sdim),
            jnp.power(10000.0, -2.0 * (findex - tcount - scount) / sdim),
        ),
    )
    token = jnp.arange(count)
    row_pos = (token // GRID_W).astype(jnp.float32)[:, None]
    col_pos = (token % GRID_W).astype(jnp.float32)[:, None]
    frame_f = jnp.zeros((count, 1), jnp.float32) + frame_value.astype(jnp.float32)
    pos = jnp.where(
        index[None, :] < tcount,
        frame_f,
        jnp.where(index[None, :] < tcount + scount, row_pos, col_pos),
    )
    return pos * freq[None, :]


def rotate(block, angle):
    count = block.shape[0]
    heads_here = block.shape[1] // HDIM
    parts = block.astype(jnp.float32).reshape(count, heads_here, HDIM // 2, 2)
    cosine = jnp.cos(angle)[:, None, :]
    sine = jnp.sin(angle)[:, None, :]
    first = parts[..., 0] * cosine - parts[..., 1] * sine
    second = parts[..., 0] * sine + parts[..., 1] * cosine
    return (
        jnp.stack([first, second], axis=-1).reshape(count, heads_here * HDIM).astype(jnp.bfloat16)
    )


def attend_block(query, key_block, value_block):
    count = query.shape[0]
    heads_here = query.shape[1] // HDIM
    qh = query.reshape(count, heads_here, HDIM)
    kh = key_block.reshape(-1, heads_here, HDIM)
    vh = value_block.reshape(-1, heads_here, HDIM)
    scores = jnp.einsum("qhd,khd->hqk", qh, kh, preferred_element_type=jnp.float32) / jnp.sqrt(
        jnp.float32(HDIM)
    )
    peak = jnp.max(scores, axis=-1)
    weights = jnp.exp(scores - peak[..., None]).astype(jnp.bfloat16)
    total = jnp.sum(weights.astype(jnp.float32), axis=-1)
    partial_value = jnp.einsum("hqk,khd->hqd", weights, vh, preferred_element_type=jnp.float32)
    return (peak, total, partial_value)


FRAME_AXES = ("z", "xh", "y")
HEAD_AXES = ("xl", "c")


def frame_index():
    return (lax.axis_index("z") * lax.axis_size("xh") + lax.axis_index("xh")) * lax.axis_size("y") + lax.axis_index(
        "y"
    )


def cyclic(array, axis, by):
    length = lax.axis_size(axis)
    return lax.ppermute(array, axis, [(i, (i + by) % length) for i in range(length)])


def ring_stage(data, axis, source):
    length = lax.axis_size(axis)
    if length == 1:
        return data
    rel = (lax.axis_index(axis) - source) % length
    if length == 2:
        got = cyclic(data, axis, 1)
        return jnp.where(rel == 0, data, got)
    assert length == 4
    half = data.shape[0] // 2
    h0, h1 = data[:half], data[half:]
    g0 = cyclic(h0, axis, 1)
    g1 = cyclic(h1, axis, -1)
    a0 = jnp.where(rel == 1, g0, h0)
    a1 = jnp.where(rel == 3, g1, h1)
    r_p = cyclic(jnp.where(rel == 0, h1, a0), axis, 1)
    r_m = cyclic(jnp.where(rel == 0, h0, a1), axis, -1)
    out0 = jnp.where(rel == 0, h0, jnp.where(rel == 1, g0, jnp.where(rel == 2, r_p, r_m)))
    out1 = jnp.where(rel == 0, h1, jnp.where(rel == 1, r_p, jnp.where(rel == 2, r_m, g1)))
    return jnp.concatenate([out0, out1], axis=0)


def exchange(data, sink):
    n_frame = lax.axis_size(FRAME_AXES)
    piece = data.shape[0] // n_frame
    spread = lax.all_to_all(data, FRAME_AXES, 0, 0, tiled=True)
    pieces = spread.reshape((n_frame, piece) + data.shape[1:])
    before = jnp.concatenate([pieces[-1:], pieces[:-1]], axis=0).reshape(data.shape)
    prev_full = lax.all_to_all(before, FRAME_AXES, 0, 0, tiled=True)
    mine = lax.dynamic_slice_in_dim(spread, sink * piece, piece, axis=0)
    copies = jnp.broadcast_to(mine[None], (n_frame,) + mine.shape).reshape(data.shape)
    copies, prev_full = lax.optimization_barrier((copies, prev_full))
    return prev_full, lax.all_to_all(copies, FRAME_AXES, 0, 0, tiled=True)


def rope_tables(frame_value, count):
    tdim = HDIM - 4 * (HDIM // 6)
    sdim = 2 * (HDIM // 6)
    tcount = tdim // 2
    scount = sdim // 2
    lane = jnp.arange(HDIM)
    index = lane // 2
    findex = index.astype(jnp.float32)
    freq = jnp.where(
        index < tcount,
        jnp.power(10000.0, -2.0 * findex / tdim),
        jnp.where(
            index < tcount + scount,
            jnp.power(10000.0, -2.0 * (findex - tcount) / sdim),
            jnp.power(10000.0, -2.0 * (findex - tcount - scount) / sdim),
        ),
    )
    token = jnp.arange(count)
    row_pos = (token // GRID_W).astype(jnp.float32)[:, None]
    col_pos = (token % GRID_W).astype(jnp.float32)[:, None]
    frame_f = jnp.zeros((count, 1), jnp.float32) + frame_value.astype(jnp.float32)
    pos = jnp.where(
        index[None, :] < tcount,
        frame_f,
        jnp.where(index[None, :] < tcount + scount, row_pos, col_pos),
    )
    angle = pos * freq[None, :]
    sine = jnp.sin(angle)
    return jnp.cos(angle), jnp.where(lane[None, :] % 2 == 0, -sine, sine)


def rotate_ref(x_ref, cos_ref, sin_ref, swap):
    x = x_ref[...]
    partner = jnp.dot(x, swap, preferred_element_type=jnp.float32)
    return (x.astype(jnp.float32) * cos_ref[...] + partner * sin_ref[...]).astype(jnp.bfloat16)


def attend_ref(q, k, v_ref):
    scale = 1.0 / jnp.sqrt(jnp.float32(HDIM))
    raw = lax.dot_general(q, k, (((1,), (1,)), ((), ())), preferred_element_type=jnp.float32)
    raw_peak = jnp.max(raw, axis=-1, keepdims=True)
    peak = raw_peak * scale
    weights = jnp.exp((raw - raw_peak) * scale).astype(jnp.bfloat16)
    total = jnp.sum(weights.astype(jnp.float32), axis=-1, keepdims=True)
    partial_value = jnp.dot(weights, v_ref[...], preferred_element_type=jnp.float32)
    return peak, total, partial_value


def near_kernel(flags, q_ref, ks_ref, vs_ref, kp_ref, vp_ref, swap_ref, cq, sq, m_ref, l_ref, o_ref):
    swap = swap_ref[...]
    q = rotate_ref(q_ref, cq, sq, swap)
    m_self, l_self, o_self = attend_ref(q, ks_ref[...], vs_ref)
    m_prev, l_prev, o_prev = attend_ref(q, kp_ref[...], vp_ref)
    prev_used = flags[0] != 0
    top = jnp.maximum(m_self, jnp.where(prev_used, m_prev, m_self))
    c_self = jnp.exp(m_self - top)
    c_prev = jnp.where(prev_used, jnp.exp(m_prev - top), 0.0)
    m_ref[...] = jnp.broadcast_to(top, m_ref.shape)
    l_ref[...] = jnp.broadcast_to(l_self * c_self + l_prev * c_prev, l_ref.shape)
    o_ref[...] = o_self * c_self + o_prev * c_prev


def rope_kernel(x_ref, swap_ref, cos_ref, sin_ref, out_ref):
    swap = swap_ref[...]
    for j in range(x_ref.shape[1] // HDIM):
        cols = slice(j * HDIM, (j + 1) * HDIM)
        out_ref[:, cols] = rotate_ref(x_ref.at[:, cols], cos_ref, sin_ref, swap)


def rope(x, tables):
    count, width = x.shape
    wide = 5 * HDIM
    head = pl.BlockSpec((count, wide), lambda h: (0, h))
    whole = pl.BlockSpec((count, HDIM), lambda h: (0, 0))
    swap = pl.BlockSpec((HDIM, HDIM), lambda h: (0, 0))
    return pl.pallas_call(
        rope_kernel,
        grid=(width // wide,),
        in_specs=[head, swap, whole, whole],
        out_specs=head,
        out_shape=jax.ShapeDtypeStruct((count, width), jnp.bfloat16),
        cost_estimate=pl.CostEstimate(flops=2 * count * width * HDIM, transcendentals=0, bytes_accessed=4 * count * width),
    )(x, swap_matrix(), *tables)


def sink_kernel(flags, q_ref, kk_ref, vk_ref, swap_ref, cq, sq, m_ref, l_ref, o_ref, out_ref):
    swap = swap_ref[...]
    sink_used = flags[1] != 0
    for j in range(q_ref.shape[1] // HDIM):
        cols = slice(j * HDIM, (j + 1) * HDIM)
        q = rotate_ref(q_ref.at[:, cols], cq, sq, swap)
        m_sink, l_sink, o_sink = attend_ref(q, kk_ref[:, cols], vk_ref.at[:, cols])
        m_near = m_ref[:, j * HDIM : j * HDIM + 1]
        top = jnp.maximum(m_near, jnp.where(sink_used, m_sink, m_near))
        c_near = jnp.exp(m_near - top)
        c_sink = jnp.where(sink_used, jnp.exp(m_sink - top), 0.0)
        numer = o_ref[:, cols] * c_near + o_sink * c_sink
        denom = l_ref[:, j * HDIM : j * HDIM + 1] * c_near + l_sink * c_sink
        out_ref[:, cols] = (numer / denom).astype(out_ref.dtype)


def specs(count):
    head = pl.BlockSpec((count, HDIM), lambda h, flags: (0, h))
    whole = pl.BlockSpec((count, HDIM), lambda h, flags: (0, 0))
    swap = pl.BlockSpec((HDIM, HDIM), lambda h, flags: (0, 0))
    return head, whole, swap


def swap_matrix():
    lane = jnp.arange(HDIM)
    return (lane[:, None] == (lane[None, :] ^ 1)).astype(jnp.bfloat16)


def near_attention(flags, queries, blocks, tables):
    count, width = queries.shape
    heads_here = width // HDIM
    head, whole, swap = specs(count)
    value_spec = pl.BlockSpec((count, HDIM), lambda h, flags: (1, h))
    grid_spec = pltpu.PrefetchScalarGridSpec(
        num_scalar_prefetch=1,
        grid=(heads_here,),
        in_specs=[head] * 4 + [value_spec, swap] + [whole] * 2,
        out_specs=[head] * 3,
    )
    cost = pl.CostEstimate(
        flops=heads_here * 2 * 4 * count * count * HDIM,
        transcendentals=heads_here * 2 * count * count,
        bytes_accessed=5 * count * width * 2 + 3 * count * width * 4,
    )
    f32 = jax.ShapeDtypeStruct((count, width), jnp.float32)
    return pl.pallas_call(
        near_kernel, grid_spec=grid_spec, out_shape=[f32] * 3, cost_estimate=cost
    )(flags, queries, *blocks, swap_matrix(), *tables)


def sink_attention(flags, queries, blocks, tables, near, half, halves):
    count, width = queries.shape
    group = 5
    heads_here = width // HDIM // group
    rows = count // halves
    wide = group * HDIM
    part = pl.BlockSpec((rows, wide), lambda h, flags: (half, h))
    part_table = pl.BlockSpec((rows, HDIM), lambda h, flags: (half, 0))
    key_spec = pl.BlockSpec((count, wide), lambda h, flags: (0, h))
    value_spec = pl.BlockSpec((count, wide), lambda h, flags: (1, h))
    swap = pl.BlockSpec((HDIM, HDIM), lambda h, flags: (0, 0))
    grid_spec = pltpu.PrefetchScalarGridSpec(
        num_scalar_prefetch=1,
        grid=(heads_here,),
        in_specs=[part, key_spec, value_spec, swap] + [part_table] * 2 + [part] * 3,
        out_specs=pl.BlockSpec((rows, wide), lambda h, flags: (0, h)),
    )
    cost = pl.CostEstimate(
        flops=heads_here * group * 4 * rows * count * HDIM,
        transcendentals=heads_here * group * rows * count,
        bytes_accessed=(rows + 2 * count) * width * 2 + 3 * rows * width * 4,
    )
    return pl.pallas_call(
        sink_kernel,
        grid_spec=grid_spec,
        out_shape=jax.ShapeDtypeStruct((rows, width), jnp.bfloat16),
        cost_estimate=cost,
    )(flags, queries, *blocks, swap_matrix(), *tables, *near)


def weight_blocks(out_weight):
    n_xl, n_c = lax.axis_size("xl"), lax.axis_size("c")
    block = out_weight.shape[1] // (n_xl * n_c)
    c = lax.axis_index("c")

    def columns(core):
        return jnp.stack(
            [lax.dynamic_slice_in_dim(out_weight, (x * n_c + core) * block, block, axis=1) for x in range(n_xl)]
        )

    return columns(c), columns(1 - c)


def head_reduce(attended, mine_w, other_w):
    xl = lax.axis_index("xl")
    mine = jnp.einsum("rk,xkn->xrn", attended, mine_w, preferred_element_type=jnp.float32).astype(jnp.bfloat16)
    other = jnp.einsum("rk,xkn->xrn", attended, other_w, preferred_element_type=jnp.float32).astype(jnp.bfloat16)
    got = lax.ppermute(other, "c", [(0, 1), (1, 0)])
    chip = (mine.astype(jnp.float32) + got.astype(jnp.float32)).astype(jnp.bfloat16)
    keep = lax.dynamic_index_in_dim(chip, xl, axis=0, keepdims=False)
    send = lax.dynamic_index_in_dim(chip, 1 - xl, axis=0, keepdims=False)
    got = lax.ppermute(send, "xl", [(0, 1), (1, 0)])
    return (keep.astype(jnp.float32) + got.astype(jnp.float32)).astype(jnp.bfloat16)


def shards(queries, keys, values, out_weight, sink_owner, frame_pos):
    count = queries.shape[0]
    place = frame_index()
    n_frame = lax.axis_size(FRAME_AXES)
    sink = sink_owner[0] % (n_frame // 2)
    own_tables = rope_tables(frame_pos[0], count)
    rot_k = rope(keys, own_tables)
    prev_kv, sink_kv = exchange(jnp.concatenate([rot_k, values], axis=0), sink)
    prev_used = (place >= 1) & (place - 1 != sink)
    sink_used = sink < place
    flags = jnp.stack([prev_used, sink_used]).astype(jnp.int32)
    near = near_attention(flags, queries, (rot_k, values, prev_kv, prev_kv), own_tables)
    halves = 2
    mine_w, other_w = weight_blocks(out_weight)
    outs = []
    for half in range(halves):
        attended = sink_attention(flags, queries, (sink_kv, sink_kv), own_tables, near, half, halves)
        outs.append(head_reduce(attended, mine_w, other_w))
    mixed = jnp.concatenate(outs, axis=0)
    return mixed


def solution(mesh):
    frame_phys = {"z": 4, "xh": 2, "y": 4}
    head_phys = {"xl": 2, "c": 2}
    assert mesh.shape["frame"] == 32 and mesh.shape["head"] == 4
    devices = mesh.devices.reshape(tuple(frame_phys.values()) + tuple(head_phys.values()))
    fine = Mesh(devices, FRAME_AXES + HEAD_AXES)
    in_specs = (
        P(FRAME_AXES, HEAD_AXES),
        P(FRAME_AXES, HEAD_AXES),
        P(FRAME_AXES, HEAD_AXES),
        P(HEAD_AXES, None),
        P(),
        P(FRAME_AXES),
    )
    out_specs = P(FRAME_AXES, HEAD_AXES)
    inner = jax.shard_map(shards, mesh=fine, in_specs=in_specs, out_specs=out_specs, check_vma=False)

    def run(*args):
        out = inner(*args)
        return jax.lax.with_sharding_constraint(out, NamedSharding(mesh, P("frame", "head")))

    return run
```
